32 devices in a mesh: dp: 16 (over z, x, core), mp: 2 (over y).
Axes of the slice: x: 2, y: 2, z: 4, core: 2. Of those that a mesh axis runs over, the one named last changes fastest.
Arguments:
- tokens: bfloat16 [16384, 768], P('dp'), may hold values from -6 to 6
- doc_ids: int32 [16, 1024], P('dp'), may hold values from 0 to 3, never falling along the last dimension, each value on 1 to 512 neighbouring positions
- ln1_gain: bfloat16 [768], replicated, may hold values from 0.25 to 1.75
- ln1_bias: bfloat16 [768], replicated, may hold values from -2.5 to 2.5
- w_qkv: bfloat16 [768, 3, 768], P(None, None, 'mp'), may hold values from -0.21875 to 0.21875
- b_qv: bfloat16 [2, 768], P(None, 'mp'), may hold values from -3 to 3
- w_out: bfloat16 [768, 768], P('mp'), may hold values from -1.75 to 1.75
- b_out: bfloat16 [768], replicated, may hold values from -3 to 3
- ln2_gain: bfloat16 [768], replicated, may hold values from 0.25 to 1.75
- ln2_bias: bfloat16 [768], replicated, may hold values from -2.5 to 2.5
- w_up: bfloat16 [768, 3072], P(None, 'mp'), may hold values from -0.21875 to 0.21875
- b_up: bfloat16 [3072], P('mp'), may hold values from -3 to 3
- w_down: bfloat16 [3072, 768], P('mp'), may hold values from -0.15625 to 0.15625
- b_down: bfloat16 [768], replicated, may hold values from -3 to 3
- cotangent: bfloat16 [16384, 768], P('dp'), may hold values from -6 to 6
Outputs:
- block_out: bfloat16 [16384, 768], P('dp')
- grad_tokens: float32 [16384, 768], P('dp')
- grad_ln1_gain: float32 [768], replicated
- grad_ln1_bias: float32 [768], replicated
- grad_w_qkv: float32 [768, 3, 768], P('dp', None, 'mp')
- grad_b_qv: float32 [2, 768], P(None, 'mp')
- grad_w_out: float32 [768, 768], P('mp', 'dp')
- grad_b_out: float32 [768], replicated
- grad_ln2_gain: float32 [768], replicated
- grad_ln2_bias: float32 [768], replicated
- grad_w_up: float32 [768, 3072], P('dp', 'mp')
- grad_b_up: float32 [3072], P('mp')
- grad_w_down: float32 [3072, 768], P('mp', 'dp')
- grad_b_down: float32 [768], replicated
The draws below stay inside these ranges and needn't reach their ends.
Inputs may be any that keep to these rules, and one draw needn't show every extreme that they name: `doc_ids`: within each packed row the ids start at 0, never fall, and each id covers 1 to 512 consecutive positions, one of them exactly that many.
All inputs are finite; a program needn't handle non-finite values.
Results may differ from the reference program's by a relative error of at most 0.009.
Values may be sent and summed in bfloat16 or wider, within the bound.
No kernel may reach another device: no remote copies, remote signals or barrier semaphores. Data moves between devices by JAX's collectives and lax.ppermute only.
A program may use at most 192 MiB of HBM per device.

```python
import math
import jax
import jax.numpy as jnp
import numpy as np
from jax import lax

D = 768
HEADS = 12
HD = 64
FF = 3072
LEN = 1024
DOCS = 4
SEQS = 16
TOKENS = 16384


def raised(values, stream_key, source, target, shards_of, factor):
    owner, partner = [(jnp.arange(values.shape[dim]) // (values.shape[dim] // shards_of)).reshape([-1 if axis == dim else 1 for axis in range(values.ndim)]) for dim in (source, target)]
    chosen = jax.random.permutation(stream_key, shards_of)[partner]
    strong = (owner == chosen) | (owner == (partner + shards_of // 2) % shards_of)
    return jnp.where(strong, factor * values, values)


def block_levels(own_key, shape, split, smallest, top_value):
    def one(dim, parts):
        draws = jax.random.uniform(jax.random.fold_in(jax.random.fold_in(own_key, 6), dim), (parts,), jnp.float32, smallest / len(split), top_value / len(split))
        return jnp.repeat(jnp.exp(draws), shape[dim] // parts).reshape((-1,) + (1,) * (len(shape) - dim - 1))

    factor_of = one(*split[0])
    for cut in split[1:]:
        factor_of = factor_of * one(*cut)
    return factor_of


def length_profile(number_of, total, bound, skew):
    portions = [(1 << 20) // math.isqrt(grade ** skew) + 1 for grade in range(2, number_of + 1)]
    spare, holding = total - bound - (number_of - 1), [1] * (number_of - 1)
    while spare > 0:
        movable = [i for i in range(number_of - 1) if holding[i] < bound]
        pool, budget = sum([portions[i] for i in movable]), spare
        for i in movable:
            more = min(bound - holding[i], max(1, budget * portions[i] // pool), spare)
            holding[i] = holding[i] + more
            spare = spare - more
    return np.array([bound] + holding)


def uneven(own_key, amount, total, bound, skew):
    if amount == 2:
        one = jax.random.randint(own_key, (), max(1, total - bound), min(bound, total - 1) + 1)
        return jnp.stack([one, total - one])
    sizes = jnp.asarray(length_profile(amount, total, bound, skew), jnp.int32)
    twos = (amount - 1) // 2
    giver, sink = sizes[1:1 + 2 * twos:2], sizes[2:2 + 2 * twos:2]
    slack = jnp.minimum(giver - 1, bound - sink)
    shifted = jax.random.randint(jax.random.fold_in(own_key, 1), (twos,), 0, 1 << 20) % (slack + 1)
    sizes = sizes.at[1:1 + 2 * twos:2].set(giver - shifted).at[2:2 + 2 * twos:2].set(sink + shifted)
    return sizes[jax.random.permutation(jax.random.fold_in(own_key, 2), amount)]


def gaussian(stream_key, shape, deviation, most, pieces=(), kind=jnp.bfloat16):
    values = deviation * jax.random.normal(stream_key, shape, jnp.float32)
    if pieces:
        values = values * block_levels(stream_key, shape, pieces, -0.22, 0.18)
    return jnp.clip(values, -most, most).astype(kind)


def bell_draw_with(stream_key, dims, width, limit, split, heavy, kind=jnp.bfloat16):
    drawn = width * jax.random.normal(stream_key, dims, jnp.float32)
    if split:
        drawn = drawn * block_levels(stream_key, dims, split, -0.22, 0.18)
    return jnp.clip(raised(drawn, jax.random.fold_in(stream_key, 3), *heavy), -limit, limit).astype(kind)


def setup_inputs(seed: int = 0) -> dict:
    arg_keys = jax.random.split(jax.random.key(seed), 16)
    return {
        "tokens": bell_draw_with(arg_keys[0], (TOKENS, D), 1.0, 6.0, ((0, 16),), (0, 1, 16, 2.0)),
        "doc_ids": jax.vmap(lambda own: jnp.searchsorted(jnp.cumsum(uneven(own, DOCS, LEN, LEN // 2, 2)), jnp.arange(LEN), side="right"))(jax.random.split(arg_keys[1], SEQS)).reshape((SEQS, LEN)).astype(jnp.int32),
        "ln1_gain": jnp.clip(1.0 + 0.15 * jax.random.normal(arg_keys[2], (D,), jnp.float32), 0.25, 1.75).astype(jnp.bfloat16),
        "ln1_bias": gaussian(arg_keys[3], (D,), 0.4, 2.5),
        "w_qkv": gaussian(arg_keys[4], (D, 3, D), D ** -0.5, 0.21875, ((2, 2),)),
        "b_qv": gaussian(arg_keys[5], (2, D), 0.5, 3.0, ((1, 2),)),
        "w_out": gaussian(arg_keys[6], (D, D), (D // 64) ** -0.5, 1.75, ((0, 2),)),
        "b_out": gaussian(arg_keys[7], (D,), 0.5, 3.0),
        "ln2_gain": jnp.clip(1.0 + 0.15 * jax.random.normal(arg_keys[8], (D,), jnp.float32), 0.25, 1.75).astype(jnp.bfloat16),
        "ln2_bias": gaussian(arg_keys[9], (D,), 0.4, 2.5),
        "w_up": gaussian(arg_keys[10], (D, FF), D ** -0.5, 0.21875, ((1, 2),)),
        "b_up": gaussian(arg_keys[11], (FF,), 0.5, 3.0, ((0, 2),)),
        "w_down": gaussian(arg_keys[12], (FF, D), (FF // 2) ** -0.5, 0.15625, ((0, 2),)),
        "b_down": gaussian(arg_keys[13], (D,), 0.5, 3.0),
        "cotangent": bell_draw_with(arg_keys[14], (TOKENS, D), 1.0, 6.0, ((0, 16),), (0, 1, 16, 2.0)),
    }


@jax.custom_vjp
def low(v):
    return lax.optimization_barrier(v.astype(jnp.bfloat16)).astype(jnp.float32)

@jax.custom_vjp
def low_back(v):
    return v

def low_keep(v):
    return (low(v), None)

def low_pass(kept, grad):
    return (grad,)

def back_keep(v):
    return (v, None)

def back_low(kept, grad):
    return (low(grad),)
low.defvjp(low_keep, low_pass)
low_back.defvjp(back_keep, back_low)
highest = lax.Precision.HIGHEST
epsilon = 1e-05

def layer_norm(values, gain, shift):
    average = lax.optimization_barrier(jnp.mean(values, axis=-1, keepdims=True))
    centered = values - average
    variance = lax.optimization_barrier(jnp.mean(centered * centered, axis=-1, keepdims=True))
    return centered * lax.rsqrt(variance + epsilon) * gain + shift

def gelu_tanh(values):
    return 0.5 * values * (1.0 + jnp.tanh(0.7978845608028654 * (values + 0.044715 * values * values * values)))

def attend_sequence(packed):
    queries, key_rows, value_rows, doc_rows = packed
    seq_len = queries.shape[0]
    scores = low_back(jnp.einsum('qhd,khd->hqk', queries, key_rows, precision=highest) * (1.0 / math.sqrt(HD)))
    position = jnp.arange(seq_len, dtype=jnp.int32)
    allowed = (doc_rows[:, None] == doc_rows[None, :]) & (position[:, None] >= position[None, :])
    masked = jnp.where(allowed[None], scores, -1e+30)
    row_max = lax.optimization_barrier(jnp.max(masked, axis=-1, keepdims=True))
    weights_exp = jnp.exp(masked - row_max)
    probabilities = low(weights_exp / lax.optimization_barrier(jnp.sum(weights_exp, axis=-1, keepdims=True)))
    return jnp.einsum('hqk,khd->qhd', probabilities, value_rows, precision=highest)

def block_forward(params, token_rows, doc_group):
    ln1_gain, ln1_bias, w_qkv, b_qv, w_out, b_out, ln2_gain, ln2_bias, w_up, b_up, w_down, b_down = params
    row_count = token_rows.shape[0]
    normed_one = low(layer_norm(token_rows, ln1_gain, ln1_bias))
    projected = jnp.einsum('td,dce->tce', normed_one, w_qkv, precision=highest)
    queries = low(low_back(projected[:, 0] + b_qv[0]))
    key_rows = low(low_back(projected[:, 1]))
    value_rows = low(low_back(projected[:, 2] + b_qv[1]))
    seq_shape = (doc_group.shape[0], doc_group.shape[1], HEADS, HD)
    attended = lax.map(jax.checkpoint(attend_sequence), (queries.reshape(seq_shape), key_rows.reshape(seq_shape), value_rows.reshape(seq_shape), doc_group))
    mixed = low(low_back(attended.reshape(row_count, D)))
    after_attn = token_rows + low_back(jnp.dot(mixed, w_out, precision=highest) + b_out)
    normed_two = low(layer_norm(after_attn, ln2_gain, ln2_bias))
    up_rows = low_back(jnp.dot(normed_two, w_up, precision=highest) + b_up)
    activated = low(gelu_tanh(up_rows))
    return after_attn + low_back(jnp.dot(activated, w_down, precision=highest) + b_down)

def reference(tokens, doc_ids, ln1_gain, ln1_bias, w_qkv, b_qv, w_out, b_out, ln2_gain, ln2_bias, w_up, b_up, w_down, b_down, cotangent):
    params = tuple((entry.astype(jnp.float32) for entry in (ln1_gain, ln1_bias, w_qkv, b_qv, w_out, b_out, ln2_gain, ln2_bias, w_up, b_up, w_down, b_down)))
    group_size = math.gcd(SEQS, 4)
    group_count = SEQS // group_size
    inputs = tokens.astype(jnp.float32).reshape(group_count, group_size * LEN, D)
    cot_groups = cotangent.astype(jnp.float32).reshape(group_count, group_size * LEN, D)
    doc_groups = doc_ids.astype(jnp.int32).reshape(group_count, group_size, LEN)

    def accumulate(totals, packed):
        token_rows, doc_group, cot_rows = packed
        outputs, pull_back = jax.vjp(lambda weights_in, rows_in: block_forward(weights_in, rows_in, doc_group), params, token_rows)
        grad_params, grad_rows = pull_back(cot_rows)
        return (jax.tree.map(jnp.add, totals, grad_params), (outputs.astype(jnp.bfloat16), grad_rows))
    zeros_init = jax.tree.map(jnp.zeros_like, params)
    totals, (outputs, grad_rows) = lax.scan(accumulate, zeros_init, (inputs, doc_groups, cot_groups))
    return (outputs.reshape(TOKENS, D), grad_rows.reshape(TOKENS, D), totals[0], totals[1], totals[2], totals[3], totals[4], totals[5], totals[6], totals[7], totals[8], totals[9], totals[10], totals[11])
```

```python
import math

import jax
import jax.numpy as jnp
from jax import lax
from jax.sharding import PartitionSpec as P

HD = 64


epsilon = 1e-05


def normalize(values):
    average = jnp.mean(values, axis=-1, keepdims=True)
    centered = values - average
    variance = jnp.mean(centered * centered, axis=-1, keepdims=True)
    inverse = lax.rsqrt(variance + epsilon)
    return (centered * inverse, inverse)


def norm_back(grad_out, normal_rows, inverse, gain):
    grad_unit = grad_out * gain
    return inverse * (
        grad_unit
        - jnp.mean(grad_unit, axis=-1, keepdims=True)
        - normal_rows * jnp.mean(grad_unit * normal_rows, axis=-1, keepdims=True)
    )


def gelu_tanh(values):
    return (
        0.5
        * values
        * (1.0 + jnp.tanh(0.7978845608028654 * (values + 0.044715 * values * values * values)))
    )


def block_scores(query_block, key_rows, doc_rows, offset):
    block_rows = query_block.shape[0]
    scores = jnp.einsum(
        "qhd,khd->hqk", query_block, key_rows, preferred_element_type=jnp.float32
    ) * (1.0 / math.sqrt(HD))
    query_pos = offset + lax.iota(jnp.int32, block_rows)
    key_pos = lax.iota(jnp.int32, key_rows.shape[0])
    block_docs = doc_rows[offset : offset + block_rows]
    allowed = (block_docs[:, None] == doc_rows[None, :]) & (query_pos[:, None] >= key_pos[None, :])
    return jnp.where(allowed[None], scores, -1e30)


def attend_forward(queries, key_rows, value_rows, doc_rows):
    seq_len = queries.shape[0]
    block_rows = min(512, seq_len)
    outputs = []
    log_parts = []
    for offset in range(0, seq_len, block_rows):
        scores = block_scores(queries[offset : offset + block_rows], key_rows, doc_rows, offset)
        row_max = jnp.max(scores, axis=-1, keepdims=True)
        log_total = row_max + jnp.log(jnp.sum(jnp.exp(scores - row_max), axis=-1, keepdims=True))
        probabilities = jnp.exp(scores - log_total).astype(jnp.bfloat16)
        outputs.append(
            jnp.einsum(
                "hqk,khd->qhd", probabilities, value_rows, preferred_element_type=jnp.float32
            )
        )
        log_parts.append(log_total[..., 0])
    return (jnp.concatenate(outputs, axis=0), jnp.concatenate(log_parts, axis=1))


def attend_backward(queries, key_rows, value_rows, doc_rows, log_totals, grad_out):
    seq_len = queries.shape[0]
    block_rows = min(512, seq_len)
    scale_factor = 1.0 / math.sqrt(HD)
    grad_queries = []
    grad_keys = jnp.zeros(key_rows.shape, jnp.float32)
    grad_values = jnp.zeros(value_rows.shape, jnp.float32)
    for offset in range(0, seq_len, block_rows):
        query_block = queries[offset : offset + block_rows]
        grad_block = grad_out[offset : offset + block_rows]
        scores = block_scores(query_block, key_rows, doc_rows, offset)
        probabilities = jnp.exp(scores - log_totals[:, offset : offset + block_rows, None])
        grad_probs = jnp.einsum(
            "qhd,khd->hqk", grad_block, value_rows, preferred_element_type=jnp.float32
        )
        row_dots = jnp.sum(probabilities * grad_probs, axis=-1, keepdims=True)
        grad_scores = (probabilities * (grad_probs - row_dots)).astype(jnp.bfloat16)
        grad_queries.append(
            scale_factor
            * jnp.einsum("hqk,khd->qhd", grad_scores, key_rows, preferred_element_type=jnp.float32)
        )
        grad_keys = grad_keys + scale_factor * jnp.einsum(
            "hqk,qhd->khd", grad_scores, query_block, preferred_element_type=jnp.float32
        )
        grad_values = grad_values + jnp.einsum(
            "hqk,qhd->khd",
            probabilities.astype(jnp.bfloat16),
            grad_block,
            preferred_element_type=jnp.float32,
        )
    return (jnp.concatenate(grad_queries, axis=0), grad_keys, grad_values)


def swap_mp(x):
    return lax.ppermute(x, "mp", [(0, 1), (1, 0)])


def row_halves(x, m):
    half = x.shape[0] // 2
    own = lax.dynamic_slice_in_dim(x, m * half, half, axis=0)
    other = lax.dynamic_slice_in_dim(x, (1 - m) * half, half, axis=0)
    return own, other


def join_pair(own, other, m, axis):
    return jnp.where(
        m == 0,
        jnp.concatenate([own, other], axis=axis),
        jnp.concatenate([other, own], axis=axis),
    )


def scatter_rows_mp(partial, m, send_dtype):
    own, other = row_halves(partial, m)
    return own + swap_mp(other.astype(send_dtype)).astype(own.dtype)


def gather_rows_mp(own, m):
    return join_pair(own, swap_mp(own), m, 0)


def scatter_dp(x, ndp):
    idx = lax.axis_index("dp")
    bits = ndp.bit_length() - 1
    chunk = x.shape[0] // ndp
    rest = x.shape[1:]
    cur = x.reshape((2,) * bits + (chunk,) + rest)
    remaining = list(range(bits - 1, -1, -1))
    for bit in range(bits):
        pos = remaining.index(bit)
        mine = (idx >> bit) & 1
        keep = lax.dynamic_index_in_dim(cur, mine, pos, keepdims=False)
        send = lax.dynamic_index_in_dim(cur, 1 - mine, pos, keepdims=False)
        got = lax.ppermute(send, "dp", [(i, i ^ (1 << bit)) for i in range(ndp)])
        cur = keep + got
        remaining.pop(pos)
    return cur.reshape((chunk,) + rest)


def reduce_tree(x, name, size):
    bits = size.bit_length() - 1
    for bit in range(bits):
        x = x + lax.ppermute(x, name, [(i, i ^ (1 << bit)) for i in range(size)])
    return x


def make_shards(ndp, nmp):
    def shards(
        tokens,
        doc_ids,
        ln1_gain,
        ln1_bias,
        w_qkv,
        b_qv,
        w_out,
        b_out,
        ln2_gain,
        ln2_bias,
        w_up,
        b_up,
        w_down,
        b_down,
        cotangent,
    ):
        m = lax.axis_index("mp")
        row_count = tokens.shape[0]
        local_width = w_qkv.shape[2]
        seq_count, seq_len = doc_ids.shape
        seq_shape = (seq_count, seq_len, local_width // HD, HD)
        token_rows = tokens.astype(jnp.float32)
        normal_one, inv_one = normalize(token_rows)
        gain_one = ln1_gain.astype(jnp.float32)
        normed_one = (normal_one * gain_one + ln1_bias.astype(jnp.float32)).astype(jnp.bfloat16)
        projected = jnp.einsum(
            "td,dce->tce", normed_one, w_qkv, preferred_element_type=jnp.float32
        )
        bias_qv = b_qv.astype(jnp.float32)
        queries = (projected[:, 0] + bias_qv[0]).astype(jnp.bfloat16).reshape(seq_shape)
        key_rows = projected[:, 1].astype(jnp.bfloat16).reshape(seq_shape)
        value_rows = (projected[:, 2] + bias_qv[1]).astype(jnp.bfloat16).reshape(seq_shape)
        attended = []
        log_totals = []
        for s in range(seq_count):
            out_s, lse_s = attend_forward(queries[s], key_rows[s], value_rows[s], doc_ids[s])
            attended.append(out_s)
            log_totals.append(lse_s)
        mixed = jnp.stack(attended).reshape(row_count, local_width).astype(jnp.bfloat16)
        mixed_all = join_pair(mixed, swap_mp(mixed), m, 1)
        w_out_all = join_pair(w_out, swap_mp(w_out), m, 0)
        attn_all = jnp.dot(mixed_all, w_out_all, preferred_element_type=jnp.float32)
        after_attn = token_rows + attn_all + b_out.astype(jnp.float32)
        gain_two = ln2_gain.astype(jnp.float32)
        normal_two, inv_two = normalize(after_attn)
        normed_two = (normal_two * gain_two + ln2_bias.astype(jnp.float32)).astype(jnp.bfloat16)
        up_rows = jnp.dot(normed_two, w_up, preferred_element_type=jnp.float32) + b_up.astype(
            jnp.float32
        )
        activated, gelu_pull = jax.vjp(gelu_tanh, up_rows)
        act_rows = activated.astype(jnp.bfloat16)
        ffn_part = jnp.dot(act_rows, w_down, preferred_element_type=jnp.float32)
        ffn_own = scatter_rows_mp(ffn_part, m, jnp.bfloat16)
        after_own, _ = row_halves(after_attn, m)
        out_own = (after_own + (ffn_own + b_down.astype(jnp.float32))).astype(jnp.bfloat16)
        block_out = gather_rows_mp(out_own, m)

        cot_rows = cotangent.astype(jnp.float32)
        cot_own, _ = row_halves(cot_rows, m)
        grad_w_down_t = jnp.einsum(
            "td,tf->df", cotangent, act_rows, preferred_element_type=jnp.float32
        )
        grad_act = jnp.einsum("td,fd->tf", cotangent, w_down, preferred_element_type=jnp.float32)
        grad_up = gelu_pull(grad_act)[0].astype(jnp.bfloat16)
        grad_w_up = jnp.einsum("td,tf->df", normed_two, grad_up, preferred_element_type=jnp.float32)
        grad_b_up = jnp.sum(grad_up.astype(jnp.float32), axis=0)
        norm_two_part = jnp.einsum("tf,df->td", grad_up, w_up, preferred_element_type=jnp.float32)
        grad_two_own = scatter_rows_mp(norm_two_part, m, jnp.float32)
        normal_two_own, _ = row_halves(normal_two, m)
        inv_two_own, _ = row_halves(inv_two, m)
        grad_after_own = cot_own + norm_back(grad_two_own, normal_two_own, inv_two_own, gain_two)
        grad_attn_own = grad_after_own.astype(jnp.bfloat16)
        grad_attn_here = gather_rows_mp(grad_attn_own, m)
        grad_w_out_t = jnp.einsum(
            "td,te->de", grad_attn_here, mixed, preferred_element_type=jnp.float32
        )
        grad_mixed = jnp.einsum(
            "td,ed->te", grad_attn_here, w_out, preferred_element_type=jnp.float32
        ).astype(jnp.bfloat16)
        grad_mixed = grad_mixed.reshape(seq_shape)
        gq, gk, gv = [], [], []
        for s in range(seq_count):
            dq_s, dk_s, dv_s = attend_backward(
                queries[s], key_rows[s], value_rows[s], doc_ids[s], log_totals[s], grad_mixed[s]
            )
            gq.append(dq_s)
            gk.append(dk_s)
            gv.append(dv_s)
        grad_q = jnp.stack(gq).reshape(row_count, local_width).astype(jnp.bfloat16)
        grad_k = jnp.stack(gk).reshape(row_count, local_width).astype(jnp.bfloat16)
        grad_v = jnp.stack(gv).reshape(row_count, local_width).astype(jnp.bfloat16)
        grad_proj = jnp.stack([grad_q, grad_k, grad_v], axis=1)
        grad_w_qkv = jnp.einsum(
            "td,tce->dce", normed_one, grad_proj, preferred_element_type=jnp.float32
        )
        grad_b_qv = jnp.stack(
            [
                jnp.sum(grad_q.astype(jnp.float32), axis=0),
                jnp.sum(grad_v.astype(jnp.float32), axis=0),
            ]
        )
        norm_one_part = jnp.einsum(
            "tce,dce->td", grad_proj, w_qkv, preferred_element_type=jnp.float32
        )
        grad_one_own = scatter_rows_mp(norm_one_part, m, jnp.float32)
        normal_one_own, _ = row_halves(normal_one, m)
        inv_one_own, _ = row_halves(inv_one, m)
        grad_input_own = grad_after_own + norm_back(
            grad_one_own, normal_one_own, inv_one_own, gain_one
        )
        grad_input = gather_rows_mp(grad_input_own, m)
        vector_terms = jnp.stack(
            [
                jnp.sum(grad_one_own * normal_one_own, axis=0),
                jnp.sum(grad_one_own, axis=0),
                jnp.sum(grad_two_own * normal_two_own, axis=0),
                jnp.sum(grad_two_own, axis=0),
                jnp.sum(grad_attn_own.astype(jnp.float32), axis=0),
                jnp.sum(cot_own, axis=0),
            ]
        )
        n_vec = vector_terms.size
        n_qv = grad_b_qv.size
        packed = jnp.concatenate([vector_terms.reshape(-1), grad_b_qv.reshape(-1), grad_b_up])
        packed = reduce_tree(packed, "dp", ndp)
        vector_sum = reduce_tree(packed[:n_vec], "mp", nmp).reshape(vector_terms.shape)
        qv_sum = packed[n_vec : n_vec + n_qv].reshape(grad_b_qv.shape)
        up_sum = packed[n_vec + n_qv :]
        sum_qkv = scatter_dp(grad_w_qkv, ndp)
        sum_out = scatter_dp(grad_w_out_t, ndp).T
        sum_up = scatter_dp(grad_w_up, ndp)
        sum_down = scatter_dp(grad_w_down_t, ndp).T
        return (
            block_out,
            grad_input,
            vector_sum[0],
            vector_sum[1],
            sum_qkv,
            qv_sum,
            sum_out,
            vector_sum[4],
            vector_sum[2],
            vector_sum[3],
            sum_up,
            up_sum,
            sum_down,
            vector_sum[5],
        )

    return shards


def solution(mesh):
    return jax.shard_map(
        make_shards(mesh.shape["dp"], mesh.shape["mp"]),
        mesh=mesh,
        in_specs=(
            P("dp", None),
            P("dp", None),
            P(),
            P(),
            P(None, None, "mp"),
            P(None, "mp"),
            P("mp", None),
            P(),
            P(),
            P(),
            P(None, "mp"),
            P("mp"),
            P("mp", None),
            P(),
            P("dp", None),
        ),
        out_specs=(
            P("dp", None),
            P("dp", None),
            P(),
            P(),
            P("dp", None, "mp"),
            P(None, "mp"),
            P("mp", "dp"),
            P(),
            P(),
            P(),
            P("dp", "mp"),
            P("mp"),
            P("mp", "dp"),
            P(),
        ),
        check_vma=False,
    )
```

```python
import math

import jax
import jax.numpy as jnp
from jax import lax
from jax.experimental import pallas as pl
from jax.experimental.pallas import tpu as pltpu
from jax.sharding import PartitionSpec as P

HD = 64


epsilon = 1e-05


def normalize(values):
    average = jnp.mean(values, axis=-1, keepdims=True)
    centered = values - average
    variance = jnp.mean(centered * centered, axis=-1, keepdims=True)
    inverse = lax.rsqrt(variance + epsilon)
    return (centered * inverse, inverse)


def norm_back(grad_out, normal_rows, inverse, gain):
    grad_unit = grad_out * gain
    return inverse * (
        grad_unit
        - jnp.mean(grad_unit, axis=-1, keepdims=True)
        - normal_rows * jnp.mean(grad_unit * normal_rows, axis=-1, keepdims=True)
    )


def gelu_tanh(values):
    return (
        0.5
        * values
        * (1.0 + jnp.tanh(0.7978845608028654 * (values + 0.044715 * values * values * values)))
    )


def block_scores(query_block, key_rows, doc_rows, offset):
    block_rows = query_block.shape[0]
    scores = jnp.einsum(
        "qhd,khd->hqk", query_block, key_rows, preferred_element_type=jnp.float32
    ) * (1.0 / math.sqrt(HD))
    query_pos = offset + lax.iota(jnp.int32, block_rows)
    key_pos = lax.iota(jnp.int32, key_rows.shape[0])
    block_docs = doc_rows[offset : offset + block_rows]
    allowed = (block_docs[:, None] == doc_rows[None, :]) & (query_pos[:, None] >= key_pos[None, :])
    return jnp.where(allowed[None], scores, -1e30)


def attend_forward(queries, key_rows, value_rows, doc_rows):
    seq_len = queries.shape[0]
    block_rows = min(512, seq_len)
    outputs = []
    log_parts = []
    for offset in range(0, seq_len, block_rows):
        scores = block_scores(queries[offset : offset + block_rows], key_rows, doc_rows, offset)
        row_max = jnp.max(scores, axis=-1, keepdims=True)
        log_total = row_max + jnp.log(jnp.sum(jnp.exp(scores - row_max), axis=-1, keepdims=True))
        probabilities = jnp.exp(scores - log_total).astype(jnp.bfloat16)
        outputs.append(
            jnp.einsum(
                "hqk,khd->qhd", probabilities, value_rows, preferred_element_type=jnp.float32
            )
        )
        log_parts.append(log_total[..., 0])
    return (jnp.concatenate(outputs, axis=0), jnp.concatenate(log_parts, axis=1))


def attend_backward(queries, key_rows, value_rows, doc_rows, log_totals, grad_out):
    seq_len = queries.shape[0]
    block_rows = min(512, seq_len)
    scale_factor = 1.0 / math.sqrt(HD)
    grad_queries = []
    grad_keys = jnp.zeros(key_rows.shape, jnp.float32)
    grad_values = jnp.zeros(value_rows.shape, jnp.float32)
    for offset in range(0, seq_len, block_rows):
        query_block = queries[offset : offset + block_rows]
        grad_block = grad_out[offset : offset + block_rows]
        scores = block_scores(query_block, key_rows, doc_rows, offset)
        probabilities = jnp.exp(scores - log_totals[:, offset : offset + block_rows, None])
        grad_probs = jnp.einsum(
            "qhd,khd->hqk", grad_block, value_rows, preferred_element_type=jnp.float32
        )
        row_dots = jnp.sum(probabilities * grad_probs, axis=-1, keepdims=True)
        grad_scores = (probabilities * (grad_probs - row_dots)).astype(jnp.bfloat16)
        grad_queries.append(
            scale_factor
            * jnp.einsum("hqk,khd->qhd", grad_scores, key_rows, preferred_element_type=jnp.float32)
        )
        grad_keys = grad_keys + scale_factor * jnp.einsum(
            "hqk,qhd->khd", grad_scores, query_block, preferred_element_type=jnp.float32
        )
        grad_values = grad_values + jnp.einsum(
            "hqk,qhd->khd",
            probabilities.astype(jnp.bfloat16),
            grad_block,
            preferred_element_type=jnp.float32,
        )
    return (jnp.concatenate(grad_queries, axis=0), grad_keys, grad_values)


BQ = 128
BK = 128
SCALE = 0.125
NEG = -1e30


def _nt(a, b):
    return lax.dot_general(a, b, (((1,), (1,)), ((), ())), preferred_element_type=jnp.float32)


def _tn(a, b):
    return lax.dot_general(a, b, (((0,), (0,)), ((), ())), preferred_element_type=jnp.float32)


def _scores(q, k_ref, drow_ref, dcol, qpos, j):
    start = pl.multiple_of(j * BK, BK)
    k = k_ref[0, pl.ds(start, BK), :]
    s = _nt(q, k) * SCALE
    kpos = start + lax.broadcasted_iota(jnp.int32, (1, BK), 1)
    allowed = (dcol == drow_ref[:, pl.ds(start, BK)]) & (qpos >= kpos)
    return jnp.where(allowed, s, NEG), start


def _fwd_kernel(lo_ref, q_ref, k_ref, v_ref, dcol_ref, drow_ref, o_ref, lse_ref):
    i = pl.program_id(1)
    q = q_ref[0]
    dcol = dcol_ref[...]
    qpos = i * BQ + lax.broadcasted_iota(jnp.int32, (BQ, 1), 0)
    lo = lo_ref[i]

    def stats(j, carry):
        m, l = carry
        s, _ = _scores(q, k_ref, drow_ref, dcol, qpos, j)
        m_new = jnp.maximum(m, jnp.max(s, axis=1, keepdims=True))
        l = l * jnp.exp(m - m_new) + jnp.sum(jnp.exp(s - m_new), axis=1, keepdims=True)
        return m_new, l

    m0 = jnp.full((BQ, 1), NEG, jnp.float32)
    l0 = jnp.zeros((BQ, 1), jnp.float32)
    m, l = lax.fori_loop(lo, i + 1, stats, (m0, l0))
    lse = m + jnp.log(l)

    def accumulate(j, acc):
        s, start = _scores(q, k_ref, drow_ref, dcol, qpos, j)
        p = jnp.exp(s - lse).astype(jnp.bfloat16)
        v = v_ref[0, pl.ds(start, BK), :]
        return acc + jnp.dot(p, v, preferred_element_type=jnp.float32)

    acc = lax.fori_loop(lo, i + 1, accumulate, jnp.zeros(o_ref.shape[1:], jnp.float32))
    o_ref[0] = acc.astype(o_ref.dtype)
    lse_ref[0] = lse


def _bwd_kernel(lo_ref, q_ref, k_ref, v_ref, do_ref, lse_ref, dcol_ref, drow_ref,
                dq_ref, dk_ref, dv_ref, dk_acc, dv_acc):
    i = pl.program_id(1)
    nq = pl.num_programs(1)

    @pl.when(i == 0)
    def _():
        dk_acc[...] = jnp.zeros_like(dk_acc)
        dv_acc[...] = jnp.zeros_like(dv_acc)

    q = q_ref[0]
    do = do_ref[0]
    lse = lse_ref[0]
    dcol = dcol_ref[...]
    qpos = i * BQ + lax.broadcasted_iota(jnp.int32, (BQ, 1), 0)
    lo = lo_ref[i]

    def probs(j):
        s, start = _scores(q, k_ref, drow_ref, dcol, qpos, j)
        p = jnp.exp(s - lse)
        v = v_ref[0, pl.ds(start, BK), :]
        return p, _nt(do, v), start

    def row_dot(j, total):
        p, dp, _ = probs(j)
        return total + jnp.sum(p * dp, axis=1, keepdims=True)

    dsum = lax.fori_loop(lo, i + 1, row_dot, jnp.zeros((BQ, 1), jnp.float32))

    def grads(j, dq):
        p, dp, start = probs(j)
        ds = (p * (dp - dsum)).astype(jnp.bfloat16)
        k = k_ref[0, pl.ds(start, BK), :]
        dk_acc[pl.ds(start, BK), :] += _tn(ds, q)
        dv_acc[pl.ds(start, BK), :] += _tn(p.astype(jnp.bfloat16), do)
        return dq + jnp.dot(ds, k, preferred_element_type=jnp.float32)

    dq = lax.fori_loop(lo, i + 1, grads, jnp.zeros(dq_ref.shape[1:], jnp.float32))
    dq_ref[0] = (dq * SCALE).astype(dq_ref.dtype)

    @pl.when(i == nq - 1)
    def _():
        dk_ref[0] = (dk_acc[...] * SCALE).astype(dk_ref.dtype)
        dv_ref[0] = dv_acc[...].astype(dv_ref.dtype)


def block_starts(doc_row):
    seq_len = doc_row.shape[0]
    firsts = doc_row[::BQ]
    before = jnp.sum((doc_row[None, :] < firsts[:, None]).astype(jnp.int32), axis=1)
    return (before // BK).astype(jnp.int32)


def attn_fwd(q, k, v, doc_row):
    heads, seq_len, dim = q.shape
    nq = seq_len // BQ
    lo = block_starts(doc_row)
    dcol = doc_row.reshape(seq_len, 1)
    drow = doc_row.reshape(1, seq_len)
    full = pl.BlockSpec((1, seq_len, dim), lambda h, i, lo: (h, 0, 0))
    blk = pl.BlockSpec((1, BQ, dim), lambda h, i, lo: (h, i, 0))
    grid_spec = pltpu.PrefetchScalarGridSpec(
        num_scalar_prefetch=1,
        grid=(heads, nq),
        in_specs=[blk, full, full,
                  pl.BlockSpec((BQ, 1), lambda h, i, lo: (i, 0)),
                  pl.BlockSpec((1, seq_len), lambda h, i, lo: (0, 0))],
        out_specs=[blk, pl.BlockSpec((1, BQ, 1), lambda h, i, lo: (h, i, 0))],
    )
    return pl.pallas_call(
        _fwd_kernel,
        grid_spec=grid_spec,
        out_shape=[jax.ShapeDtypeStruct(q.shape, jnp.bfloat16),
                   jax.ShapeDtypeStruct((heads, seq_len, 1), jnp.float32)],
        compiler_params=pltpu.CompilerParams(dimension_semantics=("arbitrary", "arbitrary")),
    )(lo, q, k, v, dcol, drow)


def attn_bwd(q, k, v, do, lse, doc_row):
    heads, seq_len, dim = q.shape
    nq = seq_len // BQ
    lo = block_starts(doc_row)
    dcol = doc_row.reshape(seq_len, 1)
    drow = doc_row.reshape(1, seq_len)
    full = pl.BlockSpec((1, seq_len, dim), lambda h, i, lo: (h, 0, 0))
    blk = pl.BlockSpec((1, BQ, dim), lambda h, i, lo: (h, i, 0))
    grid_spec = pltpu.PrefetchScalarGridSpec(
        num_scalar_prefetch=1,
        grid=(heads, nq),
        in_specs=[blk, full, full, blk,
                  pl.BlockSpec((1, BQ, 1), lambda h, i, lo: (h, i, 0)),
                  pl.BlockSpec((BQ, 1), lambda h, i, lo: (i, 0)),
                  pl.BlockSpec((1, seq_len), lambda h, i, lo: (0, 0))],
        out_specs=[blk, full, full],
        scratch_shapes=[pltpu.VMEM((seq_len, dim), jnp.float32),
                        pltpu.VMEM((seq_len, dim), jnp.float32)],
    )
    return pl.pallas_call(
        _bwd_kernel,
        grid_spec=grid_spec,
        out_shape=[jax.ShapeDtypeStruct(q.shape, jnp.bfloat16)] * 3,
        compiler_params=pltpu.CompilerParams(dimension_semantics=("arbitrary", "arbitrary")),
    )(lo, q, k, v, do, lse, dcol, drow)


def swap_mp(x):
    return lax.ppermute(x, "mp", [(0, 1), (1, 0)])


def row_halves(x, m):
    half = x.shape[0] // 2
    own = lax.dynamic_slice_in_dim(x, m * half, half, axis=0)
    other = lax.dynamic_slice_in_dim(x, (1 - m) * half, half, axis=0)
    return own, other


def join_pair(own, other, m, axis):
    return jnp.where(
        m == 0,
        jnp.concatenate([own, other], axis=axis),
        jnp.concatenate([other, own], axis=axis),
    )


def scatter_rows_mp(partial, m, send_dtype):
    own, other = row_halves(partial, m)
    return own + swap_mp(other.astype(send_dtype)).astype(own.dtype)


def gather_rows_mp(own, m):
    return join_pair(own, swap_mp(own), m, 0)


def scatter_dp(x, ndp):
    idx = lax.axis_index("dp")
    bits = ndp.bit_length() - 1
    chunk = x.shape[0] // ndp
    rest = x.shape[1:]
    cur = x.reshape((2,) * bits + (chunk,) + rest)
    remaining = list(range(bits - 1, -1, -1))
    for bit in range(bits):
        pos = remaining.index(bit)
        mine = (idx >> bit) & 1
        keep = lax.dynamic_index_in_dim(cur, mine, pos, keepdims=False)
        send = lax.dynamic_index_in_dim(cur, 1 - mine, pos, keepdims=False)
        got = lax.ppermute(send, "dp", [(i, i ^ (1 << bit)) for i in range(ndp)])
        cur = keep + got
        remaining.pop(pos)
    return cur.reshape((chunk,) + rest)


def reduce_tree(x, name, size):
    bits = size.bit_length() - 1
    for bit in range(bits):
        x = x + lax.ppermute(x, name, [(i, i ^ (1 << bit)) for i in range(size)])
    return x


def make_shards(ndp, nmp):
    def shards(
        tokens,
        doc_ids,
        ln1_gain,
        ln1_bias,
        w_qkv,
        b_qv,
        w_out,
        b_out,
        ln2_gain,
        ln2_bias,
        w_up,
        b_up,
        w_down,
        b_down,
        cotangent,
    ):
        m = lax.axis_index("mp")
        row_count = tokens.shape[0]
        local_width = w_qkv.shape[2]
        seq_count, seq_len = doc_ids.shape
        seq_shape = (seq_count, seq_len, local_width // HD, HD)
        token_rows = tokens.astype(jnp.float32)
        normal_one, inv_one = normalize(token_rows)
        gain_one = ln1_gain.astype(jnp.float32)
        normed_one = (normal_one * gain_one + ln1_bias.astype(jnp.float32)).astype(jnp.bfloat16)
        projected = jnp.einsum(
            "td,dce->tce", normed_one, w_qkv, preferred_element_type=jnp.float32
        )
        bias_qv = b_qv.astype(jnp.float32)
        queries = (projected[:, 0] + bias_qv[0]).astype(jnp.bfloat16).reshape(seq_shape)
        key_rows = projected[:, 1].astype(jnp.bfloat16).reshape(seq_shape)
        value_rows = (projected[:, 2] + bias_qv[1]).astype(jnp.bfloat16).reshape(seq_shape)
        heads_major = lambda x: jnp.transpose(x, (0, 2, 1, 3))
        q_h, k_h, v_h = heads_major(queries), heads_major(key_rows), heads_major(value_rows)
        attended = []
        log_totals = []
        for s in range(seq_count):
            out_s, lse_s = attn_fwd(q_h[s], k_h[s], v_h[s], doc_ids[s])
            attended.append(out_s)
            log_totals.append(lse_s)
        mixed = jnp.transpose(jnp.stack(attended), (0, 2, 1, 3)).reshape(row_count, local_width)
        mixed_all = join_pair(mixed, swap_mp(mixed), m, 1)
        w_out_all = join_pair(w_out, swap_mp(w_out), m, 0)
        attn_all = jnp.dot(mixed_all, w_out_all, preferred_element_type=jnp.float32)
        after_attn = token_rows + attn_all + b_out.astype(jnp.float32)
        gain_two = ln2_gain.astype(jnp.float32)
        normal_two, inv_two = normalize(after_attn)
        normed_two = (normal_two * gain_two + ln2_bias.astype(jnp.float32)).astype(jnp.bfloat16)
        up_rows = jnp.dot(normed_two, w_up, preferred_element_type=jnp.float32) + b_up.astype(
            jnp.float32
        )
        activated, gelu_pull = jax.vjp(gelu_tanh, up_rows)
        act_rows = activated.astype(jnp.bfloat16)
        ffn_part = jnp.dot(act_rows, w_down, preferred_element_type=jnp.float32)
        ffn_own = scatter_rows_mp(ffn_part, m, jnp.bfloat16)
        after_own, _ = row_halves(after_attn, m)
        out_own = (after_own + (ffn_own + b_down.astype(jnp.float32))).astype(jnp.bfloat16)
        block_out = gather_rows_mp(out_own, m)

        cot_rows = cotangent.astype(jnp.float32)
        cot_own, _ = row_halves(cot_rows, m)
        grad_w_down_t = jnp.einsum(
            "td,tf->df", cotangent, act_rows, preferred_element_type=jnp.float32
        )
        grad_act = jnp.einsum("td,fd->tf", cotangent, w_down, preferred_element_type=jnp.float32)
        grad_up = gelu_pull(grad_act)[0].astype(jnp.bfloat16)
        grad_w_up = jnp.einsum("td,tf->df", normed_two, grad_up, preferred_element_type=jnp.float32)
        grad_b_up = jnp.sum(grad_up.astype(jnp.float32), axis=0)
        norm_two_part = jnp.einsum("tf,df->td", grad_up, w_up, preferred_element_type=jnp.float32)
        grad_two_own = scatter_rows_mp(norm_two_part, m, jnp.float32)
        normal_two_own, _ = row_halves(normal_two, m)
        inv_two_own, _ = row_halves(inv_two, m)
        grad_after_own = cot_own + norm_back(grad_two_own, normal_two_own, inv_two_own, gain_two)
        grad_attn_own = grad_after_own.astype(jnp.bfloat16)
        grad_attn_here = gather_rows_mp(grad_attn_own, m)
        grad_w_out_t = jnp.einsum(
            "td,te->de", grad_attn_here, mixed, preferred_element_type=jnp.float32
        )
        grad_mixed = jnp.einsum(
            "td,ed->te", grad_attn_here, w_out, preferred_element_type=jnp.float32
        ).astype(jnp.bfloat16)
        grad_mixed = heads_major(grad_mixed.reshape(seq_shape))
        gq, gk, gv = [], [], []
        for s in range(seq_count):
            dq_s, dk_s, dv_s = attn_bwd(
                q_h[s], k_h[s], v_h[s], grad_mixed[s], log_totals[s], doc_ids[s]
            )
            gq.append(dq_s)
            gk.append(dk_s)
            gv.append(dv_s)
        token_major = lambda parts: jnp.transpose(jnp.stack(parts), (0, 2, 1, 3)).reshape(
            row_count, local_width
        )
        grad_q = token_major(gq)
        grad_k = token_major(gk)
        grad_v = token_major(gv)
        grad_proj = jnp.stack([grad_q, grad_k, grad_v], axis=1)
        grad_w_qkv = jnp.einsum(
            "td,tce->dce", normed_one, grad_proj, preferred_element_type=jnp.float32
        )
        grad_b_qv = jnp.stack(
            [
                jnp.sum(grad_q.astype(jnp.float32), axis=0),
                jnp.sum(grad_v.astype(jnp.float32), axis=0),
            ]
        )
        norm_one_part = jnp.einsum(
            "tce,dce->td", grad_proj, w_qkv, preferred_element_type=jnp.float32
        )
        grad_one_own = scatter_rows_mp(norm_one_part, m, jnp.float32)
        normal_one_own, _ = row_halves(normal_one, m)
        inv_one_own, _ = row_halves(inv_one, m)
        grad_input_own = grad_after_own + norm_back(
            grad_one_own, normal_one_own, inv_one_own, gain_one
        )
        grad_input = gather_rows_mp(grad_input_own, m)
        vector_terms = jnp.stack(
            [
                jnp.sum(grad_one_own * normal_one_own, axis=0),
                jnp.sum(grad_one_own, axis=0),
                jnp.sum(grad_two_own * normal_two_own, axis=0),
                jnp.sum(grad_two_own, axis=0),
                jnp.sum(grad_attn_own.astype(jnp.float32), axis=0),
                jnp.sum(cot_own, axis=0),
            ]
        )
        n_vec = vector_terms.size
        n_qv = grad_b_qv.size
        packed = jnp.concatenate([vector_terms.reshape(-1), grad_b_qv.reshape(-1), grad_b_up])
        packed = reduce_tree(packed, "dp", ndp)
        vector_sum = reduce_tree(packed[:n_vec], "mp", nmp).reshape(vector_terms.shape)
        qv_sum = packed[n_vec : n_vec + n_qv].reshape(grad_b_qv.shape)
        up_sum = packed[n_vec + n_qv :]
        sum_qkv = scatter_dp(grad_w_qkv, ndp)
        sum_out = scatter_dp(grad_w_out_t, ndp).T
        sum_up = scatter_dp(grad_w_up, ndp)
        sum_down = scatter_dp(grad_w_down_t, ndp).T
        return (
            block_out,
            grad_input,
            vector_sum[0],
            vector_sum[1],
            sum_qkv,
            qv_sum,
            sum_out,
            vector_sum[4],
            vector_sum[2],
            vector_sum[3],
            sum_up,
            up_sum,
            sum_down,
            vector_sum[5],
        )

    return shards


def solution(mesh):
    return jax.shard_map(
        make_shards(mesh.shape["dp"], mesh.shape["mp"]),
        mesh=mesh,
        in_specs=(
            P("dp", None),
            P("dp", None),
            P(),
            P(),
            P(None, None, "mp"),
            P(None, "mp"),
            P("mp", None),
            P(),
            P(),
            P(),
            P(None, "mp"),
            P("mp"),
            P("mp", None),
            P(),
            P("dp", None),
        ),
        out_specs=(
            P("dp", None),
            P("dp", None),
            P(),
            P(),
            P("dp", None, "mp"),
            P(None, "mp"),
            P("mp", "dp"),
            P(),
            P(),
            P(),
            P("dp", "mp"),
            P("mp"),
            P("mp", "dp"),
            P(),
        ),
        check_vma=False,
    )
```

```python
import math

import jax
import jax.numpy as jnp
from jax import lax
from jax.sharding import PartitionSpec as P


HD = 64


epsilon = 1e-05


def normalize(values):
    average = jnp.mean(values, axis=-1, keepdims=True)
    centered = values - average
    variance = jnp.mean(centered * centered, axis=-1, keepdims=True)
    inverse = lax.rsqrt(variance + epsilon)
    return (centered * inverse, inverse)


def norm_back(grad_out, normal_rows, inverse, gain):
    grad_unit = grad_out * gain
    return inverse * (
        grad_unit
        - jnp.mean(grad_unit, axis=-1, keepdims=True)
        - normal_rows * jnp.mean(grad_unit * normal_rows, axis=-1, keepdims=True)
    )


def gelu_tanh(values):
    return (
        0.5
        * values
        * (1.0 + jnp.tanh(0.7978845608028654 * (values + 0.044715 * values * values * values)))
    )


def block_scores(query_block, key_rows, doc_rows, offset):
    block_rows = query_block.shape[0]
    scores = jnp.einsum(
        "qhd,khd->hqk", query_block, key_rows, preferred_element_type=jnp.float32
    ) * (1.0 / math.sqrt(HD))
    query_pos = offset + lax.iota(jnp.int32, block_rows)
    key_pos = lax.iota(jnp.int32, key_rows.shape[0])
    block_docs = doc_rows[offset : offset + block_rows]
    allowed = (block_docs[:, None] == doc_rows[None, :]) & (query_pos[:, None] >= key_pos[None, :])
    return jnp.where(allowed[None], scores, -1e30)


def attend_forward(queries, key_rows, value_rows, doc_rows):
    seq_len = queries.shape[0]
    block_rows = min(512, seq_len)
    outputs = []
    log_parts = []
    for offset in range(0, seq_len, block_rows):
        scores = block_scores(queries[offset : offset + block_rows], key_rows, doc_rows, offset)
        row_max = jnp.max(scores, axis=-1, keepdims=True)
        log_total = row_max + jnp.log(jnp.sum(jnp.exp(scores - row_max), axis=-1, keepdims=True))
        probabilities = jnp.exp(scores - log_total).astype(jnp.bfloat16)
        outputs.append(
            jnp.einsum(
                "hqk,khd->qhd", probabilities, value_rows, preferred_element_type=jnp.float32
            )
        )
        log_parts.append(log_total[..., 0])
    return (jnp.concatenate(outputs, axis=0), jnp.concatenate(log_parts, axis=1))


def attend_backward(queries, key_rows, value_rows, doc_rows, log_totals, grad_out):
    seq_len = queries.shape[0]
    block_rows = min(512, seq_len)
    scale_factor = 1.0 / math.sqrt(HD)
    grad_queries = []
    grad_keys = jnp.zeros(key_rows.shape, jnp.float32)
    grad_values = jnp.zeros(value_rows.shape, jnp.float32)
    for offset in range(0, seq_len, block_rows):
        query_block = queries[offset : offset + block_rows]
        grad_block = grad_out[offset : offset + block_rows]
        scores = block_scores(query_block, key_rows, doc_rows, offset)
        probabilities = jnp.exp(scores - log_totals[:, offset : offset + block_rows, None])
        grad_probs = jnp.einsum(
            "qhd,khd->hqk", grad_block, value_rows, preferred_element_type=jnp.float32
        )
        row_dots = jnp.sum(probabilities * grad_probs, axis=-1, keepdims=True)
        grad_scores = (probabilities * (grad_probs - row_dots)).astype(jnp.bfloat16)
        grad_queries.append(
            scale_factor
            * jnp.einsum("hqk,khd->qhd", grad_scores, key_rows, preferred_element_type=jnp.float32)
        )
        grad_keys = grad_keys + scale_factor * jnp.einsum(
            "hqk,qhd->khd", grad_scores, query_block, preferred_element_type=jnp.float32
        )
        grad_values = grad_values + jnp.einsum(
            "hqk,qhd->khd",
            probabilities.astype(jnp.bfloat16),
            grad_block,
            preferred_element_type=jnp.float32,
        )
    return (jnp.concatenate(grad_queries, axis=0), grad_keys, grad_values)


def swap_mp(x):
    return lax.ppermute(x, "mp", [(0, 1), (1, 0)])


def row_halves(x, m):
    half = x.shape[0] // 2
    own = lax.dynamic_slice_in_dim(x, m * half, half, axis=0)
    other = lax.dynamic_slice_in_dim(x, (1 - m) * half, half, axis=0)
    return own, other


def join_pair(own, other, m, axis):
    return jnp.where(
        m == 0,
        jnp.concatenate([own, other], axis=axis),
        jnp.concatenate([other, own], axis=axis),
    )


def scatter_rows_mp(partial, m, send_dtype):
    own, other = row_halves(partial, m)
    return own + swap_mp(other.astype(send_dtype)).astype(own.dtype)


def gather_rows_mp(own, m):
    return join_pair(own, swap_mp(own), m, 0)


def scatter_dp(x, ndp):
    idx = lax.axis_index("dp")
    bits = ndp.bit_length() - 1
    chunk = x.shape[0] // ndp
    rest = x.shape[1:]
    cur = x.reshape((2,) * bits + (chunk,) + rest)
    remaining = list(range(bits - 1, -1, -1))
    for bit in range(bits):
        pos = remaining.index(bit)
        mine = (idx >> bit) & 1
        keep = lax.dynamic_index_in_dim(cur, mine, pos, keepdims=False)
        send = lax.dynamic_index_in_dim(cur, 1 - mine, pos, keepdims=False)
        got = lax.ppermute(send, "dp", [(i, i ^ (1 << bit)) for i in range(ndp)])
        cur = keep + got
        remaining.pop(pos)
    return cur.reshape((chunk,) + rest)


def reduce_tree(x, name, size):
    bits = size.bit_length() - 1
    for bit in range(bits):
        x = x + lax.ppermute(x, name, [(i, i ^ (1 << bit)) for i in range(size)])
    return x


def make_shards(ndp, nmp):
    def shards_body(
        tokens,
        doc_ids,
        ln1_gain,
        ln1_bias,
        w_qkv,
        b_qv,
        w_out,
        b_out,
        ln2_gain,
        ln2_bias,
        w_up,
        b_up,
        w_down,
        b_down,
        cotangent,
    ):
        m = lax.axis_index("mp")
        w_out_other = swap_mp(w_out)
        row_count = tokens.shape[0]
        local_width = w_qkv.shape[2]
        seq_count, seq_len = doc_ids.shape
        seq_shape = (seq_count, seq_len, local_width // HD, HD)
        token_rows = tokens.astype(jnp.float32)
        normal_one, inv_one = normalize(token_rows)
        gain_one = ln1_gain.astype(jnp.float32)
        normed_one = (normal_one * gain_one + ln1_bias.astype(jnp.float32)).astype(jnp.bfloat16)
        projected = jnp.einsum(
            "td,dce->tce", normed_one, w_qkv, preferred_element_type=jnp.float32
        )
        bias_qv = b_qv.astype(jnp.float32)
        queries = (projected[:, 0] + bias_qv[0]).astype(jnp.bfloat16).reshape(seq_shape)
        key_rows = projected[:, 1].astype(jnp.bfloat16).reshape(seq_shape)
        value_rows = (projected[:, 2] + bias_qv[1]).astype(jnp.bfloat16).reshape(seq_shape)
        attended = []
        log_totals = []
        for s in range(seq_count):
            out_s, lse_s = attend_forward(queries[s], key_rows[s], value_rows[s], doc_ids[s])
            attended.append(out_s)
            log_totals.append(lse_s)
        mixed = jnp.stack(attended).reshape(row_count, local_width).astype(jnp.bfloat16)
        mixed_all = join_pair(mixed, swap_mp(mixed), m, 1)
        w_out_all = join_pair(w_out, w_out_other, m, 0)
        attn_all = jnp.dot(mixed_all, w_out_all, preferred_element_type=jnp.float32)
        after_attn = token_rows + attn_all + b_out.astype(jnp.float32)
        gain_two = ln2_gain.astype(jnp.float32)
        normal_two, inv_two = normalize(after_attn)
        normed_two = (normal_two * gain_two + ln2_bias.astype(jnp.float32)).astype(jnp.bfloat16)
        up_rows = jnp.dot(normed_two, w_up, preferred_element_type=jnp.float32) + b_up.astype(
            jnp.float32
        )
        activated, gelu_pull = jax.vjp(gelu_tanh, up_rows)
        act_rows = activated.astype(jnp.bfloat16)
        ffn_part = jnp.dot(act_rows, w_down, preferred_element_type=jnp.float32)

        cot_rows = cotangent.astype(jnp.float32)
        cot_own, _ = row_halves(cot_rows, m)
        grad_w_down_t = jnp.einsum(
            "td,tf->df", cotangent, act_rows, preferred_element_type=jnp.float32
        )
        grad_act = jnp.einsum("td,fd->tf", cotangent, w_down, preferred_element_type=jnp.float32)
        grad_up = gelu_pull(grad_act)[0].astype(jnp.bfloat16)
        grad_w_up = jnp.einsum("td,tf->df", normed_two, grad_up, preferred_element_type=jnp.float32)
        grad_b_up = jnp.sum(grad_up.astype(jnp.float32), axis=0)
        norm_two_part = jnp.einsum("tf,df->td", grad_up, w_up, preferred_element_type=jnp.float32)
        grad_two_own = scatter_rows_mp(norm_two_part, m, jnp.float32)
        normal_two_own, _ = row_halves(normal_two, m)
        inv_two_own, _ = row_halves(inv_two, m)
        grad_after_own = cot_own + norm_back(grad_two_own, normal_two_own, inv_two_own, gain_two)
        grad_attn_own = grad_after_own.astype(jnp.bfloat16)
        grad_attn_here = gather_rows_mp(grad_attn_own, m)
        ffn_late, grad_attn_here = lax.optimization_barrier((ffn_part, grad_attn_here))
        ffn_own = scatter_rows_mp(ffn_late, m, jnp.bfloat16)
        after_own, _ = row_halves(after_attn, m)
        out_own = (after_own + (ffn_own + b_down.astype(jnp.float32))).astype(jnp.bfloat16)
        block_out = gather_rows_mp(out_own, m)
        grad_w_out_t = jnp.einsum(
            "td,te->de", grad_attn_here, mixed, preferred_element_type=jnp.float32
        )
        grad_mixed = jnp.einsum(
            "td,ed->te", grad_attn_here, w_out, preferred_element_type=jnp.float32
        ).astype(jnp.bfloat16)
        grad_mixed = grad_mixed.reshape(seq_shape)
        gq, gk, gv = [], [], []
        for s in range(seq_count):
            dq_s, dk_s, dv_s = attend_backward(
                queries[s], key_rows[s], value_rows[s], doc_ids[s], log_totals[s], grad_mixed[s]
            )
            gq.append(dq_s)
            gk.append(dk_s)
            gv.append(dv_s)
        grad_q = jnp.stack(gq).reshape(row_count, local_width).astype(jnp.bfloat16)
        grad_k = jnp.stack(gk).reshape(row_count, local_width).astype(jnp.bfloat16)
        grad_v = jnp.stack(gv).reshape(row_count, local_width).astype(jnp.bfloat16)
        grad_proj = jnp.stack([grad_q, grad_k, grad_v], axis=1)
        grad_w_qkv = jnp.einsum(
            "td,tce->dce", normed_one, grad_proj, preferred_element_type=jnp.float32
        )
        grad_b_qv = jnp.stack(
            [
                jnp.sum(grad_q.astype(jnp.float32), axis=0),
                jnp.sum(grad_v.astype(jnp.float32), axis=0),
            ]
        )
        norm_one_part = jnp.einsum(
            "tce,dce->td", grad_proj, w_qkv, preferred_element_type=jnp.float32
        )
        grad_one_own = scatter_rows_mp(norm_one_part, m, jnp.float32)
        normal_one_own, _ = row_halves(normal_one, m)
        inv_one_own, _ = row_halves(inv_one, m)
        grad_input_own = grad_after_own + norm_back(
            grad_one_own, normal_one_own, inv_one_own, gain_one
        )
        grad_input = gather_rows_mp(grad_input_own, m)
        vector_terms = jnp.stack(
            [
                jnp.sum(grad_one_own * normal_one_own, axis=0),
                jnp.sum(grad_one_own, axis=0),
                jnp.sum(grad_two_own * normal_two_own, axis=0),
                jnp.sum(grad_two_own, axis=0),
                jnp.sum(grad_attn_own.astype(jnp.float32), axis=0),
                jnp.sum(cot_own, axis=0),
            ]
        )
        n_vec = vector_terms.size
        n_qv = grad_b_qv.size
        packed = jnp.concatenate([vector_terms.reshape(-1), grad_b_qv.reshape(-1), grad_b_up])
        packed = reduce_tree(packed, "dp", ndp)
        vector_sum = reduce_tree(packed[:n_vec], "mp", nmp).reshape(vector_terms.shape)
        qv_sum = packed[n_vec : n_vec + n_qv].reshape(grad_b_qv.shape)
        up_sum = packed[n_vec + n_qv :]
        sum_qkv = scatter_dp(grad_w_qkv, ndp)
        sum_out = scatter_dp(grad_w_out_t, ndp).T
        sum_up = scatter_dp(grad_w_up, ndp)
        sum_down = scatter_dp(grad_w_down_t, ndp).T
        return (
            block_out,
            grad_input,
            vector_sum[0],
            vector_sum[1],
            sum_qkv,
            qv_sum,
            sum_out,
            vector_sum[4],
            vector_sum[2],
            vector_sum[3],
            sum_up,
            up_sum,
            sum_down,
            vector_sum[5],
        )

    return shards_body


def solution(mesh):
    return jax.shard_map(
        make_shards(mesh.shape["dp"], mesh.shape["mp"]),
        mesh=mesh,
        in_specs=(
            P("dp", None),
            P("dp", None),
            P(),
            P(),
            P(None, None, "mp"),
            P(None, "mp"),
            P("mp", None),
            P(),
            P(),
            P(),
            P(None, "mp"),
            P("mp"),
            P("mp", None),
            P(),
            P("dp", None),
        ),
        out_specs=(
            P("dp", None),
            P("dp", None),
            P(),
            P(),
            P("dp", None, "mp"),
            P(None, "mp"),
            P("mp", "dp"),
            P(),
            P(),
            P(),
            P("dp", "mp"),
            P("mp"),
            P("mp", "dp"),
            P(),
        ),
        check_vma=False,
    )
```

```python
import math

import jax
import jax.numpy as jnp
from jax import lax
from jax.sharding import PartitionSpec as P


HD = 64


epsilon = 1e-05


def normalize(values):
    average = jnp.mean(values, axis=-1, keepdims=True)
    centered = values - average
    variance = jnp.mean(centered * centered, axis=-1, keepdims=True)
    inverse = lax.rsqrt(variance + epsilon)
    return (centered * inverse, inverse)


def norm_back(grad_out, normal_rows, inverse, gain):
    grad_unit = grad_out * gain
    return inverse * (
        grad_unit
        - jnp.mean(grad_unit, axis=-1, keepdims=True)
        - normal_rows * jnp.mean(grad_unit * normal_rows, axis=-1, keepdims=True)
    )


def gelu_tanh(values):
    return (
        0.5
        * values
        * (1.0 + jnp.tanh(0.7978845608028654 * (values + 0.044715 * values * values * values)))
    )


def key_end(offset, block_rows, seq_len):
    return min(seq_len, offset + block_rows)


def block_scores(query_block, key_rows, doc_rows, offset):
    block_rows = query_block.shape[0]
    kend = key_end(offset, block_rows, key_rows.shape[0])
    key_rows = key_rows[:kend]
    scores = jnp.einsum(
        "qhd,khd->hqk", query_block, key_rows, preferred_element_type=jnp.float32
    ) * (1.0 / math.sqrt(HD))
    query_pos = offset + lax.iota(jnp.int32, block_rows)
    key_pos = lax.iota(jnp.int32, key_rows.shape[0])
    block_docs = doc_rows[offset : offset + block_rows]
    allowed = (block_docs[:, None] == doc_rows[None, :kend]) & (query_pos[:, None] >= key_pos[None, :])
    return jnp.where(allowed[None], scores, -1e30)


def attend_forward(queries, key_rows, value_rows, doc_rows):
    seq_len = queries.shape[0]
    block_rows = min(512, seq_len)
    outputs = []
    log_parts = []
    for offset in range(0, seq_len, block_rows):
        scores = block_scores(queries[offset : offset + block_rows], key_rows, doc_rows, offset)
        row_max = jnp.max(scores, axis=-1, keepdims=True)
        log_total = row_max + jnp.log(jnp.sum(jnp.exp(scores - row_max), axis=-1, keepdims=True))
        probabilities = jnp.exp(scores - log_total).astype(jnp.bfloat16)
        kend = key_end(offset, block_rows, seq_len)
        outputs.append(
            jnp.einsum(
                "hqk,khd->qhd", probabilities, value_rows[:kend], preferred_element_type=jnp.float32
            )
        )
        log_parts.append(log_total[..., 0])
    return (jnp.concatenate(outputs, axis=0), jnp.concatenate(log_parts, axis=1))


def attend_backward(queries, key_rows, value_rows, doc_rows, log_totals, grad_out):
    seq_len = queries.shape[0]
    block_rows = min(512, seq_len)
    scale_factor = 1.0 / math.sqrt(HD)
    grad_queries = []
    grad_keys = jnp.zeros(key_rows.shape, jnp.float32)
    grad_values = jnp.zeros(value_rows.shape, jnp.float32)
    for offset in range(0, seq_len, block_rows):
      query_block = queries[offset : offset + block_rows]
      grad_block = grad_out[offset : offset + block_rows]
      kend = key_end(offset, block_rows, seq_len)
      scores = block_scores(query_block, key_rows, doc_rows, offset)
      probabilities = jnp.exp(scores - log_totals[:, offset : offset + block_rows, None])
      grad_probs = jnp.einsum(
          "qhd,khd->hqk", grad_block, value_rows[:kend], preferred_element_type=jnp.float32
      )
      row_dots = jnp.sum(probabilities * grad_probs, axis=-1, keepdims=True)
      grad_scores = (probabilities * (grad_probs - row_dots)).astype(jnp.bfloat16)
      grad_queries.append(
          scale_factor
          * jnp.einsum(
              "hqk,khd->qhd", grad_scores, key_rows[:kend], preferred_element_type=jnp.float32
          )
      )
      grad_keys = grad_keys.at[:kend].add(scale_factor * jnp.einsum(
          "hqk,qhd->khd", grad_scores, query_block, preferred_element_type=jnp.float32
      ))
      grad_values = grad_values.at[:kend].add(jnp.einsum(
          "hqk,qhd->khd",
          probabilities.astype(jnp.bfloat16),
          grad_block,
          preferred_element_type=jnp.float32,
      ))
    return (jnp.concatenate(grad_queries, axis=0), grad_keys, grad_values)


def swap_mp(x):
    return lax.ppermute(x, "mp", [(0, 1), (1, 0)])


def row_halves(x, m):
    half = x.shape[0] // 2
    own = lax.dynamic_slice_in_dim(x, m * half, half, axis=0)
    other = lax.dynamic_slice_in_dim(x, (1 - m) * half, half, axis=0)
    return own, other


def join_pair(own, other, m, axis):
    return jnp.where(
        m == 0,
        jnp.concatenate([own, other], axis=axis),
        jnp.concatenate([other, own], axis=axis),
    )


def scatter_rows_mp(partial, m, send_dtype):
    own, other = row_halves(partial, m)
    return own + swap_mp(other.astype(send_dtype)).astype(own.dtype)


def gather_rows_mp(own, m):
    return join_pair(own, swap_mp(own), m, 0)


def scatter_dp(x, ndp):
    idx = lax.axis_index("dp")
    bits = ndp.bit_length() - 1
    chunk = x.shape[0] // ndp
    rest = x.shape[1:]
    cur = x.reshape((2,) * bits + (chunk,) + rest)
    remaining = list(range(bits - 1, -1, -1))
    for bit in range(bits):
        pos = remaining.index(bit)
        mine = (idx >> bit) & 1
        keep = lax.dynamic_index_in_dim(cur, mine, pos, keepdims=False)
        send = lax.dynamic_index_in_dim(cur, 1 - mine, pos, keepdims=False)
        got = lax.ppermute(send, "dp", [(i, i ^ (1 << bit)) for i in range(ndp)])
        cur = keep + got
        remaining.pop(pos)
    return cur.reshape((chunk,) + rest)


def reduce_tree(x, name, size):
    bits = size.bit_length() - 1
    for bit in range(bits):
        x = x + lax.ppermute(x, name, [(i, i ^ (1 << bit)) for i in range(size)])
    return x


def make_shards(ndp, nmp):
    def shards_body(
        tokens,
        doc_ids,
        ln1_gain,
        ln1_bias,
        w_qkv,
        b_qv,
        w_out,
        b_out,
        ln2_gain,
        ln2_bias,
        w_up,
        b_up,
        w_down,
        b_down,
        cotangent,
    ):
        m = lax.axis_index("mp")
        w_out_other = swap_mp(w_out)
        row_count = tokens.shape[0]
        local_width = w_qkv.shape[2]
        seq_count, seq_len = doc_ids.shape
        seq_shape = (seq_count, seq_len, local_width // HD, HD)
        token_rows = tokens.astype(jnp.float32)
        normal_one, inv_one = normalize(token_rows)
        gain_one = ln1_gain.astype(jnp.float32)
        normed_one = (normal_one * gain_one + ln1_bias.astype(jnp.float32)).astype(jnp.bfloat16)
        projected = jnp.einsum(
            "td,dce->tce", normed_one, w_qkv, preferred_element_type=jnp.float32
        )
        bias_qv = b_qv.astype(jnp.float32)
        queries = (projected[:, 0] + bias_qv[0]).astype(jnp.bfloat16).reshape(seq_shape)
        key_rows = projected[:, 1].astype(jnp.bfloat16).reshape(seq_shape)
        value_rows = (projected[:, 2] + bias_qv[1]).astype(jnp.bfloat16).reshape(seq_shape)
        attended = []
        log_totals = []
        for s in range(seq_count):
            out_s, lse_s = attend_forward(queries[s], key_rows[s], value_rows[s], doc_ids[s])
            attended.append(out_s)
            log_totals.append(lse_s)
        mixed = jnp.stack(attended).reshape(row_count, local_width).astype(jnp.bfloat16)
        mixed_all = join_pair(mixed, swap_mp(mixed), m, 1)
        w_out_all = join_pair(w_out, w_out_other, m, 0)
        attn_all = jnp.dot(mixed_all, w_out_all, preferred_element_type=jnp.float32)
        after_attn = token_rows + attn_all + b_out.astype(jnp.float32)
        gain_two = ln2_gain.astype(jnp.float32)
        normal_two, inv_two = normalize(after_attn)
        normed_two = (normal_two * gain_two + ln2_bias.astype(jnp.float32)).astype(jnp.bfloat16)
        up_rows = jnp.dot(normed_two, w_up, preferred_element_type=jnp.float32) + b_up.astype(
            jnp.float32
        )
        activated, gelu_pull = jax.vjp(gelu_tanh, up_rows)
        act_rows = activated.astype(jnp.bfloat16)
        ffn_part = jnp.dot(act_rows, w_down, preferred_element_type=jnp.float32)

        cot_rows = cotangent.astype(jnp.float32)
        cot_own, _ = row_halves(cot_rows, m)
        grad_w_down_t = jnp.einsum(
            "td,tf->df", cotangent, act_rows, preferred_element_type=jnp.float32
        )
        grad_act = jnp.einsum("td,fd->tf", cotangent, w_down, preferred_element_type=jnp.float32)
        grad_up = gelu_pull(grad_act)[0].astype(jnp.bfloat16)
        grad_w_up = jnp.einsum("td,tf->df", normed_two, grad_up, preferred_element_type=jnp.float32)
        grad_b_up = jnp.sum(grad_up.astype(jnp.float32), axis=0)
        norm_two_part = jnp.einsum("tf,df->td", grad_up, w_up, preferred_element_type=jnp.float32)
        grad_two_own = scatter_rows_mp(norm_two_part, m, jnp.float32)
        normal_two_own, _ = row_halves(normal_two, m)
        inv_two_own, _ = row_halves(inv_two, m)
        grad_after_own = cot_own + norm_back(grad_two_own, normal_two_own, inv_two_own, gain_two)
        grad_attn_own = grad_after_own.astype(jnp.bfloat16)
        grad_attn_here = gather_rows_mp(grad_attn_own, m)
        ffn_late, grad_attn_here = lax.optimization_barrier((ffn_part, grad_attn_here))
        ffn_own = scatter_rows_mp(ffn_late, m, jnp.bfloat16)
        after_own, _ = row_halves(after_attn, m)
        out_own = (after_own + (ffn_own + b_down.astype(jnp.float32))).astype(jnp.bfloat16)
        block_out = gather_rows_mp(out_own, m)
        grad_w_out_t = jnp.einsum(
            "td,te->de", grad_attn_here, mixed, preferred_element_type=jnp.float32
        )
        grad_mixed = jnp.einsum(
            "td,ed->te", grad_attn_here, w_out, preferred_element_type=jnp.float32
        ).astype(jnp.bfloat16)
        grad_mixed = grad_mixed.reshape(seq_shape)
        gq, gk, gv = [], [], []
        for s in range(seq_count):
            dq_s, dk_s, dv_s = attend_backward(
                queries[s], key_rows[s], value_rows[s], doc_ids[s], log_totals[s], grad_mixed[s]
            )
            gq.append(dq_s)
            gk.append(dk_s)
            gv.append(dv_s)
        grad_q = jnp.stack(gq).reshape(row_count, local_width).astype(jnp.bfloat16)
        grad_k = jnp.stack(gk).reshape(row_count, local_width).astype(jnp.bfloat16)
        grad_v = jnp.stack(gv).reshape(row_count, local_width).astype(jnp.bfloat16)
        grad_proj = jnp.stack([grad_q, grad_k, grad_v], axis=1)
        grad_w_qkv = jnp.einsum(
            "td,tce->dce", normed_one, grad_proj, preferred_element_type=jnp.float32
        )
        grad_b_qv = jnp.stack(
            [
                jnp.sum(grad_q.astype(jnp.float32), axis=0),
                jnp.sum(grad_v.astype(jnp.float32), axis=0),
            ]
        )
        norm_one_part = jnp.einsum(
            "tce,dce->td", grad_proj, w_qkv, preferred_element_type=jnp.float32
        )
        grad_one_own = scatter_rows_mp(norm_one_part, m, jnp.float32)
        normal_one_own, _ = row_halves(normal_one, m)
        inv_one_own, _ = row_halves(inv_one, m)
        grad_input_own = grad_after_own + norm_back(
            grad_one_own, normal_one_own, inv_one_own, gain_one
        )
        grad_input = gather_rows_mp(grad_input_own, m)
        vector_terms = jnp.stack(
            [
                jnp.sum(grad_one_own * normal_one_own, axis=0),
                jnp.sum(grad_one_own, axis=0),
                jnp.sum(grad_two_own * normal_two_own, axis=0),
                jnp.sum(grad_two_own, axis=0),
                jnp.sum(grad_attn_own.astype(jnp.float32), axis=0),
                jnp.sum(cot_own, axis=0),
            ]
        )
        n_vec = vector_terms.size
        n_qv = grad_b_qv.size
        packed = jnp.concatenate([vector_terms.reshape(-1), grad_b_qv.reshape(-1), grad_b_up])
        sum_qkv = scatter_dp(grad_w_qkv, ndp)
        packed, sum_qkv = lax.optimization_barrier((packed, sum_qkv))
        packed = reduce_tree(packed, "dp", ndp)
        vector_sum = reduce_tree(packed[:n_vec], "mp", nmp).reshape(vector_terms.shape)
        qv_sum = packed[n_vec : n_vec + n_qv].reshape(grad_b_qv.shape)
        up_sum = packed[n_vec + n_qv :]
        sum_out = scatter_dp(grad_w_out_t, ndp).T
        sum_up = scatter_dp(grad_w_up, ndp)
        sum_down = scatter_dp(grad_w_down_t, ndp).T
        return (
            block_out,
            grad_input,
            vector_sum[0],
            vector_sum[1],
            sum_qkv,
            qv_sum,
            sum_out,
            vector_sum[4],
            vector_sum[2],
            vector_sum[3],
            sum_up,
            up_sum,
            sum_down,
            vector_sum[5],
        )

    return shards_body


def solution(mesh):
    return jax.shard_map(
        make_shards(mesh.shape["dp"], mesh.shape["mp"]),
        mesh=mesh,
        in_specs=(
            P("dp", None),
            P("dp", None),
            P(),
            P(),
            P(None, None, "mp"),
            P(None, "mp"),
            P("mp", None),
            P(),
            P(),
            P(),
            P(None, "mp"),
            P("mp"),
            P("mp", None),
            P(),
            P("dp", None),
        ),
        out_specs=(
            P("dp", None),
            P("dp", None),
            P(),
            P(),
            P("dp", None, "mp"),
            P(None, "mp"),
            P("mp", "dp"),
            P(),
            P(),
            P(),
            P("dp", "mp"),
            P("mp"),
            P("mp", "dp"),
            P(),
        ),
        check_vma=False,
    )
```

```python
import math

import jax
import jax.numpy as jnp
from jax import lax
from jax.sharding import PartitionSpec as P


HD = 64


epsilon = 1e-05


def normalize(values):
    average = jnp.mean(values, axis=-1, keepdims=True)
    centered = values - average
    variance = jnp.mean(centered * centered, axis=-1, keepdims=True)
    inverse = lax.rsqrt(variance + epsilon)
    return (centered * inverse, inverse)


def norm_back(grad_out, normal_rows, inverse, gain):
    grad_unit = grad_out * gain
    return inverse * (
        grad_unit
        - jnp.mean(grad_unit, axis=-1, keepdims=True)
        - normal_rows * jnp.mean(grad_unit * normal_rows, axis=-1, keepdims=True)
    )


def gelu_tanh(values):
    return (
        0.5
        * values
        * (1.0 + jnp.tanh(0.7978845608028654 * (values + 0.044715 * values * values * values)))
    )


def key_end(offset, block_rows, seq_len):
    return min(seq_len, offset + block_rows)


def block_scores(query_block, key_rows, doc_rows, offset):
    block_rows = query_block.shape[0]
    kend = key_end(offset, block_rows, key_rows.shape[0])
    key_rows = key_rows[:kend]
    scores = jnp.einsum(
        "qhd,khd->hqk", query_block, key_rows, preferred_element_type=jnp.float32
    ) * (1.0 / math.sqrt(HD))
    query_pos = offset + lax.iota(jnp.int32, block_rows)
    key_pos = lax.iota(jnp.int32, key_rows.shape[0])
    block_docs = doc_rows[offset : offset + block_rows]
    allowed = (block_docs[:, None] == doc_rows[None, :kend]) & (query_pos[:, None] >= key_pos[None, :])
    return jnp.where(allowed[None], scores, -1e30)


def attend_forward(queries, key_rows, value_rows, doc_rows):
    seq_len = queries.shape[0]
    block_rows = min(512, seq_len)
    outputs = []
    log_parts = []
    for offset in range(0, seq_len, block_rows):
      scores = block_scores(queries[offset : offset + block_rows], key_rows, doc_rows, offset)
      row_max = jnp.max(scores, axis=-1, keepdims=True)
      log_total = row_max + jnp.log(jnp.sum(jnp.exp(scores - row_max), axis=-1, keepdims=True))
      probabilities = jnp.exp(scores - log_total).astype(jnp.bfloat16)
      kend = key_end(offset, block_rows, seq_len)
      outputs.append(
          jnp.einsum(
              "hqk,khd->qhd", probabilities, value_rows[:kend], preferred_element_type=jnp.float32
          )
      )
      log_parts.append(log_total[..., 0])
    return (jnp.concatenate(outputs, axis=0), jnp.concatenate(log_parts, axis=1))


def attend_backward(queries, key_rows, value_rows, doc_rows, log_totals, grad_out):
    seq_len = queries.shape[0]
    block_rows = min(512, seq_len)
    scale_factor = 1.0 / math.sqrt(HD)
    grad_queries = []
    grad_keys = jnp.zeros(key_rows.shape, jnp.float32)
    grad_values = jnp.zeros(value_rows.shape, jnp.float32)
    for offset in range(0, seq_len, block_rows):
      query_block = queries[offset : offset + block_rows]
      grad_block = grad_out[offset : offset + block_rows]
      kend = key_end(offset, block_rows, seq_len)
      scores = block_scores(query_block, key_rows, doc_rows, offset)
      probabilities = jnp.exp(scores - log_totals[:, offset : offset + block_rows, None])
      grad_probs = jnp.einsum(
          "qhd,khd->hqk", grad_block, value_rows[:kend], preferred_element_type=jnp.float32
      )
      row_dots = jnp.sum(probabilities * grad_probs, axis=-1, keepdims=True)
      grad_scores = (probabilities * (grad_probs - row_dots)).astype(jnp.bfloat16)
      grad_queries.append(
          scale_factor
          * jnp.einsum(
              "hqk,khd->qhd", grad_scores, key_rows[:kend], preferred_element_type=jnp.float32
          )
      )
      grad_keys = grad_keys.at[:kend].add(scale_factor * jnp.einsum(
          "hqk,qhd->khd", grad_scores, query_block, preferred_element_type=jnp.float32
      ))
      grad_values = grad_values.at[:kend].add(jnp.einsum(
          "hqk,qhd->khd",
          probabilities.astype(jnp.bfloat16),
          grad_block,
          preferred_element_type=jnp.float32,
      ))
    return (jnp.concatenate(grad_queries, axis=0), grad_keys, grad_values)


def swap_mp(x):
    return lax.ppermute(x, "mp", [(0, 1), (1, 0)])


def row_halves(x, m):
    half = x.shape[0] // 2
    own = lax.dynamic_slice_in_dim(x, m * half, half, axis=0)
    other = lax.dynamic_slice_in_dim(x, (1 - m) * half, half, axis=0)
    return own, other


def join_pair(own, other, m, axis):
    return jnp.where(
        m == 0,
        jnp.concatenate([own, other], axis=axis),
        jnp.concatenate([other, own], axis=axis),
    )


def scatter_rows_mp(partial, m, send_dtype):
    own, other = row_halves(partial, m)
    return own + swap_mp(other.astype(send_dtype)).astype(own.dtype)


def gather_rows_mp(own, m):
    return join_pair(own, swap_mp(own), m, 0)


def scatter_dp(x, ndp):
    idx = lax.axis_index("dp")
    bits = ndp.bit_length() - 1
    chunk = x.shape[0] // ndp
    rest = x.shape[1:]
    cur = x.reshape((2,) * bits + (chunk,) + rest)
    remaining = list(range(bits - 1, -1, -1))
    for bit in range(bits):
        pos = remaining.index(bit)
        mine = (idx >> bit) & 1
        keep = lax.dynamic_index_in_dim(cur, mine, pos, keepdims=False)
        send = lax.dynamic_index_in_dim(cur, 1 - mine, pos, keepdims=False)
        got = lax.ppermute(send, "dp", [(i, i ^ (1 << bit)) for i in range(ndp)])
        cur = keep + got
        remaining.pop(pos)
    return cur.reshape((chunk,) + rest)


def reduce_tree(x, name, size):
    bits = size.bit_length() - 1
    for bit in range(bits):
        x = x + lax.ppermute(x, name, [(i, i ^ (1 << bit)) for i in range(size)])
    return x


def make_shards(ndp, nmp):
    def shards_body(
        tokens,
        doc_ids,
        ln1_gain,
        ln1_bias,
        w_qkv,
        b_qv,
        w_out,
        b_out,
        ln2_gain,
        ln2_bias,
        w_up,
        b_up,
        w_down,
        b_down,
        cotangent,
    ):
        m = lax.axis_index("mp")
        w_out_other = swap_mp(w_out)
        row_count = tokens.shape[0]
        local_width = w_qkv.shape[2]
        seq_count, seq_len = doc_ids.shape
        seq_shape = (seq_count, seq_len, local_width // HD, HD)
        token_rows = tokens.astype(jnp.float32)
        normal_one, inv_one = normalize(token_rows)
        gain_one = ln1_gain.astype(jnp.float32)
        normed_one = (normal_one * gain_one + ln1_bias.astype(jnp.float32)).astype(jnp.bfloat16)
        projected = jnp.einsum(
            "td,dce->tce", normed_one, w_qkv, preferred_element_type=jnp.float32
        )
        bias_qv = b_qv.astype(jnp.float32)
        queries = (projected[:, 0] + bias_qv[0]).astype(jnp.bfloat16).reshape(seq_shape)
        key_rows = projected[:, 1].astype(jnp.bfloat16).reshape(seq_shape)
        value_rows = (projected[:, 2] + bias_qv[1]).astype(jnp.bfloat16).reshape(seq_shape)
        attended = []
        log_totals = []
        for s in range(seq_count):
            out_s, lse_s = attend_forward(queries[s], key_rows[s], value_rows[s], doc_ids[s])
            attended.append(out_s)
            log_totals.append(lse_s)
        mixed = jnp.stack(attended).reshape(row_count, local_width).astype(jnp.bfloat16)
        w_out_all = join_pair(w_out, w_out_other, m, 0)
        half_rows = row_count // 2
        attn_parts = []
        for part in range(2):
            rows = mixed[part * half_rows : (part + 1) * half_rows]
            rows_other = swap_mp(rows)
            attn_parts.append(
                jnp.dot(join_pair(rows, rows_other, m, 1), w_out_all,
                        preferred_element_type=jnp.float32)
            )
        attn_all = jnp.concatenate(attn_parts, axis=0)
        after_attn = token_rows + attn_all + b_out.astype(jnp.float32)
        gain_two = ln2_gain.astype(jnp.float32)
        normal_two, inv_two = normalize(after_attn)
        normed_two = (normal_two * gain_two + ln2_bias.astype(jnp.float32)).astype(jnp.bfloat16)
        up_rows = jnp.dot(normed_two, w_up, preferred_element_type=jnp.float32) + b_up.astype(
            jnp.float32
        )
        activated, gelu_pull = jax.vjp(gelu_tanh, up_rows)
        act_rows = activated.astype(jnp.bfloat16)
        ffn_part = jnp.dot(act_rows, w_down, preferred_element_type=jnp.float32)

        cot_rows = cotangent.astype(jnp.float32)
        cot_own, _ = row_halves(cot_rows, m)
        grad_w_down_t = jnp.einsum(
            "td,tf->df", cotangent, act_rows, preferred_element_type=jnp.float32
        )
        grad_act = jnp.einsum("td,fd->tf", cotangent, w_down, preferred_element_type=jnp.float32)
        grad_up = gelu_pull(grad_act)[0].astype(jnp.bfloat16)
        grad_w_up = jnp.einsum("td,tf->df", normed_two, grad_up, preferred_element_type=jnp.float32)
        grad_b_up = jnp.sum(grad_up.astype(jnp.float32), axis=0)
        norm_two_part = jnp.einsum("tf,df->td", grad_up, w_up, preferred_element_type=jnp.float32)
        grad_two_own = scatter_rows_mp(norm_two_part, m, jnp.bfloat16)
        normal_two_own, _ = row_halves(normal_two, m)
        inv_two_own, _ = row_halves(inv_two, m)
        grad_after_own = cot_own + norm_back(grad_two_own, normal_two_own, inv_two_own, gain_two)
        grad_attn_own = grad_after_own.astype(jnp.bfloat16)
        grad_attn_here = gather_rows_mp(grad_attn_own, m)
        ffn_late, grad_attn_here = lax.optimization_barrier((ffn_part, grad_attn_here))
        ffn_own = scatter_rows_mp(ffn_late, m, jnp.bfloat16)
        after_own, _ = row_halves(after_attn, m)
        out_own = (after_own + (ffn_own + b_down.astype(jnp.float32))).astype(jnp.bfloat16)
        block_out = gather_rows_mp(out_own, m)
        grad_w_out_t = jnp.einsum(
            "td,te->de", grad_attn_here, mixed, preferred_element_type=jnp.float32
        )
        grad_mixed = jnp.einsum(
            "td,ed->te", grad_attn_here, w_out, preferred_element_type=jnp.float32
        ).astype(jnp.bfloat16)
        grad_mixed = grad_mixed.reshape(seq_shape)
        gq, gk, gv = [], [], []
        for s in range(seq_count):
            dq_s, dk_s, dv_s = attend_backward(
                queries[s], key_rows[s], value_rows[s], doc_ids[s], log_totals[s], grad_mixed[s]
            )
            gq.append(dq_s)
            gk.append(dk_s)
            gv.append(dv_s)
        grad_q = jnp.stack(gq).reshape(row_count, local_width).astype(jnp.bfloat16)
        grad_k = jnp.stack(gk).reshape(row_count, local_width).astype(jnp.bfloat16)
        grad_v = jnp.stack(gv).reshape(row_count, local_width).astype(jnp.bfloat16)
        grad_proj = jnp.stack([grad_q, grad_k, grad_v], axis=1)
        grad_w_qkv = jnp.einsum(
            "td,tce->dce", normed_one, grad_proj, preferred_element_type=jnp.float32
        )
        grad_b_qv = jnp.stack(
            [
                jnp.sum(grad_q.astype(jnp.float32), axis=0),
                jnp.sum(grad_v.astype(jnp.float32), axis=0),
            ]
        )
        norm_one_part = jnp.einsum(
            "tce,dce->td", grad_proj, w_qkv, preferred_element_type=jnp.float32
        )
        grad_one_own = scatter_rows_mp(norm_one_part, m, jnp.bfloat16)
        normal_one_own, _ = row_halves(normal_one, m)
        inv_one_own, _ = row_halves(inv_one, m)
        grad_input_own = grad_after_own + norm_back(
            grad_one_own, normal_one_own, inv_one_own, gain_one
        )
        grad_input = gather_rows_mp(grad_input_own, m)
        vector_terms = jnp.stack(
            [
                jnp.sum(grad_one_own * normal_one_own, axis=0),
                jnp.sum(grad_one_own, axis=0),
                jnp.sum(grad_two_own * normal_two_own, axis=0),
                jnp.sum(grad_two_own, axis=0),
                jnp.sum(grad_attn_own.astype(jnp.float32), axis=0),
                jnp.sum(cot_own, axis=0),
            ]
        )
        n_vec = vector_terms.size
        n_qv = grad_b_qv.size
        packed = jnp.concatenate([vector_terms.reshape(-1), grad_b_qv.reshape(-1), grad_b_up])
        sum_qkv = scatter_dp(grad_w_qkv, ndp)
        packed, sum_qkv = lax.optimization_barrier((packed, sum_qkv))
        packed = reduce_tree(packed, "dp", ndp)
        vector_sum = reduce_tree(packed[:n_vec], "mp", nmp).reshape(vector_terms.shape)
        qv_sum = packed[n_vec : n_vec + n_qv].reshape(grad_b_qv.shape)
        up_sum = packed[n_vec + n_qv :]
        sum_out = scatter_dp(grad_w_out_t, ndp).T
        sum_up = scatter_dp(grad_w_up, ndp)
        sum_down = scatter_dp(grad_w_down_t, ndp).T
        return (
            block_out,
            grad_input,
            vector_sum[0],
            vector_sum[1],
            sum_qkv,
            qv_sum,
            sum_out,
            vector_sum[4],
            vector_sum[2],
            vector_sum[3],
            sum_up,
            up_sum,
            sum_down,
            vector_sum[5],
        )

    return shards_body


def solution(mesh):
    return jax.shard_map(
        make_shards(mesh.shape["dp"], mesh.shape["mp"]),
        mesh=mesh,
        in_specs=(
            P("dp", None),
            P("dp", None),
            P(),
            P(),
            P(None, None, "mp"),
            P(None, "mp"),
            P("mp", None),
            P(),
            P(),
            P(),
            P(None, "mp"),
            P("mp"),
            P("mp", None),
            P(),
            P("dp", None),
        ),
        out_specs=(
            P("dp", None),
            P("dp", None),
            P(),
            P(),
            P("dp", None, "mp"),
            P(None, "mp"),
            P("mp", "dp"),
            P(),
            P(),
            P(),
            P("dp", "mp"),
            P("mp"),
            P("mp", "dp"),
            P(),
        ),
        check_vma=False,
    )
```

```python
import math

import jax
import jax.numpy as jnp
from jax import lax
from jax.sharding import PartitionSpec as P


HD = 64


epsilon = 1e-05


def normalize(values):
    average = jnp.mean(values, axis=-1, keepdims=True)
    centered = values - average
    variance = jnp.mean(centered * centered, axis=-1, keepdims=True)
    inverse = lax.rsqrt(variance + epsilon)
    return (centered * inverse, inverse)


def norm_back(grad_out, normal_rows, inverse, gain):
    grad_unit = grad_out * gain
    return inverse * (
        grad_unit
        - jnp.mean(grad_unit, axis=-1, keepdims=True)
        - normal_rows * jnp.mean(grad_unit * normal_rows, axis=-1, keepdims=True)
    )


def gelu_tanh(values):
    return (
        0.5
        * values
        * (1.0 + jnp.tanh(0.7978845608028654 * (values + 0.044715 * values * values * values)))
    )


def key_end(offset, block_rows, seq_len):
    return min(seq_len, offset + block_rows)


def block_scores(query_block, key_rows, doc_rows, offset):
    block_rows = query_block.shape[0]
    kend = key_end(offset, block_rows, key_rows.shape[0])
    key_rows = key_rows[:kend]
    scores = jnp.einsum(
        "qhd,khd->hqk", query_block, key_rows, preferred_element_type=jnp.float32
    ) * (1.0 / math.sqrt(HD))
    query_pos = offset + lax.iota(jnp.int32, block_rows)
    key_pos = lax.iota(jnp.int32, key_rows.shape[0])
    block_docs = doc_rows[offset : offset + block_rows]
    allowed = (block_docs[:, None] == doc_rows[None, :kend]) & (query_pos[:, None] >= key_pos[None, :])
    return jnp.where(allowed[None], scores, -1e30)


def attend_forward(queries, key_rows, value_rows, doc_rows):
    seq_len = queries.shape[0]
    block_rows = min(512, seq_len)
    outputs = []
    log_parts = []
    for offset in range(0, seq_len, block_rows):
      scores = block_scores(queries[offset : offset + block_rows], key_rows, doc_rows, offset)
      row_max = jnp.max(scores, axis=-1, keepdims=True)
      log_total = row_max + jnp.log(jnp.sum(jnp.exp(scores - row_max), axis=-1, keepdims=True))
      probabilities = jnp.exp(scores - log_total).astype(jnp.bfloat16)
      kend = key_end(offset, block_rows, seq_len)
      outputs.append(
          jnp.einsum(
              "hqk,khd->qhd", probabilities, value_rows[:kend], preferred_element_type=jnp.float32
          )
      )
      log_parts.append(log_total[..., 0])
    return (jnp.concatenate(outputs, axis=0), jnp.concatenate(log_parts, axis=1))


def attend_backward(queries, key_rows, value_rows, doc_rows, log_totals, grad_out):
    seq_len = queries.shape[0]
    block_rows = min(512, seq_len)
    scale_factor = 1.0 / math.sqrt(HD)
    grad_queries = []
    grad_keys = jnp.zeros(key_rows.shape, jnp.float32)
    grad_values = jnp.zeros(value_rows.shape, jnp.float32)
    for offset in range(0, seq_len, block_rows):
      query_block = queries[offset : offset + block_rows]
      grad_block = grad_out[offset : offset + block_rows]
      kend = key_end(offset, block_rows, seq_len)
      scores = block_scores(query_block, key_rows, doc_rows, offset)
      probabilities = jnp.exp(scores - log_totals[:, offset : offset + block_rows, None])
      grad_probs = jnp.einsum(
          "qhd,khd->hqk", grad_block, value_rows[:kend], preferred_element_type=jnp.float32
      )
      row_dots = jnp.sum(probabilities * grad_probs, axis=-1, keepdims=True)
      grad_scores = (probabilities * (grad_probs - row_dots)).astype(jnp.bfloat16)
      grad_queries.append(
          scale_factor
          * jnp.einsum(
              "hqk,khd->qhd", grad_scores, key_rows[:kend], preferred_element_type=jnp.float32
          )
      )
      grad_keys = grad_keys.at[:kend].add(scale_factor * jnp.einsum(
          "hqk,qhd->khd", grad_scores, query_block, preferred_element_type=jnp.float32
      ))
      grad_values = grad_values.at[:kend].add(jnp.einsum(
          "hqk,qhd->khd",
          probabilities.astype(jnp.bfloat16),
          grad_block,
          preferred_element_type=jnp.float32,
      ))
    return (jnp.concatenate(grad_queries, axis=0), grad_keys, grad_values)


def swap_mp(x):
    return lax.ppermute(x, "mp", [(0, 1), (1, 0)])


def row_halves(x, m):
    half = x.shape[0] // 2
    own = lax.dynamic_slice_in_dim(x, m * half, half, axis=0)
    other = lax.dynamic_slice_in_dim(x, (1 - m) * half, half, axis=0)
    return own, other


def join_pair(own, other, m, axis):
    return jnp.where(
        m == 0,
        jnp.concatenate([own, other], axis=axis),
        jnp.concatenate([other, own], axis=axis),
    )


def scatter_rows_mp(partial, m, send_dtype):
    own, other = row_halves(partial, m)
    return own + swap_mp(other.astype(send_dtype)).astype(own.dtype)


def gather_rows_mp(own, m):
    return join_pair(own, swap_mp(own), m, 0)


def scatter_dp(x, ndp, swap=False):
    idx = lax.axis_index("dp")
    bits = ndp.bit_length() - 1
    chunk = x.shape[0] // ndp
    rest = x.shape[1:]
    cur = x.reshape((2,) * bits + (chunk,) + rest)
    remaining = list(range(bits - 1, -1, -1))
    order = list(range(bits))
    if swap and bits >= 3:
        order[1], order[2] = order[2], order[1]
    for bit in order:
        pos = remaining.index(bit)
        mine = (idx >> bit) & 1
        keep = lax.dynamic_index_in_dim(cur, mine, pos, keepdims=False)
        send = lax.dynamic_index_in_dim(cur, 1 - mine, pos, keepdims=False)
        got = lax.ppermute(send, "dp", [(i, i ^ (1 << bit)) for i in range(ndp)])
        cur = keep + got
        remaining.pop(pos)
    return cur.reshape((chunk,) + rest)


def reduce_tree(x, name, size):
    bits = size.bit_length() - 1
    for bit in range(bits):
        x = x + lax.ppermute(x, name, [(i, i ^ (1 << bit)) for i in range(size)])
    return x


def make_shards(ndp, nmp):
    def shards_body(
        tokens,
        doc_ids,
        ln1_gain,
        ln1_bias,
        w_qkv,
        b_qv,
        w_out,
        b_out,
        ln2_gain,
        ln2_bias,
        w_up,
        b_up,
        w_down,
        b_down,
        cotangent,
    ):
        m = lax.axis_index("mp")
        w_out_other = swap_mp(w_out)
        row_count = tokens.shape[0]
        local_width = w_qkv.shape[2]
        seq_count, seq_len = doc_ids.shape
        seq_shape = (seq_count, seq_len, local_width // HD, HD)
        token_rows = tokens.astype(jnp.float32)
        normal_one, inv_one = normalize(token_rows)
        gain_one = ln1_gain.astype(jnp.float32)
        normed_one = (normal_one * gain_one + ln1_bias.astype(jnp.float32)).astype(jnp.bfloat16)
        projected = jnp.einsum(
            "td,dce->tce", normed_one, w_qkv, preferred_element_type=jnp.float32
        )
        bias_qv = b_qv.astype(jnp.float32)
        queries = (projected[:, 0] + bias_qv[0]).astype(jnp.bfloat16).reshape(seq_shape)
        key_rows = projected[:, 1].astype(jnp.bfloat16).reshape(seq_shape)
        value_rows = (projected[:, 2] + bias_qv[1]).astype(jnp.bfloat16).reshape(seq_shape)
        attended = []
        log_totals = []
        for s in range(seq_count):
            out_s, lse_s = attend_forward(queries[s], key_rows[s], value_rows[s], doc_ids[s])
            attended.append(out_s)
            log_totals.append(lse_s)
        mixed = jnp.stack(attended).reshape(row_count, local_width).astype(jnp.bfloat16)
        w_out_all = join_pair(w_out, w_out_other, m, 0)
        half_rows = row_count // 2
        attn_parts = []
        for part in range(2):
            rows = mixed[part * half_rows : (part + 1) * half_rows]
            rows_other = swap_mp(rows)
            attn_parts.append(
                jnp.dot(join_pair(rows, rows_other, m, 1), w_out_all,
                        preferred_element_type=jnp.float32)
            )
        attn_all = jnp.concatenate(attn_parts, axis=0)
        after_attn = token_rows + attn_all + b_out.astype(jnp.float32)
        gain_two = ln2_gain.astype(jnp.float32)
        normal_two, inv_two = normalize(after_attn)
        normed_two = (normal_two * gain_two + ln2_bias.astype(jnp.float32)).astype(jnp.bfloat16)
        up_rows = jnp.dot(normed_two, w_up, preferred_element_type=jnp.float32) + b_up.astype(
            jnp.float32
        )
        activated, gelu_pull = jax.vjp(gelu_tanh, up_rows)
        act_rows = activated.astype(jnp.bfloat16)
        ffn_part = jnp.dot(act_rows, w_down, preferred_element_type=jnp.float32)

        cot_rows = cotangent.astype(jnp.float32)
        cot_own, _ = row_halves(cot_rows, m)
        grad_w_down_t = jnp.einsum(
            "td,tf->df", cotangent, act_rows, preferred_element_type=jnp.float32
        )
        grad_act = jnp.einsum("td,fd->tf", cotangent, w_down, preferred_element_type=jnp.float32)
        grad_up = gelu_pull(grad_act)[0].astype(jnp.bfloat16)
        grad_w_up = jnp.einsum("td,tf->df", normed_two, grad_up, preferred_element_type=jnp.float32)
        grad_b_up = jnp.sum(grad_up.astype(jnp.float32), axis=0)
        norm_two_part = jnp.einsum("tf,df->td", grad_up, w_up, preferred_element_type=jnp.float32)
        grad_two_own = scatter_rows_mp(norm_two_part, m, jnp.bfloat16)
        normal_two_own, _ = row_halves(normal_two, m)
        inv_two_own, _ = row_halves(inv_two, m)
        grad_after_own = cot_own + norm_back(grad_two_own, normal_two_own, inv_two_own, gain_two)
        grad_attn_own = grad_after_own.astype(jnp.bfloat16)
        grad_attn_here = gather_rows_mp(grad_attn_own, m)
        ffn_late, grad_attn_here = lax.optimization_barrier((ffn_part, grad_attn_here))
        ffn_own = scatter_rows_mp(ffn_late, m, jnp.bfloat16)
        after_own, _ = row_halves(after_attn, m)
        out_own = (after_own + (ffn_own + b_down.astype(jnp.float32))).astype(jnp.bfloat16)
        block_out = gather_rows_mp(out_own, m)
        grad_w_out_t = jnp.einsum(
            "td,te->de", grad_attn_here, mixed, preferred_element_type=jnp.float32
        )
        grad_mixed = jnp.einsum(
            "td,ed->te", grad_attn_here, w_out, preferred_element_type=jnp.float32
        ).astype(jnp.bfloat16)
        grad_mixed = grad_mixed.reshape(seq_shape)
        gq, gk, gv = [], [], []
        for s in range(seq_count):
            dq_s, dk_s, dv_s = attend_backward(
                queries[s], key_rows[s], value_rows[s], doc_ids[s], log_totals[s], grad_mixed[s]
            )
            gq.append(dq_s)
            gk.append(dk_s)
            gv.append(dv_s)
        grad_q = jnp.stack(gq).reshape(row_count, local_width).astype(jnp.bfloat16)
        grad_k = jnp.stack(gk).reshape(row_count, local_width).astype(jnp.bfloat16)
        grad_v = jnp.stack(gv).reshape(row_count, local_width).astype(jnp.bfloat16)
        grad_proj = jnp.stack([grad_q, grad_k, grad_v], axis=1)
        grad_w_qkv = jnp.einsum(
            "td,tce->dce", normed_one, grad_proj, preferred_element_type=jnp.float32
        )
        grad_b_qv = jnp.stack(
            [
                jnp.sum(grad_q.astype(jnp.float32), axis=0),
                jnp.sum(grad_v.astype(jnp.float32), axis=0),
            ]
        )
        norm_one_part = jnp.einsum(
            "tce,dce->td", grad_proj, w_qkv, preferred_element_type=jnp.float32
        )
        grad_one_own = scatter_rows_mp(norm_one_part, m, jnp.bfloat16)
        normal_one_own, _ = row_halves(normal_one, m)
        inv_one_own, _ = row_halves(inv_one, m)
        grad_input_own = grad_after_own + norm_back(
            grad_one_own, normal_one_own, inv_one_own, gain_one
        )
        grad_input = gather_rows_mp(grad_input_own, m)
        vector_terms = jnp.stack(
            [
                jnp.sum(grad_one_own * normal_one_own, axis=0),
                jnp.sum(grad_one_own, axis=0),
                jnp.sum(grad_two_own * normal_two_own, axis=0),
                jnp.sum(grad_two_own, axis=0),
                jnp.sum(grad_attn_own.astype(jnp.float32), axis=0),
                jnp.sum(cot_own, axis=0),
            ]
        )
        n_vec = vector_terms.size
        n_qv = grad_b_qv.size
        packed = jnp.concatenate([vector_terms.reshape(-1), grad_b_qv.reshape(-1), grad_b_up])
        qkv_cols = grad_w_qkv.shape[2] // 2
        sum_qkv = jnp.concatenate(
            [
                scatter_dp(grad_w_qkv[:, :, :qkv_cols], ndp),
                scatter_dp(grad_w_qkv[:, :, qkv_cols:], ndp, swap=True),
            ],
            axis=2,
        )
        packed, sum_qkv = lax.optimization_barrier((packed, sum_qkv))
        packed = reduce_tree(packed, "dp", ndp)
        vector_sum = reduce_tree(packed[:n_vec], "mp", nmp).reshape(vector_terms.shape)
        qv_sum = packed[n_vec : n_vec + n_qv].reshape(grad_b_qv.shape)
        up_sum = packed[n_vec + n_qv :]
        sum_out = scatter_dp(grad_w_out_t, ndp).T
        sum_up = scatter_dp(grad_w_up, ndp)
        sum_down = scatter_dp(grad_w_down_t, ndp, swap=True).T
        return (
            block_out,
            grad_input,
            vector_sum[0],
            vector_sum[1],
            sum_qkv,
            qv_sum,
            sum_out,
            vector_sum[4],
            vector_sum[2],
            vector_sum[3],
            sum_up,
            up_sum,
            sum_down,
            vector_sum[5],
        )

    return shards_body


def solution(mesh):
    return jax.shard_map(
        make_shards(mesh.shape["dp"], mesh.shape["mp"]),
        mesh=mesh,
        in_specs=(
            P("dp", None),
            P("dp", None),
            P(),
            P(),
            P(None, None, "mp"),
            P(None, "mp"),
            P("mp", None),
            P(),
            P(),
            P(),
            P(None, "mp"),
            P("mp"),
            P("mp", None),
            P(),
            P("dp", None),
        ),
        out_specs=(
            P("dp", None),
            P("dp", None),
            P(),
            P(),
            P("dp", None, "mp"),
            P(None, "mp"),
            P("mp", "dp"),
            P(),
            P(),
            P(),
            P("dp", "mp"),
            P("mp"),
            P("mp", "dp"),
            P(),
        ),
        check_vma=False,
    )
```

```python
import math

import jax
import jax.numpy as jnp
from jax import lax
from jax.sharding import PartitionSpec as P


HD = 64


epsilon = 1e-05


def normalize(values):
    average = jnp.mean(values, axis=-1, keepdims=True)
    centered = values - average
    variance = jnp.mean(centered * centered, axis=-1, keepdims=True)
    inverse = lax.rsqrt(variance + epsilon)
    return (centered * inverse, inverse)


def norm_back(grad_out, normal_rows, inverse, gain):
    grad_unit = grad_out * gain
    return inverse * (
        grad_unit
        - jnp.mean(grad_unit, axis=-1, keepdims=True)
        - normal_rows * jnp.mean(grad_unit * normal_rows, axis=-1, keepdims=True)
    )


def gelu_tanh(values):
    return (
        0.5
        * values
        * (1.0 + jnp.tanh(0.7978845608028654 * (values + 0.044715 * values * values * values)))
    )


def key_end(offset, block_rows, seq_len):
    return min(seq_len, offset + block_rows)


def block_scores(query_block, key_rows, doc_rows, offset):
    block_rows = query_block.shape[0]
    kend = key_end(offset, block_rows, key_rows.shape[0])
    key_rows = key_rows[:kend]
    scores = jnp.einsum(
        "qhd,khd->hqk", query_block, key_rows, preferred_element_type=jnp.float32
    ) * (1.0 / math.sqrt(HD))
    query_pos = offset + lax.iota(jnp.int32, block_rows)
    key_pos = lax.iota(jnp.int32, key_rows.shape[0])
    block_docs = doc_rows[offset : offset + block_rows]
    allowed = (block_docs[:, None] == doc_rows[None, :kend]) & (query_pos[:, None] >= key_pos[None, :])
    return jnp.where(allowed[None], scores, -1e30)


def attend_forward(queries, key_rows, value_rows, doc_rows):
    seq_len = queries.shape[0]
    block_rows = min(512, seq_len)
    outputs = []
    log_parts = []
    for offset in range(0, seq_len, block_rows):
      scores = block_scores(queries[offset : offset + block_rows], key_rows, doc_rows, offset)
      row_max = jnp.max(scores, axis=-1, keepdims=True)
      log_total = row_max + jnp.log(jnp.sum(jnp.exp(scores - row_max), axis=-1, keepdims=True))
      probabilities = jnp.exp(scores - log_total).astype(jnp.bfloat16)
      kend = key_end(offset, block_rows, seq_len)
      outputs.append(
          jnp.einsum(
              "hqk,khd->qhd", probabilities, value_rows[:kend], preferred_element_type=jnp.float32
          )
      )
      log_parts.append(log_total[..., 0])
    return (jnp.concatenate(outputs, axis=0), jnp.concatenate(log_parts, axis=1))


def attend_backward(queries, key_rows, value_rows, doc_rows, log_totals, grad_out):
    seq_len = queries.shape[0]
    block_rows = min(512, seq_len)
    scale_factor = 1.0 / math.sqrt(HD)
    grad_queries = []
    grad_keys = jnp.zeros(key_rows.shape, jnp.float32)
    grad_values = jnp.zeros(value_rows.shape, jnp.float32)
    for offset in range(0, seq_len, block_rows):
      query_block = queries[offset : offset + block_rows]
      grad_block = grad_out[offset : offset + block_rows]
      kend = key_end(offset, block_rows, seq_len)
      scores = block_scores(query_block, key_rows, doc_rows, offset)
      probabilities = jnp.exp(scores - log_totals[:, offset : offset + block_rows, None])
      grad_probs = jnp.einsum(
          "qhd,khd->hqk", grad_block, value_rows[:kend], preferred_element_type=jnp.float32
      )
      row_dots = jnp.sum(probabilities * grad_probs, axis=-1, keepdims=True)
      grad_scores = (probabilities * (grad_probs - row_dots)).astype(jnp.bfloat16)
      grad_queries.append(
          scale_factor
          * jnp.einsum(
              "hqk,khd->qhd", grad_scores, key_rows[:kend], preferred_element_type=jnp.float32
          )
      )
      grad_keys = grad_keys.at[:kend].add(scale_factor * jnp.einsum(
          "hqk,qhd->khd", grad_scores, query_block, preferred_element_type=jnp.float32
      ))
      grad_values = grad_values.at[:kend].add(jnp.einsum(
          "hqk,qhd->khd",
          probabilities.astype(jnp.bfloat16),
          grad_block,
          preferred_element_type=jnp.float32,
      ))
    return (jnp.concatenate(grad_queries, axis=0), grad_keys, grad_values)


def swap_mp(x):
    return lax.ppermute(x, "mp", [(0, 1), (1, 0)])


def row_halves(x, m):
    half = x.shape[0] // 2
    own = lax.dynamic_slice_in_dim(x, m * half, half, axis=0)
    other = lax.dynamic_slice_in_dim(x, (1 - m) * half, half, axis=0)
    return own, other


def join_pair(own, other, m, axis):
    return jnp.where(
        m == 0,
        jnp.concatenate([own, other], axis=axis),
        jnp.concatenate([other, own], axis=axis),
    )


def scatter_rows_mp(partial, m, send_dtype):
    own, other = row_halves(partial, m)
    return own + swap_mp(other.astype(send_dtype)).astype(own.dtype)


def gather_rows_mp(own, m):
    half = own.shape[0]
    other = swap_mp(own)
    rows = jnp.zeros((2 * half,) + own.shape[1:], own.dtype)
    rows = lax.dynamic_update_slice_in_dim(rows, own, m * half, axis=0)
    return lax.dynamic_update_slice_in_dim(rows, other, (1 - m) * half, axis=0)


def scatter_dp(x, ndp, swap=False):
    idx = lax.axis_index("dp")
    bits = ndp.bit_length() - 1
    chunk = x.shape[0] // ndp
    rest = x.shape[1:]
    cur = x.reshape((2,) * bits + (chunk,) + rest)
    remaining = list(range(bits - 1, -1, -1))
    order = list(range(bits))
    if swap and bits >= 3:
        order[1], order[2] = order[2], order[1]
    for bit in order:
        pos = remaining.index(bit)
        mine = (idx >> bit) & 1
        keep = lax.dynamic_index_in_dim(cur, mine, pos, keepdims=False)
        send = lax.dynamic_index_in_dim(cur, 1 - mine, pos, keepdims=False)
        got = lax.ppermute(send, "dp", [(i, i ^ (1 << bit)) for i in range(ndp)])
        cur = keep + got
        remaining.pop(pos)
    return cur.reshape((chunk,) + rest)


def reduce_tree(x, name, size):
    bits = size.bit_length() - 1
    for bit in range(bits):
        x = x + lax.ppermute(x, name, [(i, i ^ (1 << bit)) for i in range(size)])
    return x


def make_shards(ndp, nmp):
    def shards_body(
        tokens,
        doc_ids,
        ln1_gain,
        ln1_bias,
        w_qkv,
        b_qv,
        w_out,
        b_out,
        ln2_gain,
        ln2_bias,
        w_up,
        b_up,
        w_down,
        b_down,
        cotangent,
    ):
        m = lax.axis_index("mp")
        w_out_other = swap_mp(w_out)
        row_count = tokens.shape[0]
        local_width = w_qkv.shape[2]
        seq_count, seq_len = doc_ids.shape
        seq_shape = (seq_count, seq_len, local_width // HD, HD)
        token_rows = tokens.astype(jnp.float32)
        normal_one, inv_one = normalize(token_rows)
        gain_one = ln1_gain.astype(jnp.float32)
        normed_one = (normal_one * gain_one + ln1_bias.astype(jnp.float32)).astype(jnp.bfloat16)
        projected = jnp.einsum(
            "td,dce->tce", normed_one, w_qkv, preferred_element_type=jnp.float32
        )
        bias_qv = b_qv.astype(jnp.float32)
        queries = (projected[:, 0] + bias_qv[0]).astype(jnp.bfloat16).reshape(seq_shape)
        key_rows = projected[:, 1].astype(jnp.bfloat16).reshape(seq_shape)
        value_rows = (projected[:, 2] + bias_qv[1]).astype(jnp.bfloat16).reshape(seq_shape)
        attended = []
        log_totals = []
        for s in range(seq_count):
            out_s, lse_s = attend_forward(queries[s], key_rows[s], value_rows[s], doc_ids[s])
            attended.append(out_s)
            log_totals.append(lse_s)
        mixed = jnp.stack(attended).reshape(row_count, local_width).astype(jnp.bfloat16)
        w_out_all = join_pair(w_out, w_out_other, m, 0)
        half_rows = row_count // 2
        attn_parts = []
        for part in range(2):
            rows = mixed[part * half_rows : (part + 1) * half_rows]
            rows_other = swap_mp(rows)
            attn_parts.append(
                jnp.dot(join_pair(rows, rows_other, m, 1), w_out_all,
                        preferred_element_type=jnp.float32)
            )
        attn_all = jnp.concatenate(attn_parts, axis=0)
        after_attn = token_rows + attn_all + b_out.astype(jnp.float32)
        gain_two = ln2_gain.astype(jnp.float32)
        normal_two, inv_two = normalize(after_attn)
        normed_two = (normal_two * gain_two + ln2_bias.astype(jnp.float32)).astype(jnp.bfloat16)
        up_rows = jnp.dot(normed_two, w_up, preferred_element_type=jnp.float32) + b_up.astype(
            jnp.float32
        )
        activated, gelu_pull = jax.vjp(gelu_tanh, up_rows)
        act_rows = activated.astype(jnp.bfloat16)
        ffn_part = jnp.dot(act_rows, w_down, preferred_element_type=jnp.float32)

        cot_rows = cotangent.astype(jnp.float32)
        cot_own, _ = row_halves(cot_rows, m)
        grad_w_down_t = jnp.einsum(
            "td,tf->df", cotangent, act_rows, preferred_element_type=jnp.float32
        )
        grad_act = jnp.einsum("td,fd->tf", cotangent, w_down, preferred_element_type=jnp.float32)
        grad_up = gelu_pull(grad_act)[0].astype(jnp.bfloat16)
        grad_w_up = jnp.einsum("td,tf->df", normed_two, grad_up, preferred_element_type=jnp.float32)
        grad_b_up = jnp.sum(grad_up.astype(jnp.float32), axis=0)
        norm_two_part = jnp.einsum("tf,df->td", grad_up, w_up, preferred_element_type=jnp.float32)
        grad_two_own = scatter_rows_mp(norm_two_part, m, jnp.bfloat16)
        normal_two_own, _ = row_halves(normal_two, m)
        inv_two_own, _ = row_halves(inv_two, m)
        grad_after_own = cot_own + norm_back(grad_two_own, normal_two_own, inv_two_own, gain_two)
        grad_attn_own = grad_after_own.astype(jnp.bfloat16)
        grad_attn_here = gather_rows_mp(grad_attn_own, m)
        ffn_late, grad_attn_here = lax.optimization_barrier((ffn_part, grad_attn_here))
        ffn_own = scatter_rows_mp(ffn_late, m, jnp.bfloat16)
        after_own, _ = row_halves(after_attn, m)
        out_own = (after_own + (ffn_own + b_down.astype(jnp.float32))).astype(jnp.bfloat16)
        block_out = gather_rows_mp(out_own, m)
        grad_w_out_t = jnp.einsum(
            "td,te->de", grad_attn_here, mixed, preferred_element_type=jnp.float32
        )
        grad_mixed = jnp.einsum(
            "td,ed->te", grad_attn_here, w_out, preferred_element_type=jnp.float32
        ).astype(jnp.bfloat16)
        grad_mixed = grad_mixed.reshape(seq_shape)
        gq, gk, gv = [], [], []
        for s in range(seq_count):
            dq_s, dk_s, dv_s = attend_backward(
                queries[s], key_rows[s], value_rows[s], doc_ids[s], log_totals[s], grad_mixed[s]
            )
            gq.append(dq_s)
            gk.append(dk_s)
            gv.append(dv_s)
        grad_q = jnp.stack(gq).reshape(row_count, local_width).astype(jnp.bfloat16)
        grad_k = jnp.stack(gk).reshape(row_count, local_width).astype(jnp.bfloat16)
        grad_v = jnp.stack(gv).reshape(row_count, local_width).astype(jnp.bfloat16)
        grad_proj = jnp.stack([grad_q, grad_k, grad_v], axis=1)
        grad_w_qkv = jnp.einsum(
            "td,tce->dce", normed_one, grad_proj, preferred_element_type=jnp.float32
        )
        grad_b_qv = jnp.stack(
            [
                jnp.sum(grad_q.astype(jnp.float32), axis=0),
                jnp.sum(grad_v.astype(jnp.float32), axis=0),
            ]
        )
        norm_one_part = jnp.einsum(
            "tce,dce->td", grad_proj, w_qkv, preferred_element_type=jnp.float32
        )
        grad_one_own = scatter_rows_mp(norm_one_part, m, jnp.bfloat16)
        normal_one_own, _ = row_halves(normal_one, m)
        inv_one_own, _ = row_halves(inv_one, m)
        grad_input_own = grad_after_own + norm_back(
            grad_one_own, normal_one_own, inv_one_own, gain_one
        )
        grad_input = gather_rows_mp(grad_input_own, m)
        vector_terms = jnp.stack(
            [
                jnp.sum(grad_one_own * normal_one_own, axis=0),
                jnp.sum(grad_one_own, axis=0),
                jnp.sum(grad_two_own * normal_two_own, axis=0),
                jnp.sum(grad_two_own, axis=0),
                jnp.sum(grad_attn_own.astype(jnp.float32), axis=0),
                jnp.sum(cot_own, axis=0),
            ]
        )
        n_vec = vector_terms.size
        n_qv = grad_b_qv.size
        packed = jnp.concatenate([vector_terms.reshape(-1), grad_b_qv.reshape(-1), grad_b_up])
        qkv_cols = grad_w_qkv.shape[2] // 2
        sum_qkv = jnp.concatenate(
            [
                scatter_dp(grad_w_qkv[:, :, :qkv_cols], ndp),
                scatter_dp(grad_w_qkv[:, :, qkv_cols:], ndp, swap=True),
            ],
            axis=2,
        )
        packed = reduce_tree(packed, "dp", ndp)
        vector_sum = reduce_tree(packed[:n_vec], "mp", nmp).reshape(vector_terms.shape)
        qv_sum = packed[n_vec : n_vec + n_qv].reshape(grad_b_qv.shape)
        up_sum = packed[n_vec + n_qv :]
        sum_out = scatter_dp(grad_w_out_t, ndp).T
        sum_up = scatter_dp(grad_w_up, ndp)
        sum_down = scatter_dp(grad_w_down_t, ndp, swap=True).T
        return (
            block_out,
            grad_input,
            vector_sum[0],
            vector_sum[1],
            sum_qkv,
            qv_sum,
            sum_out,
            vector_sum[4],
            vector_sum[2],
            vector_sum[3],
            sum_up,
            up_sum,
            sum_down,
            vector_sum[5],
        )

    return shards_body


def solution(mesh):
    return jax.shard_map(
        make_shards(mesh.shape["dp"], mesh.shape["mp"]),
        mesh=mesh,
        in_specs=(
            P("dp", None),
            P("dp", None),
            P(),
            P(),
            P(None, None, "mp"),
            P(None, "mp"),
            P("mp", None),
            P(),
            P(),
            P(),
            P(None, "mp"),
            P("mp"),
            P("mp", None),
            P(),
            P("dp", None),
        ),
        out_specs=(
            P("dp", None),
            P("dp", None),
            P(),
            P(),
            P("dp", None, "mp"),
            P(None, "mp"),
            P("mp", "dp"),
            P(),
            P(),
            P(),
            P("dp", "mp"),
            P("mp"),
            P("mp", "dp"),
            P(),
        ),
        check_vma=False,
    )
```

```python
import math

import jax
import jax.numpy as jnp
from jax import lax
from jax.sharding import PartitionSpec as P


HD = 64


epsilon = 1e-05


def normalize(values):
    average = jnp.mean(values, axis=-1, keepdims=True)
    centered = values - average
    variance = jnp.mean(centered * centered, axis=-1, keepdims=True)
    inverse = lax.rsqrt(variance + epsilon)
    return (centered * inverse, inverse)


def norm_back(grad_out, normal_rows, inverse, gain):
    grad_unit = grad_out * gain
    return inverse * (
        grad_unit
        - jnp.mean(grad_unit, axis=-1, keepdims=True)
        - normal_rows * jnp.mean(grad_unit * normal_rows, axis=-1, keepdims=True)
    )


def gelu_tanh(values):
    return (
        0.5
        * values
        * (1.0 + jnp.tanh(0.7978845608028654 * (values + 0.044715 * values * values * values)))
    )


def key_end(offset, block_rows, seq_len):
    return min(seq_len, offset + block_rows)


def block_scores(query_block, key_rows, doc_rows, offset):
    block_rows = query_block.shape[0]
    kend = key_end(offset, block_rows, key_rows.shape[0])
    key_rows = key_rows[:kend]
    scores = jnp.einsum(
        "qhd,khd->hqk", query_block, key_rows, preferred_element_type=jnp.float32
    ) * (1.0 / math.sqrt(HD))
    query_pos = offset + lax.iota(jnp.int32, block_rows)
    key_pos = lax.iota(jnp.int32, key_rows.shape[0])
    block_docs = doc_rows[offset : offset + block_rows]
    allowed = (block_docs[:, None] == doc_rows[None, :kend]) & (query_pos[:, None] >= key_pos[None, :])
    return jnp.where(allowed[None], scores, -1e30)


def attend_forward(queries, key_rows, value_rows, doc_rows):
    seq_len = queries.shape[0]
    block_rows = min(512, seq_len)
    outputs = []
    log_parts = []
    for offset in range(0, seq_len, block_rows):
      scores = block_scores(queries[offset : offset + block_rows], key_rows, doc_rows, offset)
      row_max = jnp.max(scores, axis=-1, keepdims=True)
      log_total = row_max + jnp.log(jnp.sum(jnp.exp(scores - row_max), axis=-1, keepdims=True))
      probabilities = jnp.exp(scores - log_total).astype(jnp.bfloat16)
      kend = key_end(offset, block_rows, seq_len)
      outputs.append(
          jnp.einsum(
              "hqk,khd->qhd", probabilities, value_rows[:kend], preferred_element_type=jnp.float32
          )
      )
      log_parts.append(log_total[..., 0])
    return (jnp.concatenate(outputs, axis=0), jnp.concatenate(log_parts, axis=1))


def attend_backward(queries, key_rows, value_rows, doc_rows, log_totals, grad_out):
    seq_len = queries.shape[0]
    block_rows = min(512, seq_len)
    scale_factor = 1.0 / math.sqrt(HD)
    grad_queries = []
    grad_keys = jnp.zeros(key_rows.shape, jnp.float32)
    grad_values = jnp.zeros(value_rows.shape, jnp.float32)
    for offset in range(0, seq_len, block_rows):
      query_block = queries[offset : offset + block_rows]
      grad_block = grad_out[offset : offset + block_rows]
      kend = key_end(offset, block_rows, seq_len)
      scores = block_scores(query_block, key_rows, doc_rows, offset)
      probabilities = jnp.exp(scores - log_totals[:, offset : offset + block_rows, None])
      grad_probs = jnp.einsum(
          "qhd,khd->hqk", grad_block, value_rows[:kend], preferred_element_type=jnp.float32
      )
      row_dots = jnp.sum(probabilities * grad_probs, axis=-1, keepdims=True)
      grad_scores = (probabilities * (grad_probs - row_dots)).astype(jnp.bfloat16)
      grad_queries.append(
          scale_factor
          * jnp.einsum(
              "hqk,khd->qhd", grad_scores, key_rows[:kend], preferred_element_type=jnp.float32
          )
      )
      grad_keys = grad_keys.at[:kend].add(scale_factor * jnp.einsum(
          "hqk,qhd->khd", grad_scores, query_block, preferred_element_type=jnp.float32
      ))
      grad_values = grad_values.at[:kend].add(jnp.einsum(
          "hqk,qhd->khd",
          probabilities.astype(jnp.bfloat16),
          grad_block,
          preferred_element_type=jnp.float32,
      ))
    return (jnp.concatenate(grad_queries, axis=0), grad_keys, grad_values)


def swap_mp(x):
    return lax.ppermute(x, "mp", [(0, 1), (1, 0)])


def row_halves(x, m):
    half = x.shape[0] // 2
    own = lax.dynamic_slice_in_dim(x, m * half, half, axis=0)
    other = lax.dynamic_slice_in_dim(x, (1 - m) * half, half, axis=0)
    return own, other


def join_pair(own, other, m, axis):
    return jnp.where(
        m == 0,
        jnp.concatenate([own, other], axis=axis),
        jnp.concatenate([other, own], axis=axis),
    )


def scatter_rows_mp(partial, m, send_dtype):
    own, other = row_halves(partial, m)
    return own + swap_mp(other.astype(send_dtype)).astype(own.dtype)


def gather_rows_mp(own, m):
    return join_pair(own, swap_mp(own), m, 0)


def gather_rows_into(own, m):
    half = own.shape[0]
    other = swap_mp(own)
    rows = jnp.zeros((2 * half,) + own.shape[1:], own.dtype)
    rows = lax.dynamic_update_slice_in_dim(rows, own, m * half, axis=0)
    return lax.dynamic_update_slice_in_dim(rows, other, (1 - m) * half, axis=0)


def scatter_dp(x, ndp, swap=False):
    idx = lax.axis_index("dp")
    bits = ndp.bit_length() - 1
    chunk = x.shape[0] // ndp
    rest = x.shape[1:]
    cur = x.reshape((2,) * bits + (chunk,) + rest)
    remaining = list(range(bits - 1, -1, -1))
    order = list(range(bits))
    if swap and bits >= 3:
        order[1], order[2] = order[2], order[1]
    for bit in order:
        pos = remaining.index(bit)
        mine = (idx >> bit) & 1
        keep = lax.dynamic_index_in_dim(cur, mine, pos, keepdims=False)
        send = lax.dynamic_index_in_dim(cur, 1 - mine, pos, keepdims=False)
        got = lax.ppermute(send, "dp", [(i, i ^ (1 << bit)) for i in range(ndp)])
        cur = keep + got
        remaining.pop(pos)
    return cur.reshape((chunk,) + rest)


def reduce_tree(x, name, size):
    bits = size.bit_length() - 1
    for bit in range(bits):
        x = x + lax.ppermute(x, name, [(i, i ^ (1 << bit)) for i in range(size)])
    return x


def make_shards(ndp, nmp):
    def shards_body(
        tokens,
        doc_ids,
        ln1_gain,
        ln1_bias,
        w_qkv,
        b_qv,
        w_out,
        b_out,
        ln2_gain,
        ln2_bias,
        w_up,
        b_up,
        w_down,
        b_down,
        cotangent,
    ):
        m = lax.axis_index("mp")
        w_out_other = swap_mp(w_out)
        row_count = tokens.shape[0]
        local_width = w_qkv.shape[2]
        seq_count, seq_len = doc_ids.shape
        seq_shape = (seq_count, seq_len, local_width // HD, HD)
        token_rows = tokens.astype(jnp.float32)
        normal_one, inv_one = normalize(token_rows)
        gain_one = ln1_gain.astype(jnp.float32)
        normed_one = (normal_one * gain_one + ln1_bias.astype(jnp.float32)).astype(jnp.bfloat16)
        projected = jnp.einsum(
            "td,dce->tce", normed_one, w_qkv, preferred_element_type=jnp.float32
        )
        bias_qv = b_qv.astype(jnp.float32)
        queries = (projected[:, 0] + bias_qv[0]).astype(jnp.bfloat16).reshape(seq_shape)
        key_rows = projected[:, 1].astype(jnp.bfloat16).reshape(seq_shape)
        value_rows = (projected[:, 2] + bias_qv[1]).astype(jnp.bfloat16).reshape(seq_shape)
        attended = []
        log_totals = []
        for s in range(seq_count):
            out_s, lse_s = attend_forward(queries[s], key_rows[s], value_rows[s], doc_ids[s])
            attended.append(out_s)
            log_totals.append(lse_s)
        mixed = jnp.stack(attended).reshape(row_count, local_width).astype(jnp.bfloat16)
        w_out_all = join_pair(w_out, w_out_other, m, 0)
        half_rows = row_count // 2
        attn_parts = []
        for part in range(2):
            rows = mixed[part * half_rows : (part + 1) * half_rows]
            rows_other = swap_mp(rows)
            attn_parts.append(
                jnp.dot(join_pair(rows, rows_other, m, 1), w_out_all,
                        preferred_element_type=jnp.float32)
            )
        attn_all = jnp.concatenate(attn_parts, axis=0)
        after_attn = token_rows + attn_all + b_out.astype(jnp.float32)
        gain_two = ln2_gain.astype(jnp.float32)
        normal_two, inv_two = normalize(after_attn)
        normed_two = (normal_two * gain_two + ln2_bias.astype(jnp.float32)).astype(jnp.bfloat16)
        up_rows = jnp.dot(normed_two, w_up, preferred_element_type=jnp.float32) + b_up.astype(
            jnp.float32
        )
        activated, gelu_pull = jax.vjp(gelu_tanh, up_rows)
        act_rows = activated.astype(jnp.bfloat16)
        ffn_part = jnp.dot(act_rows, w_down, preferred_element_type=jnp.float32)

        cot_rows = cotangent.astype(jnp.float32)
        cot_own, _ = row_halves(cot_rows, m)
        grad_w_down_t = jnp.einsum(
            "td,tf->df", cotangent, act_rows, preferred_element_type=jnp.float32
        )
        grad_act = jnp.einsum("td,fd->tf", cotangent, w_down, preferred_element_type=jnp.float32)
        grad_up = gelu_pull(grad_act)[0].astype(jnp.bfloat16)
        grad_w_up = jnp.einsum("td,tf->df", normed_two, grad_up, preferred_element_type=jnp.float32)
        grad_b_up = jnp.sum(grad_up.astype(jnp.float32), axis=0)
        norm_two_part = jnp.einsum("tf,df->td", grad_up, w_up, preferred_element_type=jnp.float32)
        grad_two_own = scatter_rows_mp(norm_two_part, m, jnp.bfloat16)
        normal_two_own, _ = row_halves(normal_two, m)
        inv_two_own, _ = row_halves(inv_two, m)
        grad_after_own = cot_own + norm_back(grad_two_own, normal_two_own, inv_two_own, gain_two)
        grad_attn_own = grad_after_own.astype(jnp.bfloat16)
        grad_attn_here = gather_rows_mp(grad_attn_own, m)
        ffn_late, grad_attn_here = lax.optimization_barrier((ffn_part, grad_attn_here))
        ffn_own = scatter_rows_mp(ffn_late, m, jnp.bfloat16)
        after_own, _ = row_halves(after_attn, m)
        out_own = (after_own + (ffn_own + b_down.astype(jnp.float32))).astype(jnp.bfloat16)
        block_out = gather_rows_mp(out_own, m)
        grad_w_out_t = jnp.einsum(
            "td,te->de", grad_attn_here, mixed, preferred_element_type=jnp.float32
        )
        grad_mixed = jnp.einsum(
            "td,ed->te", grad_attn_here, w_out, preferred_element_type=jnp.float32
        ).astype(jnp.bfloat16)
        grad_mixed = grad_mixed.reshape(seq_shape)
        gq, gk, gv = [], [], []
        for s in range(seq_count):
            dq_s, dk_s, dv_s = attend_backward(
                queries[s], key_rows[s], value_rows[s], doc_ids[s], log_totals[s], grad_mixed[s]
            )
            gq.append(dq_s)
            gk.append(dk_s)
            gv.append(dv_s)
        grad_q = jnp.stack(gq).reshape(row_count, local_width).astype(jnp.bfloat16)
        grad_k = jnp.stack(gk).reshape(row_count, local_width).astype(jnp.bfloat16)
        grad_v = jnp.stack(gv).reshape(row_count, local_width).astype(jnp.bfloat16)
        grad_proj = jnp.stack([grad_q, grad_k, grad_v], axis=1)
        grad_w_qkv = jnp.einsum(
            "td,tce->dce", normed_one, grad_proj, preferred_element_type=jnp.float32
        )
        grad_b_qv = jnp.stack(
            [
                jnp.sum(grad_q.astype(jnp.float32), axis=0),
                jnp.sum(grad_v.astype(jnp.float32), axis=0),
            ]
        )
        norm_one_part = jnp.einsum(
            "tce,dce->td", grad_proj, w_qkv, preferred_element_type=jnp.float32
        )
        grad_one_own = scatter_rows_mp(norm_one_part, m, jnp.bfloat16)
        normal_one_own, _ = row_halves(normal_one, m)
        inv_one_own, _ = row_halves(inv_one, m)
        grad_input_own = grad_after_own + norm_back(
            grad_one_own, normal_one_own, inv_one_own, gain_one
        )
        grad_input = gather_rows_into(grad_input_own, m)
        vector_terms = jnp.stack(
            [
                jnp.sum(grad_one_own * normal_one_own, axis=0),
                jnp.sum(grad_one_own, axis=0),
                jnp.sum(grad_two_own * normal_two_own, axis=0),
                jnp.sum(grad_two_own, axis=0),
                jnp.sum(grad_attn_own.astype(jnp.float32), axis=0),
                jnp.sum(cot_own, axis=0),
            ]
        )
        n_vec = vector_terms.size
        n_qv = grad_b_qv.size
        packed = jnp.concatenate([vector_terms.reshape(-1), grad_b_qv.reshape(-1), grad_b_up])
        qkv_cols = grad_w_qkv.shape[2] // 2
        sum_qkv = jnp.concatenate(
            [
                scatter_dp(grad_w_qkv[:, :, :qkv_cols], ndp),
                scatter_dp(grad_w_qkv[:, :, qkv_cols:], ndp, swap=True),
            ],
            axis=2,
        )
        packed, sum_qkv = lax.optimization_barrier((packed, sum_qkv))
        packed = reduce_tree(packed, "dp", ndp)
        vector_sum = reduce_tree(packed[:n_vec], "mp", nmp).reshape(vector_terms.shape)
        qv_sum = packed[n_vec : n_vec + n_qv].reshape(grad_b_qv.shape)
        up_sum = packed[n_vec + n_qv :]
        sum_out = scatter_dp(grad_w_out_t, ndp).T
        sum_up = scatter_dp(grad_w_up, ndp)
        sum_down = scatter_dp(grad_w_down_t, ndp, swap=True).T
        return (
            block_out,
            grad_input,
            vector_sum[0],
            vector_sum[1],
            sum_qkv,
            qv_sum,
            sum_out,
            vector_sum[4],
            vector_sum[2],
            vector_sum[3],
            sum_up,
            up_sum,
            sum_down,
            vector_sum[5],
        )

    return shards_body


def solution(mesh):
    return jax.shard_map(
        make_shards(mesh.shape["dp"], mesh.shape["mp"]),
        mesh=mesh,
        in_specs=(
            P("dp", None),
            P("dp", None),
            P(),
            P(),
            P(None, None, "mp"),
            P(None, "mp"),
            P("mp", None),
            P(),
            P(),
            P(),
            P(None, "mp"),
            P("mp"),
            P("mp", None),
            P(),
            P("dp", None),
        ),
        out_specs=(
            P("dp", None),
            P("dp", None),
            P(),
            P(),
            P("dp", None, "mp"),
            P(None, "mp"),
            P("mp", "dp"),
            P(),
            P(),
            P(),
            P("dp", "mp"),
            P("mp"),
            P("mp", "dp"),
            P(),
        ),
        check_vma=False,
    )
```

```python
import math

import jax
import jax.numpy as jnp
from jax import lax
from jax.sharding import PartitionSpec as P


HD = 64


epsilon = 1e-05


def normalize(values):
    average = jnp.mean(values, axis=-1, keepdims=True)
    centered = values - average
    variance = jnp.mean(centered * centered, axis=-1, keepdims=True)
    inverse = lax.rsqrt(variance + epsilon)
    return (centered * inverse, inverse)


def norm_back(grad_out, normal_rows, inverse, gain):
    grad_unit = grad_out * gain
    return inverse * (
        grad_unit
        - jnp.mean(grad_unit, axis=-1, keepdims=True)
        - normal_rows * jnp.mean(grad_unit * normal_rows, axis=-1, keepdims=True)
    )


def gelu_tanh(values):
    return (
        0.5
        * values
        * (1.0 + jnp.tanh(0.7978845608028654 * (values + 0.044715 * values * values * values)))
    )


def key_end(offset, block_rows, seq_len):
    return min(seq_len, offset + block_rows)


def block_scores(query_block, key_rows, doc_rows, offset):
    block_rows = query_block.shape[0]
    kend = key_end(offset, block_rows, key_rows.shape[0])
    key_rows = key_rows[:kend]
    scores = jnp.einsum(
        "qhd,khd->hqk", query_block, key_rows, preferred_element_type=jnp.float32
    ) * (1.0 / math.sqrt(HD))
    query_pos = offset + lax.iota(jnp.int32, block_rows)
    key_pos = lax.iota(jnp.int32, key_rows.shape[0])
    block_docs = doc_rows[offset : offset + block_rows]
    allowed = (block_docs[:, None] == doc_rows[None, :kend]) & (query_pos[:, None] >= key_pos[None, :])
    return jnp.where(allowed[None], scores, -1e30)


def attend_forward(queries, key_rows, value_rows, doc_rows):
    seq_len = queries.shape[0]
    block_rows = min(512, seq_len)
    outputs = []
    log_parts = []
    for offset in range(0, seq_len, block_rows):
      scores = block_scores(queries[offset : offset + block_rows], key_rows, doc_rows, offset)
      row_max = jnp.max(scores, axis=-1, keepdims=True)
      log_total = row_max + jnp.log(jnp.sum(jnp.exp(scores - row_max), axis=-1, keepdims=True))
      probabilities = jnp.exp(scores - log_total).astype(jnp.bfloat16)
      kend = key_end(offset, block_rows, seq_len)
      outputs.append(
          jnp.einsum(
              "hqk,khd->qhd", probabilities, value_rows[:kend], preferred_element_type=jnp.float32
          )
      )
      log_parts.append(log_total[..., 0])
    return (jnp.concatenate(outputs, axis=0), jnp.concatenate(log_parts, axis=1))


def attend_backward(queries, key_rows, value_rows, doc_rows, log_totals, grad_out):
    seq_len = queries.shape[0]
    block_rows = min(512, seq_len)
    scale_factor = 1.0 / math.sqrt(HD)
    grad_queries = []
    grad_keys = jnp.zeros(key_rows.shape, jnp.float32)
    grad_values = jnp.zeros(value_rows.shape, jnp.float32)
    for offset in range(0, seq_len, block_rows):
      query_block = queries[offset : offset + block_rows]
      grad_block = grad_out[offset : offset + block_rows]
      kend = key_end(offset, block_rows, seq_len)
      scores = block_scores(query_block, key_rows, doc_rows, offset)
      probabilities = jnp.exp(scores - log_totals[:, offset : offset + block_rows, None])
      grad_probs = jnp.einsum(
          "qhd,khd->hqk", grad_block, value_rows[:kend], preferred_element_type=jnp.float32
      )
      row_dots = jnp.sum(probabilities * grad_probs, axis=-1, keepdims=True)
      grad_scores = (probabilities * (grad_probs - row_dots)).astype(jnp.bfloat16)
      grad_queries.append(
          scale_factor
          * jnp.einsum(
              "hqk,khd->qhd", grad_scores, key_rows[:kend], preferred_element_type=jnp.float32
          )
      )
      grad_keys = grad_keys.at[:kend].add(scale_factor * jnp.einsum(
          "hqk,qhd->khd", grad_scores, query_block, preferred_element_type=jnp.float32
      ))
      grad_values = grad_values.at[:kend].add(jnp.einsum(
          "hqk,qhd->khd",
          probabilities.astype(jnp.bfloat16),
          grad_block,
          preferred_element_type=jnp.float32,
      ))
    return (jnp.concatenate(grad_queries, axis=0), grad_keys, grad_values)


def swap_mp(x):
    return lax.ppermute(x, "mp", [(0, 1), (1, 0)])


def row_halves(x, m):
    half = x.shape[0] // 2
    own = lax.dynamic_slice_in_dim(x, m * half, half, axis=0)
    other = lax.dynamic_slice_in_dim(x, (1 - m) * half, half, axis=0)
    return own, other


def join_pair(own, other, m, axis):
    return jnp.where(
        m == 0,
        jnp.concatenate([own, other], axis=axis),
        jnp.concatenate([other, own], axis=axis),
    )


def scatter_rows_mp(partial, m, send_dtype):
    own, other = row_halves(partial, m)
    return own + swap_mp(other.astype(send_dtype)).astype(own.dtype)


def gather_rows_mp(own, m):
    return join_pair(own, swap_mp(own), m, 0)


def gather_rows_into(own, m):
    half = own.shape[0]
    other = swap_mp(own)
    rows = jnp.zeros((2 * half,) + own.shape[1:], own.dtype)
    rows = lax.dynamic_update_slice_in_dim(rows, own, m * half, axis=0)
    return lax.dynamic_update_slice_in_dim(rows, other, (1 - m) * half, axis=0)


def scatter_dp(x, ndp, swap=False):
    idx = lax.axis_index("dp")
    bits = ndp.bit_length() - 1
    chunk = x.shape[0] // ndp
    rest = x.shape[1:]
    cur = x.reshape((2,) * bits + (chunk,) + rest)
    remaining = list(range(bits - 1, -1, -1))
    order = list(range(bits))
    if swap and bits >= 3:
        order[1], order[2] = order[2], order[1]
    for bit in order:
        pos = remaining.index(bit)
        mine = (idx >> bit) & 1
        keep = lax.dynamic_index_in_dim(cur, mine, pos, keepdims=False)
        send = lax.dynamic_index_in_dim(cur, 1 - mine, pos, keepdims=False)
        got = lax.ppermute(send, "dp", [(i, i ^ (1 << bit)) for i in range(ndp)])
        cur = keep + got
        remaining.pop(pos)
    return cur.reshape((chunk,) + rest)


def reduce_tree(x, name, size):
    bits = size.bit_length() - 1
    for bit in range(bits):
        x = x + lax.ppermute(x, name, [(i, i ^ (1 << bit)) for i in range(size)])
    return x


def reduce_dp_once(x, ndp):
    if ndp > 16:
        return reduce_tree(x, "dp", ndp)
    idx = lax.axis_index("dp")
    parts = [x]
    for k in range(1, ndp):
        parts.append(lax.ppermute(x, "dp", [(i, i ^ k) for i in range(ndp)]))
    stacked = jnp.stack(parts)
    canon = jnp.take(stacked, idx ^ jnp.arange(ndp, dtype=idx.dtype), axis=0)
    return jnp.sum(canon, axis=0)


def make_shards(ndp, nmp):
    def shards_body(
        tokens,
        doc_ids,
        ln1_gain,
        ln1_bias,
        w_qkv,
        b_qv,
        w_out,
        b_out,
        ln2_gain,
        ln2_bias,
        w_up,
        b_up,
        w_down,
        b_down,
        cotangent,
    ):
        m = lax.axis_index("mp")
        w_out_other = swap_mp(w_out)
        row_count = tokens.shape[0]
        local_width = w_qkv.shape[2]
        seq_count, seq_len = doc_ids.shape
        seq_shape = (seq_count, seq_len, local_width // HD, HD)
        token_rows = tokens.astype(jnp.float32)
        normal_one, inv_one = normalize(token_rows)
        gain_one = ln1_gain.astype(jnp.float32)
        normed_one = (normal_one * gain_one + ln1_bias.astype(jnp.float32)).astype(jnp.bfloat16)
        projected = jnp.einsum(
            "td,dce->tce", normed_one, w_qkv, preferred_element_type=jnp.float32
        )
        bias_qv = b_qv.astype(jnp.float32)
        queries = (projected[:, 0] + bias_qv[0]).astype(jnp.bfloat16).reshape(seq_shape)
        key_rows = projected[:, 1].astype(jnp.bfloat16).reshape(seq_shape)
        value_rows = (projected[:, 2] + bias_qv[1]).astype(jnp.bfloat16).reshape(seq_shape)
        attended = []
        log_totals = []
        for s in range(seq_count):
            out_s, lse_s = attend_forward(queries[s], key_rows[s], value_rows[s], doc_ids[s])
            attended.append(out_s)
            log_totals.append(lse_s)
        mixed = jnp.stack(attended).reshape(row_count, local_width).astype(jnp.bfloat16)
        w_out_all = join_pair(w_out, w_out_other, m, 0)
        half_rows = row_count // 2
        attn_parts = []
        for part in range(2):
            rows = mixed[part * half_rows : (part + 1) * half_rows]
            rows_other = swap_mp(rows)
            attn_parts.append(
                jnp.dot(join_pair(rows, rows_other, m, 1), w_out_all,
                        preferred_element_type=jnp.float32)
            )
        attn_all = jnp.concatenate(attn_parts, axis=0)
        after_attn = token_rows + attn_all + b_out.astype(jnp.float32)
        gain_two = ln2_gain.astype(jnp.float32)
        normal_two, inv_two = normalize(after_attn)
        normed_two = (normal_two * gain_two + ln2_bias.astype(jnp.float32)).astype(jnp.bfloat16)
        up_rows = jnp.dot(normed_two, w_up, preferred_element_type=jnp.float32) + b_up.astype(
            jnp.float32
        )
        activated, gelu_pull = jax.vjp(gelu_tanh, up_rows)
        act_rows = activated.astype(jnp.bfloat16)
        ffn_part = jnp.dot(act_rows, w_down, preferred_element_type=jnp.float32)

        cot_rows = cotangent.astype(jnp.float32)
        cot_own, _ = row_halves(cot_rows, m)
        grad_w_down_t = jnp.einsum(
            "td,tf->df", cotangent, act_rows, preferred_element_type=jnp.float32
        )
        grad_act = jnp.einsum("td,fd->tf", cotangent, w_down, preferred_element_type=jnp.float32)
        grad_up = gelu_pull(grad_act)[0].astype(jnp.bfloat16)
        grad_w_up = jnp.einsum("td,tf->df", normed_two, grad_up, preferred_element_type=jnp.float32)
        grad_b_up = jnp.sum(grad_up.astype(jnp.float32), axis=0)
        norm_two_part = jnp.einsum("tf,df->td", grad_up, w_up, preferred_element_type=jnp.float32)
        grad_two_own = scatter_rows_mp(norm_two_part, m, jnp.bfloat16)
        normal_two_own, _ = row_halves(normal_two, m)
        inv_two_own, _ = row_halves(inv_two, m)
        grad_after_own = cot_own + norm_back(grad_two_own, normal_two_own, inv_two_own, gain_two)
        grad_attn_own = grad_after_own.astype(jnp.bfloat16)
        grad_attn_here = gather_rows_mp(grad_attn_own, m)
        ffn_late, grad_attn_here = lax.optimization_barrier((ffn_part, grad_attn_here))
        ffn_own = scatter_rows_mp(ffn_late, m, jnp.bfloat16)
        after_own, _ = row_halves(after_attn, m)
        out_own = (after_own + (ffn_own + b_down.astype(jnp.float32))).astype(jnp.bfloat16)
        block_out = gather_rows_mp(out_own, m)
        grad_w_out_t = jnp.einsum(
            "td,te->de", grad_attn_here, mixed, preferred_element_type=jnp.float32
        )
        grad_mixed = jnp.einsum(
            "td,ed->te", grad_attn_here, w_out, preferred_element_type=jnp.float32
        ).astype(jnp.bfloat16)
        grad_mixed = grad_mixed.reshape(seq_shape)
        gq, gk, gv = [], [], []
        for s in range(seq_count):
            dq_s, dk_s, dv_s = attend_backward(
                queries[s], key_rows[s], value_rows[s], doc_ids[s], log_totals[s], grad_mixed[s]
            )
            gq.append(dq_s)
            gk.append(dk_s)
            gv.append(dv_s)
        grad_q = jnp.stack(gq).reshape(row_count, local_width).astype(jnp.bfloat16)
        grad_k = jnp.stack(gk).reshape(row_count, local_width).astype(jnp.bfloat16)
        grad_v = jnp.stack(gv).reshape(row_count, local_width).astype(jnp.bfloat16)
        grad_proj = jnp.stack([grad_q, grad_k, grad_v], axis=1)
        grad_w_qkv = jnp.einsum(
            "td,tce->dce", normed_one, grad_proj, preferred_element_type=jnp.float32
        )
        grad_b_qv = jnp.stack(
            [
                jnp.sum(grad_q.astype(jnp.float32), axis=0),
                jnp.sum(grad_v.astype(jnp.float32), axis=0),
            ]
        )
        norm_one_part = jnp.einsum(
            "tce,dce->td", grad_proj, w_qkv, preferred_element_type=jnp.float32
        )
        grad_one_own = scatter_rows_mp(norm_one_part, m, jnp.bfloat16)
        normal_one_own, _ = row_halves(normal_one, m)
        inv_one_own, _ = row_halves(inv_one, m)
        grad_input_own = grad_after_own + norm_back(
            grad_one_own, normal_one_own, inv_one_own, gain_one
        )
        grad_input = gather_rows_into(grad_input_own, m)
        early_mp = jnp.stack(
            [
                jnp.sum(grad_two_own * normal_two_own, axis=0),
                jnp.sum(grad_two_own, axis=0),
                jnp.sum(grad_attn_own.astype(jnp.float32), axis=0),
                jnp.sum(cot_own, axis=0),
            ]
        )
        n_early = early_mp.size
        early = reduce_dp_once(jnp.concatenate([early_mp.reshape(-1), grad_b_up]), ndp)
        early_sum = reduce_tree(early[:n_early], "mp", nmp).reshape(early_mp.shape)
        up_sum = early[n_early:]
        late_mp = jnp.stack(
            [
                jnp.sum(grad_one_own * normal_one_own, axis=0),
                jnp.sum(grad_one_own, axis=0),
            ]
        )
        n_late = late_mp.size
        late = reduce_dp_once(jnp.concatenate([late_mp.reshape(-1), grad_b_qv.reshape(-1)]), ndp)
        late_sum = reduce_tree(late[:n_late], "mp", nmp).reshape(late_mp.shape)
        qv_sum = late[n_late:].reshape(grad_b_qv.shape)
        qkv_cols = grad_w_qkv.shape[2] // 2
        sum_qkv = jnp.concatenate(
            [
                scatter_dp(grad_w_qkv[:, :, :qkv_cols], ndp),
                scatter_dp(grad_w_qkv[:, :, qkv_cols:], ndp, swap=True),
            ],
            axis=2,
        )
        sum_out = scatter_dp(grad_w_out_t, ndp).T
        sum_up = scatter_dp(grad_w_up, ndp)
        sum_down = scatter_dp(grad_w_down_t, ndp, swap=True).T
        return (
            block_out,
            grad_input,
            late_sum[0],
            late_sum[1],
            sum_qkv,
            qv_sum,
            sum_out,
            early_sum[2],
            early_sum[0],
            early_sum[1],
            sum_up,
            up_sum,
            sum_down,
            early_sum[3],
        )

    return shards_body


def solution(mesh):
    return jax.shard_map(
        make_shards(mesh.shape["dp"], mesh.shape["mp"]),
        mesh=mesh,
        in_specs=(
            P("dp", None),
            P("dp", None),
            P(),
            P(),
            P(None, None, "mp"),
            P(None, "mp"),
            P("mp", None),
            P(),
            P(),
            P(),
            P(None, "mp"),
            P("mp"),
            P("mp", None),
            P(),
            P("dp", None),
        ),
        out_specs=(
            P("dp", None),
            P("dp", None),
            P(),
            P(),
            P("dp", None, "mp"),
            P(None, "mp"),
            P("mp", "dp"),
            P(),
            P(),
            P(),
            P("dp", "mp"),
            P("mp"),
            P("mp", "dp"),
            P(),
        ),
        check_vma=False,
    )
```

```python
import math

import jax
import jax.numpy as jnp
from jax import lax
from jax.sharding import PartitionSpec as P


HD = 64


epsilon = 1e-05


def normalize(values):
    average = jnp.mean(values, axis=-1, keepdims=True)
    centered = values - average
    variance = jnp.mean(centered * centered, axis=-1, keepdims=True)
    inverse = lax.rsqrt(variance + epsilon)
    return (centered * inverse, inverse)


def norm_back(grad_out, normal_rows, inverse, gain):
    grad_unit = grad_out * gain
    return inverse * (
        grad_unit
        - jnp.mean(grad_unit, axis=-1, keepdims=True)
        - normal_rows * jnp.mean(grad_unit * normal_rows, axis=-1, keepdims=True)
    )


def gelu_tanh(values):
    return (
        0.5
        * values
        * (1.0 + jnp.tanh(0.7978845608028654 * (values + 0.044715 * values * values * values)))
    )


def key_end(offset, block_rows, seq_len):
    return min(seq_len, offset + block_rows)


def block_scores(query_block, key_rows, doc_rows, offset):
    block_rows = query_block.shape[0]
    kend = key_end(offset, block_rows, key_rows.shape[0])
    key_rows = key_rows[:kend]
    scores = jnp.einsum(
        "qhd,khd->hqk", query_block, key_rows, preferred_element_type=jnp.float32
    ) * (1.0 / math.sqrt(HD))
    query_pos = offset + lax.iota(jnp.int32, block_rows)
    key_pos = lax.iota(jnp.int32, key_rows.shape[0])
    block_docs = doc_rows[offset : offset + block_rows]
    allowed = (block_docs[:, None] == doc_rows[None, :kend]) & (query_pos[:, None] >= key_pos[None, :])
    return jnp.where(allowed[None], scores, -1e30)


def attend_forward(queries, key_rows, value_rows, doc_rows):
    seq_len = queries.shape[0]
    block_rows = min(512, seq_len)
    outputs = []
    log_parts = []
    for offset in range(0, seq_len, block_rows):
      scores = block_scores(queries[offset : offset + block_rows], key_rows, doc_rows, offset)
      row_max = jnp.max(scores, axis=-1, keepdims=True)
      log_total = row_max + jnp.log(jnp.sum(jnp.exp(scores - row_max), axis=-1, keepdims=True))
      probabilities = jnp.exp(scores - log_total).astype(jnp.bfloat16)
      kend = key_end(offset, block_rows, seq_len)
      outputs.append(
          jnp.einsum(
              "hqk,khd->qhd", probabilities, value_rows[:kend], preferred_element_type=jnp.float32
          )
      )
      log_parts.append(log_total[..., 0])
    return (jnp.concatenate(outputs, axis=0), jnp.concatenate(log_parts, axis=1))


def attend_backward(queries, key_rows, value_rows, doc_rows, log_totals, grad_out):
    seq_len = queries.shape[0]
    block_rows = min(512, seq_len)
    scale_factor = 1.0 / math.sqrt(HD)
    grad_queries = []
    grad_keys = jnp.zeros(key_rows.shape, jnp.float32)
    grad_values = jnp.zeros(value_rows.shape, jnp.float32)
    for offset in range(0, seq_len, block_rows):
      query_block = queries[offset : offset + block_rows]
      grad_block = grad_out[offset : offset + block_rows]
      kend = key_end(offset, block_rows, seq_len)
      scores = block_scores(query_block, key_rows, doc_rows, offset)
      probabilities = jnp.exp(scores - log_totals[:, offset : offset + block_rows, None])
      grad_probs = jnp.einsum(
          "qhd,khd->hqk", grad_block, value_rows[:kend], preferred_element_type=jnp.float32
      )
      row_dots = jnp.sum(probabilities * grad_probs, axis=-1, keepdims=True)
      grad_scores = (probabilities * (grad_probs - row_dots)).astype(jnp.bfloat16)
      grad_queries.append(
          scale_factor
          * jnp.einsum(
              "hqk,khd->qhd", grad_scores, key_rows[:kend], preferred_element_type=jnp.float32
          )
      )
      grad_keys = grad_keys.at[:kend].add(scale_factor * jnp.einsum(
          "hqk,qhd->khd", grad_scores, query_block, preferred_element_type=jnp.float32
      ))
      grad_values = grad_values.at[:kend].add(jnp.einsum(
          "hqk,qhd->khd",
          probabilities.astype(jnp.bfloat16),
          grad_block,
          preferred_element_type=jnp.float32,
      ))
    return (jnp.concatenate(grad_queries, axis=0), grad_keys, grad_values)


def swap_mp(x):
    return lax.ppermute(x, "mp", [(0, 1), (1, 0)])


def row_halves(x, m):
    half = x.shape[0] // 2
    own = lax.dynamic_slice_in_dim(x, m * half, half, axis=0)
    other = lax.dynamic_slice_in_dim(x, (1 - m) * half, half, axis=0)
    return own, other


def join_pair(own, other, m, axis):
    return jnp.where(
        m == 0,
        jnp.concatenate([own, other], axis=axis),
        jnp.concatenate([other, own], axis=axis),
    )


def scatter_rows_mp(partial, m, send_dtype):
    own, other = row_halves(partial, m)
    return own + swap_mp(other.astype(send_dtype)).astype(own.dtype)


def gather_rows_mp(own, m):
    return join_pair(own, swap_mp(own), m, 0)


def gather_rows_into(own, m):
    half = own.shape[0]
    other = swap_mp(own)
    rows = jnp.zeros((2 * half,) + own.shape[1:], own.dtype)
    rows = lax.dynamic_update_slice_in_dim(rows, own, m * half, axis=0)
    return lax.dynamic_update_slice_in_dim(rows, other, (1 - m) * half, axis=0)


def scatter_dp(x, ndp, swap=False):
    idx = lax.axis_index("dp")
    bits = ndp.bit_length() - 1
    chunk = x.shape[0] // ndp
    rest = x.shape[1:]
    cur = x.reshape((2,) * bits + (chunk,) + rest)
    remaining = list(range(bits - 1, -1, -1))
    order = list(range(bits))
    if swap and bits >= 3:
        order[1], order[2] = order[2], order[1]
    for bit in order:
        pos = remaining.index(bit)
        mine = (idx >> bit) & 1
        keep = lax.dynamic_index_in_dim(cur, mine, pos, keepdims=False)
        send = lax.dynamic_index_in_dim(cur, 1 - mine, pos, keepdims=False)
        got = lax.ppermute(send, "dp", [(i, i ^ (1 << bit)) for i in range(ndp)])
        cur = keep + got
        remaining.pop(pos)
    return cur.reshape((chunk,) + rest)


def reduce_tree(x, name, size):
    bits = size.bit_length() - 1
    for bit in range(bits):
        x = x + lax.ppermute(x, name, [(i, i ^ (1 << bit)) for i in range(size)])
    return x


def make_shards(ndp, nmp):
    def shards_body(
        tokens,
        doc_ids,
        ln1_gain,
        ln1_bias,
        w_qkv,
        b_qv,
        w_out,
        b_out,
        ln2_gain,
        ln2_bias,
        w_up,
        b_up,
        w_down,
        b_down,
        cotangent,
    ):
        m = lax.axis_index("mp")
        w_out_other = swap_mp(w_out)
        row_count = tokens.shape[0]
        local_width = w_qkv.shape[2]
        seq_count, seq_len = doc_ids.shape
        seq_shape = (seq_count, seq_len, local_width // HD, HD)
        token_rows = tokens.astype(jnp.float32)
        normal_one, inv_one = normalize(token_rows)
        gain_one = ln1_gain.astype(jnp.float32)
        normed_one = (normal_one * gain_one + ln1_bias.astype(jnp.float32)).astype(jnp.bfloat16)
        projected = jnp.einsum(
            "td,dce->tce", normed_one, w_qkv, preferred_element_type=jnp.float32
        )
        bias_qv = b_qv.astype(jnp.float32)
        queries = (projected[:, 0] + bias_qv[0]).astype(jnp.bfloat16).reshape(seq_shape)
        key_rows = projected[:, 1].astype(jnp.bfloat16).reshape(seq_shape)
        value_rows = (projected[:, 2] + bias_qv[1]).astype(jnp.bfloat16).reshape(seq_shape)
        attended = []
        log_totals = []
        for s in range(seq_count):
            out_s, lse_s = attend_forward(queries[s], key_rows[s], value_rows[s], doc_ids[s])
            attended.append(out_s)
            log_totals.append(lse_s)
        mixed = jnp.stack(attended).reshape(row_count, local_width).astype(jnp.bfloat16)
        w_out_all = join_pair(w_out, w_out_other, m, 0)
        half_rows = row_count // 2
        attn_parts = []
        for part in range(2):
            rows = mixed[part * half_rows : (part + 1) * half_rows]
            rows_other = swap_mp(rows)
            attn_parts.append(
                jnp.dot(join_pair(rows, rows_other, m, 1), w_out_all,
                        preferred_element_type=jnp.float32)
            )
        attn_all = jnp.concatenate(attn_parts, axis=0)
        after_attn = token_rows + attn_all + b_out.astype(jnp.float32)
        gain_two = ln2_gain.astype(jnp.float32)
        normal_two, inv_two = normalize(after_attn)
        normed_two = (normal_two * gain_two + ln2_bias.astype(jnp.float32)).astype(jnp.bfloat16)
        up_rows = jnp.dot(normed_two, w_up, preferred_element_type=jnp.float32) + b_up.astype(
            jnp.float32
        )
        activated, gelu_pull = jax.vjp(gelu_tanh, up_rows)
        act_rows = activated.astype(jnp.bfloat16)
        ffn_part = jnp.dot(act_rows, w_down, preferred_element_type=jnp.float32)

        cot_rows = cotangent.astype(jnp.float32)
        cot_own, _ = row_halves(cot_rows, m)
        grad_w_down_t = jnp.einsum(
            "td,tf->df", cotangent, act_rows, preferred_element_type=jnp.float32
        )
        grad_act = jnp.einsum("td,fd->tf", cotangent, w_down, preferred_element_type=jnp.float32)
        grad_up = gelu_pull(grad_act)[0].astype(jnp.bfloat16)
        grad_w_up = jnp.einsum("td,tf->df", normed_two, grad_up, preferred_element_type=jnp.float32)
        grad_b_up = jnp.sum(grad_up.astype(jnp.float32), axis=0)
        norm_two_part = jnp.einsum("tf,df->td", grad_up, w_up, preferred_element_type=jnp.float32)
        grad_two_own = scatter_rows_mp(norm_two_part, m, jnp.bfloat16)
        normal_two_own, _ = row_halves(normal_two, m)
        inv_two_own, _ = row_halves(inv_two, m)
        grad_after_own = cot_own + norm_back(grad_two_own, normal_two_own, inv_two_own, gain_two)
        grad_attn_own = grad_after_own.astype(jnp.bfloat16)
        grad_attn_here = gather_rows_mp(grad_attn_own, m)
        ffn_late, grad_attn_here = lax.optimization_barrier((ffn_part, grad_attn_here))
        ffn_own = scatter_rows_mp(ffn_late, m, jnp.bfloat16)
        after_own, _ = row_halves(after_attn, m)
        out_own = (after_own + (ffn_own + b_down.astype(jnp.float32))).astype(jnp.bfloat16)
        block_out = gather_rows_mp(out_own, m)
        grad_w_out_t = jnp.einsum(
            "td,te->de", grad_attn_here, mixed, preferred_element_type=jnp.float32
        )
        grad_mixed = jnp.einsum(
            "td,ed->te", grad_attn_here, w_out, preferred_element_type=jnp.float32
        ).astype(jnp.bfloat16)
        grad_mixed = grad_mixed.reshape(seq_shape)
        gq, gk, gv = [], [], []
        for s in range(seq_count):
            dq_s, dk_s, dv_s = attend_backward(
                queries[s], key_rows[s], value_rows[s], doc_ids[s], log_totals[s], grad_mixed[s]
            )
            gq.append(dq_s)
            gk.append(dk_s)
            gv.append(dv_s)
        grad_q = jnp.stack(gq).reshape(row_count, local_width).astype(jnp.bfloat16)
        grad_k = jnp.stack(gk).reshape(row_count, local_width).astype(jnp.bfloat16)
        grad_v = jnp.stack(gv).reshape(row_count, local_width).astype(jnp.bfloat16)
        grad_proj = jnp.stack([grad_q, grad_k, grad_v], axis=1)
        grad_w_qkv = jnp.einsum(
            "td,tce->dce", normed_one, grad_proj, preferred_element_type=jnp.float32
        )
        grad_b_qv = jnp.stack(
            [
                jnp.sum(grad_q.astype(jnp.float32), axis=0),
                jnp.sum(grad_v.astype(jnp.float32), axis=0),
            ]
        )
        norm_one_part = jnp.einsum(
            "tce,dce->td", grad_proj, w_qkv, preferred_element_type=jnp.float32
        )
        grad_one_own = scatter_rows_mp(norm_one_part, m, jnp.bfloat16)
        normal_one_own, _ = row_halves(normal_one, m)
        inv_one_own, _ = row_halves(inv_one, m)
        grad_input_own = grad_after_own + norm_back(
            grad_one_own, normal_one_own, inv_one_own, gain_one
        )
        grad_input = gather_rows_into(grad_input_own, m)
        vector_terms = jnp.stack(
            [
                jnp.sum(grad_one_own * normal_one_own, axis=0),
                jnp.sum(grad_one_own, axis=0),
                jnp.sum(grad_two_own * normal_two_own, axis=0),
                jnp.sum(grad_two_own, axis=0),
                jnp.sum(grad_attn_own.astype(jnp.float32), axis=0),
                jnp.sum(cot_own, axis=0),
            ]
        )
        n_vec = vector_terms.size
        n_qv = grad_b_qv.size
        packed = jnp.concatenate([vector_terms.reshape(-1), grad_b_qv.reshape(-1), grad_b_up])
        qkv_cols = grad_w_qkv.shape[2] // 2
        sum_qkv = jnp.concatenate(
            [
                scatter_dp(grad_w_qkv[:, :, :qkv_cols], ndp),
                scatter_dp(grad_w_qkv[:, :, qkv_cols:], ndp, swap=True),
            ],
            axis=2,
        )
        packed, sum_qkv = lax.optimization_barrier((packed, sum_qkv))
        packed = reduce_tree(packed, "dp", ndp)
        vector_sum = reduce_tree(packed[:n_vec], "mp", nmp).reshape(vector_terms.shape)
        qv_sum = packed[n_vec : n_vec + n_qv].reshape(grad_b_qv.shape)
        up_sum = packed[n_vec + n_qv :]
        up_cols = grad_w_up.shape[1]
        sum_up_out = scatter_dp(jnp.concatenate([grad_w_up, grad_w_out_t], axis=1), ndp)
        sum_up = sum_up_out[:, :up_cols]
        sum_out = sum_up_out[:, up_cols:].T
        sum_down = scatter_dp(grad_w_down_t, ndp, swap=True).T
        return (
            block_out,
            grad_input,
            vector_sum[0],
            vector_sum[1],
            sum_qkv,
            qv_sum,
            sum_out,
            vector_sum[4],
            vector_sum[2],
            vector_sum[3],
            sum_up,
            up_sum,
            sum_down,
            vector_sum[5],
        )

    return shards_body


def solution(mesh):
    return jax.shard_map(
        make_shards(mesh.shape["dp"], mesh.shape["mp"]),
        mesh=mesh,
        in_specs=(
            P("dp", None),
            P("dp", None),
            P(),
            P(),
            P(None, None, "mp"),
            P(None, "mp"),
            P("mp", None),
            P(),
            P(),
            P(),
            P(None, "mp"),
            P("mp"),
            P("mp", None),
            P(),
            P("dp", None),
        ),
        out_specs=(
            P("dp", None),
            P("dp", None),
            P(),
            P(),
            P("dp", None, "mp"),
            P(None, "mp"),
            P("mp", "dp"),
            P(),
            P(),
            P(),
            P("dp", "mp"),
            P("mp"),
            P("mp", "dp"),
            P(),
        ),
        check_vma=False,
    )
```

```python
import math

import jax
import jax.numpy as jnp
from jax import lax
from jax.sharding import PartitionSpec as P


HD = 64


epsilon = 1e-05


def normalize(values):
    average = jnp.mean(values, axis=-1, keepdims=True)
    centered = values - average
    variance = jnp.mean(centered * centered, axis=-1, keepdims=True)
    inverse = lax.rsqrt(variance + epsilon)
    return (centered * inverse, inverse)


def norm_back(grad_out, normal_rows, inverse, gain):
    grad_unit = grad_out * gain
    return inverse * (
        grad_unit
        - jnp.mean(grad_unit, axis=-1, keepdims=True)
        - normal_rows * jnp.mean(grad_unit * normal_rows, axis=-1, keepdims=True)
    )


def gelu_tanh(values):
    return (
        0.5
        * values
        * (1.0 + jnp.tanh(0.7978845608028654 * (values + 0.044715 * values * values * values)))
    )


MAX_DOC = 512


def key_window(offset, block_rows, seq_len):
    start = max(0, offset + 1 - MAX_DOC)
    start = (start // 128) * 128
    return start, min(seq_len, offset + block_rows)


def query_block_rows(seq_len):
    return min(256, seq_len)


def block_scores(query_block, key_rows, doc_rows, offset):
    block_rows = query_block.shape[0]
    kstart, kend = key_window(offset, block_rows, key_rows.shape[0])
    scores = jnp.einsum(
        "qhd,khd->hqk", query_block, key_rows[kstart:kend], preferred_element_type=jnp.float32
    ) * (1.0 / math.sqrt(HD))
    query_pos = offset + lax.iota(jnp.int32, block_rows)
    key_pos = kstart + lax.iota(jnp.int32, kend - kstart)
    block_docs = doc_rows[offset : offset + block_rows]
    allowed = (block_docs[:, None] == doc_rows[None, kstart:kend]) & (
        query_pos[:, None] >= key_pos[None, :]
    )
    return jnp.where(allowed[None], scores, -1e30)


def attend_forward(queries, key_rows, value_rows, doc_rows):
    seq_len = queries.shape[0]
    block_rows = query_block_rows(seq_len)
    outputs = []
    log_parts = []
    for offset in range(0, seq_len, block_rows):
      scores = block_scores(queries[offset : offset + block_rows], key_rows, doc_rows, offset)
      row_max = jnp.max(scores, axis=-1, keepdims=True)
      log_total = row_max + jnp.log(jnp.sum(jnp.exp(scores - row_max), axis=-1, keepdims=True))
      probabilities = jnp.exp(scores - log_total).astype(jnp.bfloat16)
      kstart, kend = key_window(offset, block_rows, seq_len)
      outputs.append(
          jnp.einsum(
              "hqk,khd->qhd",
              probabilities,
              value_rows[kstart:kend],
              preferred_element_type=jnp.float32,
          )
      )
      log_parts.append(log_total[..., 0])
    return (jnp.concatenate(outputs, axis=0), jnp.concatenate(log_parts, axis=1))


def attend_backward(queries, key_rows, value_rows, doc_rows, log_totals, grad_out):
    seq_len = queries.shape[0]
    block_rows = query_block_rows(seq_len)
    scale_factor = 1.0 / math.sqrt(HD)
    grad_queries = []
    grad_keys = jnp.zeros(key_rows.shape, jnp.float32)
    grad_values = jnp.zeros(value_rows.shape, jnp.float32)
    for offset in range(0, seq_len, block_rows):
      query_block = queries[offset : offset + block_rows]
      grad_block = grad_out[offset : offset + block_rows]
      kstart, kend = key_window(offset, block_rows, seq_len)
      scores = block_scores(query_block, key_rows, doc_rows, offset)
      probabilities = jnp.exp(scores - log_totals[:, offset : offset + block_rows, None])
      grad_probs = jnp.einsum(
          "qhd,khd->hqk", grad_block, value_rows[kstart:kend], preferred_element_type=jnp.float32
      )
      row_dots = jnp.sum(probabilities * grad_probs, axis=-1, keepdims=True)
      grad_scores = (probabilities * (grad_probs - row_dots)).astype(jnp.bfloat16)
      grad_queries.append(
          scale_factor
          * jnp.einsum(
              "hqk,khd->qhd",
              grad_scores,
              key_rows[kstart:kend],
              preferred_element_type=jnp.float32,
          )
      )
      grad_keys = grad_keys.at[kstart:kend].add(scale_factor * jnp.einsum(
          "hqk,qhd->khd", grad_scores, query_block, preferred_element_type=jnp.float32
      ))
      grad_values = grad_values.at[kstart:kend].add(jnp.einsum(
          "hqk,qhd->khd",
          probabilities.astype(jnp.bfloat16),
          grad_block,
          preferred_element_type=jnp.float32,
      ))
    return (jnp.concatenate(grad_queries, axis=0), grad_keys, grad_values)


def swap_mp(x):
    return lax.ppermute(x, "mp", [(0, 1), (1, 0)])


def row_halves(x, m):
    half = x.shape[0] // 2
    own = lax.dynamic_slice_in_dim(x, m * half, half, axis=0)
    other = lax.dynamic_slice_in_dim(x, (1 - m) * half, half, axis=0)
    return own, other


def join_pair(own, other, m, axis):
    return jnp.where(
        m == 0,
        jnp.concatenate([own, other], axis=axis),
        jnp.concatenate([other, own], axis=axis),
    )


def scatter_rows_mp(partial, m, send_dtype):
    own, other = row_halves(partial, m)
    return own + swap_mp(other.astype(send_dtype)).astype(own.dtype)


def gather_rows_mp(own, m):
    return join_pair(own, swap_mp(own), m, 0)


def gather_rows_into(own, m):
    half = own.shape[0]
    other = swap_mp(own)
    rows = jnp.zeros((2 * half,) + own.shape[1:], own.dtype)
    rows = lax.dynamic_update_slice_in_dim(rows, own, m * half, axis=0)
    return lax.dynamic_update_slice_in_dim(rows, other, (1 - m) * half, axis=0)


def scatter_dp(x, ndp, swap=False):
    idx = lax.axis_index("dp")
    bits = ndp.bit_length() - 1
    chunk = x.shape[0] // ndp
    rest = x.shape[1:]
    cur = x.reshape((2,) * bits + (chunk,) + rest)
    remaining = list(range(bits - 1, -1, -1))
    order = list(range(bits))
    if swap and bits >= 3:
        order[1], order[2] = order[2], order[1]
    for bit in order:
        pos = remaining.index(bit)
        mine = (idx >> bit) & 1
        keep = lax.dynamic_index_in_dim(cur, mine, pos, keepdims=False)
        send = lax.dynamic_index_in_dim(cur, 1 - mine, pos, keepdims=False)
        got = lax.ppermute(send, "dp", [(i, i ^ (1 << bit)) for i in range(ndp)])
        cur = keep + got
        remaining.pop(pos)
    return cur.reshape((chunk,) + rest)


def reduce_tree(x, name, size):
    bits = size.bit_length() - 1
    for bit in range(bits):
        x = x + lax.ppermute(x, name, [(i, i ^ (1 << bit)) for i in range(size)])
    return x


def make_shards(ndp, nmp):
    def shards_body(
        tokens,
        doc_ids,
        ln1_gain,
        ln1_bias,
        w_qkv,
        b_qv,
        w_out,
        b_out,
        ln2_gain,
        ln2_bias,
        w_up,
        b_up,
        w_down,
        b_down,
        cotangent,
    ):
        m = lax.axis_index("mp")
        w_out_other = swap_mp(w_out)
        row_count = tokens.shape[0]
        local_width = w_qkv.shape[2]
        seq_count, seq_len = doc_ids.shape
        seq_shape = (seq_count, seq_len, local_width // HD, HD)
        token_rows = tokens.astype(jnp.float32)
        normal_one, inv_one = normalize(token_rows)
        gain_one = ln1_gain.astype(jnp.float32)
        normed_one = (normal_one * gain_one + ln1_bias.astype(jnp.float32)).astype(jnp.bfloat16)
        projected = jnp.einsum(
            "td,dce->tce", normed_one, w_qkv, preferred_element_type=jnp.float32
        )
        bias_qv = b_qv.astype(jnp.float32)
        queries = (projected[:, 0] + bias_qv[0]).astype(jnp.bfloat16).reshape(seq_shape)
        key_rows = projected[:, 1].astype(jnp.bfloat16).reshape(seq_shape)
        value_rows = (projected[:, 2] + bias_qv[1]).astype(jnp.bfloat16).reshape(seq_shape)
        attended = []
        log_totals = []
        for s in range(seq_count):
            out_s, lse_s = attend_forward(queries[s], key_rows[s], value_rows[s], doc_ids[s])
            attended.append(out_s)
            log_totals.append(lse_s)
        mixed = jnp.stack(attended).reshape(row_count, local_width).astype(jnp.bfloat16)
        w_out_all = join_pair(w_out, w_out_other, m, 0)
        half_rows = row_count // 2
        attn_parts = []
        for part in range(2):
            rows = mixed[part * half_rows : (part + 1) * half_rows]
            rows_other = swap_mp(rows)
            attn_parts.append(
                jnp.dot(join_pair(rows, rows_other, m, 1), w_out_all,
                        preferred_element_type=jnp.float32)
            )
        attn_all = jnp.concatenate(attn_parts, axis=0)
        after_attn = token_rows + attn_all + b_out.astype(jnp.float32)
        gain_two = ln2_gain.astype(jnp.float32)
        normal_two, inv_two = normalize(after_attn)
        normed_two = (normal_two * gain_two + ln2_bias.astype(jnp.float32)).astype(jnp.bfloat16)
        up_rows = jnp.dot(normed_two, w_up, preferred_element_type=jnp.float32) + b_up.astype(
            jnp.float32
        )
        activated, gelu_pull = jax.vjp(gelu_tanh, up_rows)
        act_rows = activated.astype(jnp.bfloat16)
        ffn_part = jnp.dot(act_rows, w_down, preferred_element_type=jnp.float32)

        cot_rows = cotangent.astype(jnp.float32)
        cot_own, _ = row_halves(cot_rows, m)
        grad_w_down_t = jnp.einsum(
            "td,tf->df", cotangent, act_rows, preferred_element_type=jnp.float32
        )
        grad_act = jnp.einsum("td,fd->tf", cotangent, w_down, preferred_element_type=jnp.float32)
        grad_up = gelu_pull(grad_act)[0].astype(jnp.bfloat16)
        grad_w_up = jnp.einsum("td,tf->df", normed_two, grad_up, preferred_element_type=jnp.float32)
        grad_b_up = jnp.sum(grad_up.astype(jnp.float32), axis=0)
        norm_two_part = jnp.einsum("tf,df->td", grad_up, w_up, preferred_element_type=jnp.float32)
        grad_two_own = scatter_rows_mp(norm_two_part, m, jnp.bfloat16)
        normal_two_own, _ = row_halves(normal_two, m)
        inv_two_own, _ = row_halves(inv_two, m)
        grad_after_own = cot_own + norm_back(grad_two_own, normal_two_own, inv_two_own, gain_two)
        grad_attn_own = grad_after_own.astype(jnp.bfloat16)
        grad_attn_here = gather_rows_mp(grad_attn_own, m)
        ffn_late, grad_attn_here = lax.optimization_barrier((ffn_part, grad_attn_here))
        ffn_own = scatter_rows_mp(ffn_late, m, jnp.bfloat16)
        after_own, _ = row_halves(after_attn, m)
        out_own = (after_own + (ffn_own + b_down.astype(jnp.float32))).astype(jnp.bfloat16)
        block_out = gather_rows_mp(out_own, m)
        grad_w_out_t = jnp.einsum(
            "td,te->de", grad_attn_here, mixed, preferred_element_type=jnp.float32
        )
        grad_mixed = jnp.einsum(
            "td,ed->te", grad_attn_here, w_out, preferred_element_type=jnp.float32
        ).astype(jnp.bfloat16)
        grad_mixed = grad_mixed.reshape(seq_shape)
        gq, gk, gv = [], [], []
        for s in range(seq_count):
            dq_s, dk_s, dv_s = attend_backward(
                queries[s], key_rows[s], value_rows[s], doc_ids[s], log_totals[s], grad_mixed[s]
            )
            gq.append(dq_s)
            gk.append(dk_s)
            gv.append(dv_s)
        grad_q = jnp.stack(gq).reshape(row_count, local_width).astype(jnp.bfloat16)
        grad_k = jnp.stack(gk).reshape(row_count, local_width).astype(jnp.bfloat16)
        grad_v = jnp.stack(gv).reshape(row_count, local_width).astype(jnp.bfloat16)
        grad_proj = jnp.stack([grad_q, grad_k, grad_v], axis=1)
        grad_w_qkv = jnp.einsum(
            "td,tce->dce", normed_one, grad_proj, preferred_element_type=jnp.float32
        )
        grad_b_qv = jnp.stack(
            [
                jnp.sum(grad_q.astype(jnp.float32), axis=0),
                jnp.sum(grad_v.astype(jnp.float32), axis=0),
            ]
        )
        norm_one_part = jnp.einsum(
            "tce,dce->td", grad_proj, w_qkv, preferred_element_type=jnp.float32
        )
        grad_one_own = scatter_rows_mp(norm_one_part, m, jnp.bfloat16)
        normal_one_own, _ = row_halves(normal_one, m)
        inv_one_own, _ = row_halves(inv_one, m)
        grad_input_own = grad_after_own + norm_back(
            grad_one_own, normal_one_own, inv_one_own, gain_one
        )
        grad_input = gather_rows_into(grad_input_own, m)
        vector_terms = jnp.stack(
            [
                jnp.sum(grad_one_own * normal_one_own, axis=0),
                jnp.sum(grad_one_own, axis=0),
                jnp.sum(grad_two_own * normal_two_own, axis=0),
                jnp.sum(grad_two_own, axis=0),
                jnp.sum(grad_attn_own.astype(jnp.float32), axis=0),
                jnp.sum(cot_own, axis=0),
            ]
        )
        n_vec = vector_terms.size
        n_qv = grad_b_qv.size
        packed = jnp.concatenate([vector_terms.reshape(-1), grad_b_qv.reshape(-1), grad_b_up])
        qkv_cols = grad_w_qkv.shape[2] // 2
        sum_qkv = jnp.concatenate(
            [
                scatter_dp(grad_w_qkv[:, :, :qkv_cols], ndp),
                scatter_dp(grad_w_qkv[:, :, qkv_cols:], ndp, swap=True),
            ],
            axis=2,
        )
        packed, sum_qkv = lax.optimization_barrier((packed, sum_qkv))
        packed = reduce_tree(packed, "dp", ndp)
        vector_sum = reduce_tree(packed[:n_vec], "mp", nmp).reshape(vector_terms.shape)
        qv_sum = packed[n_vec : n_vec + n_qv].reshape(grad_b_qv.shape)
        up_sum = packed[n_vec + n_qv :]
        sum_out = scatter_dp(grad_w_out_t, ndp).T
        sum_up = scatter_dp(grad_w_up, ndp)
        sum_down = scatter_dp(grad_w_down_t, ndp, swap=True).T
        return (
            block_out,
            grad_input,
            vector_sum[0],
            vector_sum[1],
            sum_qkv,
            qv_sum,
            sum_out,
            vector_sum[4],
            vector_sum[2],
            vector_sum[3],
            sum_up,
            up_sum,
            sum_down,
            vector_sum[5],
        )

    return shards_body


def solution(mesh):
    return jax.shard_map(
        make_shards(mesh.shape["dp"], mesh.shape["mp"]),
        mesh=mesh,
        in_specs=(
            P("dp", None),
            P("dp", None),
            P(),
            P(),
            P(None, None, "mp"),
            P(None, "mp"),
            P("mp", None),
            P(),
            P(),
            P(),
            P(None, "mp"),
            P("mp"),
            P("mp", None),
            P(),
            P("dp", None),
        ),
        out_specs=(
            P("dp", None),
            P("dp", None),
            P(),
            P(),
            P("dp", None, "mp"),
            P(None, "mp"),
            P("mp", "dp"),
            P(),
            P(),
            P(),
            P("dp", "mp"),
            P("mp"),
            P("mp", "dp"),
            P(),
        ),
        check_vma=False,
    )
```

```python
import math

import jax
import jax.numpy as jnp
from jax import lax
from jax.sharding import PartitionSpec as P


HD = 64


epsilon = 1e-05


def normalize(values):
    average = jnp.mean(values, axis=-1, keepdims=True)
    centered = values - average
    variance = jnp.mean(centered * centered, axis=-1, keepdims=True)
    inverse = lax.rsqrt(variance + epsilon)
    return (centered * inverse, inverse)


def norm_back(grad_out, normal_rows, inverse, gain):
    grad_unit = grad_out * gain
    return inverse * (
        grad_unit
        - jnp.mean(grad_unit, axis=-1, keepdims=True)
        - normal_rows * jnp.mean(grad_unit * normal_rows, axis=-1, keepdims=True)
    )


def gelu_tanh(values):
    return (
        0.5
        * values
        * (1.0 + jnp.tanh(0.7978845608028654 * (values + 0.044715 * values * values * values)))
    )


MAX_DOC = 512


def key_window(offset, block_rows, seq_len):
    start = max(0, offset + 1 - MAX_DOC)
    start = (start // 128) * 128
    return start, min(seq_len, offset + block_rows)


def query_block_rows(seq_len):
    return min(256, seq_len)


def block_scores(query_block, key_rows, doc_rows, offset):
    block_rows = query_block.shape[0]
    kstart, kend = key_window(offset, block_rows, key_rows.shape[0])
    scores = jnp.einsum(
        "qhd,khd->hqk", query_block, key_rows[kstart:kend], preferred_element_type=jnp.float32
    ) * (1.0 / math.sqrt(HD))
    query_pos = offset + lax.iota(jnp.int32, block_rows)
    key_pos = kstart + lax.iota(jnp.int32, kend - kstart)
    block_docs = doc_rows[offset : offset + block_rows]
    allowed = (block_docs[:, None] == doc_rows[None, kstart:kend]) & (
        query_pos[:, None] >= key_pos[None, :]
    )
    return jnp.where(allowed[None], scores, -1e30)


def attend_forward(queries, key_rows, value_rows, doc_rows):
    seq_len = queries.shape[0]
    block_rows = query_block_rows(seq_len)
    outputs = []
    log_parts = []
    for offset in range(0, seq_len, block_rows):
      scores = block_scores(queries[offset : offset + block_rows], key_rows, doc_rows, offset)
      row_max = jnp.max(scores, axis=-1, keepdims=True)
      log_total = row_max + jnp.log(jnp.sum(jnp.exp(scores - row_max), axis=-1, keepdims=True))
      probabilities = jnp.exp(scores - log_total).astype(jnp.bfloat16)
      kstart, kend = key_window(offset, block_rows, seq_len)
      outputs.append(
          jnp.einsum(
              "hqk,khd->qhd",
              probabilities,
              value_rows[kstart:kend],
              preferred_element_type=jnp.float32,
          )
      )
      log_parts.append(log_total[..., 0])
    return (jnp.concatenate(outputs, axis=0), jnp.concatenate(log_parts, axis=1))


def attend_backward(queries, key_rows, value_rows, doc_rows, log_totals, grad_out):
    seq_len = queries.shape[0]
    block_rows = query_block_rows(seq_len)
    scale_factor = 1.0 / math.sqrt(HD)
    grad_queries = []
    key_parts = []
    value_parts = []
    for offset in range(0, seq_len, block_rows):
      query_block = queries[offset : offset + block_rows]
      grad_block = grad_out[offset : offset + block_rows]
      kstart, kend = key_window(offset, block_rows, seq_len)
      scores = block_scores(query_block, key_rows, doc_rows, offset)
      probabilities = jnp.exp(scores - log_totals[:, offset : offset + block_rows, None])
      grad_probs = jnp.einsum(
          "qhd,khd->hqk", grad_block, value_rows[kstart:kend], preferred_element_type=jnp.float32
      )
      row_dots = jnp.sum(probabilities * grad_probs, axis=-1, keepdims=True)
      grad_scores = (probabilities * (grad_probs - row_dots)).astype(jnp.bfloat16)
      grad_queries.append(
          scale_factor
          * jnp.einsum(
              "hqk,khd->qhd",
              grad_scores,
              key_rows[kstart:kend],
              preferred_element_type=jnp.float32,
          )
      )
      pad = ((kstart, seq_len - kend), (0, 0), (0, 0))
      key_parts.append(jnp.pad(scale_factor * jnp.einsum(
          "hqk,qhd->khd", grad_scores, query_block, preferred_element_type=jnp.float32
      ), pad))
      value_parts.append(jnp.pad(jnp.einsum(
          "hqk,qhd->khd",
          probabilities.astype(jnp.bfloat16),
          grad_block,
          preferred_element_type=jnp.float32,
      ), pad))
    grad_keys = key_parts[0]
    grad_values = value_parts[0]
    for key_part, value_part in zip(key_parts[1:], value_parts[1:]):
        grad_keys = grad_keys + key_part
        grad_values = grad_values + value_part
    return (jnp.concatenate(grad_queries, axis=0), grad_keys, grad_values)


def swap_mp(x):
    return lax.ppermute(x, "mp", [(0, 1), (1, 0)])


def row_halves(x, m):
    half = x.shape[0] // 2
    own = lax.dynamic_slice_in_dim(x, m * half, half, axis=0)
    other = lax.dynamic_slice_in_dim(x, (1 - m) * half, half, axis=0)
    return own, other


def join_pair(own, other, m, axis):
    return jnp.where(
        m == 0,
        jnp.concatenate([own, other], axis=axis),
        jnp.concatenate([other, own], axis=axis),
    )


def scatter_rows_mp(partial, m, send_dtype):
    own, other = row_halves(partial, m)
    return own + swap_mp(other.astype(send_dtype)).astype(own.dtype)


def gather_rows_mp(own, m):
    return join_pair(own, swap_mp(own), m, 0)


def gather_rows_into(own, m):
    half = own.shape[0]
    other = swap_mp(own)
    rows = jnp.zeros((2 * half,) + own.shape[1:], own.dtype)
    rows = lax.dynamic_update_slice_in_dim(rows, own, m * half, axis=0)
    return lax.dynamic_update_slice_in_dim(rows, other, (1 - m) * half, axis=0)


def scatter_dp(x, ndp, swap=False, vec=None):
    idx = lax.axis_index("dp")
    bits = ndp.bit_length() - 1
    chunk = x.shape[0] // ndp
    rest = x.shape[1:]
    cur = x.reshape((2,) * bits + (chunk,) + rest)
    remaining = list(range(bits - 1, -1, -1))
    order = list(range(bits))
    if swap and bits >= 3:
        order[1], order[2] = order[2], order[1]
    for level, bit in enumerate(order):
        pos = remaining.index(bit)
        mine = (idx >> bit) & 1
        keep = lax.dynamic_index_in_dim(cur, mine, pos, keepdims=False)
        send = lax.dynamic_index_in_dim(cur, 1 - mine, pos, keepdims=False)
        pairs = [(i, i ^ (1 << bit)) for i in range(ndp)]
        if vec is not None and level >= 1:
            flat = send.reshape(-1)
            got = lax.ppermute(jnp.concatenate([flat, vec]), "dp", pairs)
            vec = vec + got[flat.size :]
            got = got[: flat.size].reshape(send.shape)
        else:
            got = lax.ppermute(send, "dp", pairs)
        cur = keep + got
        remaining.pop(pos)
    out = cur.reshape((chunk,) + rest)
    if vec is None:
        return out
    vec = vec + lax.ppermute(vec, "dp", [(i, i ^ 1) for i in range(ndp)])
    return out, vec


def reduce_tree(x, name, size):
    bits = size.bit_length() - 1
    for bit in range(bits):
        x = x + lax.ppermute(x, name, [(i, i ^ (1 << bit)) for i in range(size)])
    return x


def make_shards(ndp, nmp):
    def shards_body(
        tokens,
        doc_ids,
        ln1_gain,
        ln1_bias,
        w_qkv,
        b_qv,
        w_out,
        b_out,
        ln2_gain,
        ln2_bias,
        w_up,
        b_up,
        w_down,
        b_down,
        cotangent,
    ):
        m = lax.axis_index("mp")
        w_out_other = swap_mp(w_out)
        row_count = tokens.shape[0]
        local_width = w_qkv.shape[2]
        seq_count, seq_len = doc_ids.shape
        seq_shape = (seq_count, seq_len, local_width // HD, HD)
        token_rows = tokens.astype(jnp.float32)
        normal_one, inv_one = normalize(token_rows)
        gain_one = ln1_gain.astype(jnp.float32)
        normed_one = (normal_one * gain_one + ln1_bias.astype(jnp.float32)).astype(jnp.bfloat16)
        projected = jnp.einsum(
            "td,dce->tce", normed_one, w_qkv, preferred_element_type=jnp.float32
        )
        bias_qv = b_qv.astype(jnp.float32)
        queries = (projected[:, 0] + bias_qv[0]).astype(jnp.bfloat16).reshape(seq_shape)
        key_rows = projected[:, 1].astype(jnp.bfloat16).reshape(seq_shape)
        value_rows = (projected[:, 2] + bias_qv[1]).astype(jnp.bfloat16).reshape(seq_shape)
        attended = []
        log_totals = []
        for s in range(seq_count):
            out_s, lse_s = attend_forward(queries[s], key_rows[s], value_rows[s], doc_ids[s])
            attended.append(out_s)
            log_totals.append(lse_s)
        mixed = jnp.stack(attended).reshape(row_count, local_width).astype(jnp.bfloat16)
        w_out_all = join_pair(w_out, w_out_other, m, 0)
        half_rows = row_count // 2
        attn_parts = []
        for part in range(2):
            rows = mixed[part * half_rows : (part + 1) * half_rows]
            rows_other = swap_mp(rows)
            attn_parts.append(
                jnp.dot(join_pair(rows, rows_other, m, 1), w_out_all,
                        preferred_element_type=jnp.float32)
            )
        attn_all = jnp.concatenate(attn_parts, axis=0)
        after_attn = token_rows + attn_all + b_out.astype(jnp.float32)
        gain_two = ln2_gain.astype(jnp.float32)
        normal_two, inv_two = normalize(after_attn)
        normed_two = (normal_two * gain_two + ln2_bias.astype(jnp.float32)).astype(jnp.bfloat16)
        up_rows = jnp.dot(normed_two, w_up, preferred_element_type=jnp.float32) + b_up.astype(
            jnp.float32
        )
        activated, gelu_pull = jax.vjp(gelu_tanh, up_rows)
        act_rows = activated.astype(jnp.bfloat16)
        ffn_part = jnp.dot(act_rows, w_down, preferred_element_type=jnp.float32)

        cot_rows = cotangent.astype(jnp.float32)
        cot_own, _ = row_halves(cot_rows, m)
        grad_w_down_t = jnp.einsum(
            "td,tf->df", cotangent, act_rows, preferred_element_type=jnp.float32
        )
        grad_act = jnp.einsum("td,fd->tf", cotangent, w_down, preferred_element_type=jnp.float32)
        grad_up = gelu_pull(grad_act)[0].astype(jnp.bfloat16)
        grad_w_up = jnp.einsum("td,tf->df", normed_two, grad_up, preferred_element_type=jnp.float32)
        grad_b_up = jnp.sum(grad_up.astype(jnp.float32), axis=0)
        norm_two_part = jnp.einsum("tf,df->td", grad_up, w_up, preferred_element_type=jnp.float32)
        grad_two_own = scatter_rows_mp(norm_two_part, m, jnp.bfloat16)
        normal_two_own, _ = row_halves(normal_two, m)
        inv_two_own, _ = row_halves(inv_two, m)
        grad_after_own = cot_own + norm_back(grad_two_own, normal_two_own, inv_two_own, gain_two)
        grad_attn_own = grad_after_own.astype(jnp.bfloat16)
        grad_attn_here = gather_rows_mp(grad_attn_own, m)
        ffn_late, grad_attn_here = lax.optimization_barrier((ffn_part, grad_attn_here))
        ffn_own = scatter_rows_mp(ffn_late, m, jnp.bfloat16)
        after_own, _ = row_halves(after_attn, m)
        out_own = (after_own + (ffn_own + b_down.astype(jnp.float32))).astype(jnp.bfloat16)
        block_out = gather_rows_mp(out_own, m)
        grad_w_out_t = jnp.einsum(
            "td,te->de", grad_attn_here, mixed, preferred_element_type=jnp.float32
        )
        grad_mixed = jnp.einsum(
            "td,ed->te", grad_attn_here, w_out, preferred_element_type=jnp.float32
        ).astype(jnp.bfloat16)
        grad_mixed = grad_mixed.reshape(seq_shape)
        gq, gk, gv = [], [], []
        for s in range(seq_count):
            dq_s, dk_s, dv_s = attend_backward(
                queries[s], key_rows[s], value_rows[s], doc_ids[s], log_totals[s], grad_mixed[s]
            )
            gq.append(dq_s)
            gk.append(dk_s)
            gv.append(dv_s)
        grad_q = jnp.stack(gq).reshape(row_count, local_width).astype(jnp.bfloat16)
        grad_k = jnp.stack(gk).reshape(row_count, local_width).astype(jnp.bfloat16)
        grad_v = jnp.stack(gv).reshape(row_count, local_width).astype(jnp.bfloat16)
        grad_proj = jnp.stack([grad_q, grad_k, grad_v], axis=1)
        grad_w_qkv = jnp.einsum(
            "td,tce->dce", normed_one, grad_proj, preferred_element_type=jnp.float32
        )
        grad_b_qv = jnp.stack(
            [
                jnp.sum(grad_q.astype(jnp.float32), axis=0),
                jnp.sum(grad_v.astype(jnp.float32), axis=0),
            ]
        )
        norm_one_part = jnp.einsum(
            "tce,dce->td", grad_proj, w_qkv, preferred_element_type=jnp.float32
        )
        grad_one_own = scatter_rows_mp(norm_one_part, m, jnp.bfloat16)
        normal_one_own, _ = row_halves(normal_one, m)
        inv_one_own, _ = row_halves(inv_one, m)
        grad_input_own = grad_after_own + norm_back(
            grad_one_own, normal_one_own, inv_one_own, gain_one
        )
        grad_input = gather_rows_into(grad_input_own, m)
        vector_terms = jnp.stack(
            [
                jnp.sum(grad_one_own * normal_one_own, axis=0),
                jnp.sum(grad_one_own, axis=0),
                jnp.sum(grad_two_own * normal_two_own, axis=0),
                jnp.sum(grad_two_own, axis=0),
                jnp.sum(grad_attn_own.astype(jnp.float32), axis=0),
                jnp.sum(cot_own, axis=0),
            ]
        )
        n_vec = vector_terms.size
        n_qv = grad_b_qv.size
        packed = jnp.concatenate([vector_terms.reshape(-1), grad_b_qv.reshape(-1), grad_b_up])
        qkv_cols = grad_w_qkv.shape[2] // 2
        qkv_a, packed = scatter_dp(grad_w_qkv[:, :, :qkv_cols], ndp, vec=packed)
        qkv_b = scatter_dp(grad_w_qkv[:, :, qkv_cols:], ndp, swap=True)
        sum_qkv = jnp.concatenate([qkv_a, qkv_b], axis=2)
        vector_sum = reduce_tree(packed[:n_vec], "mp", nmp).reshape(vector_terms.shape)
        qv_sum = packed[n_vec : n_vec + n_qv].reshape(grad_b_qv.shape)
        up_sum = packed[n_vec + n_qv :]
        sum_out = scatter_dp(grad_w_out_t, ndp).T
        sum_up = scatter_dp(grad_w_up, ndp)
        sum_down = scatter_dp(grad_w_down_t, ndp, swap=True).T
        return (
            block_out,
            grad_input,
            vector_sum[0],
            vector_sum[1],
            sum_qkv,
            qv_sum,
            sum_out,
            vector_sum[4],
            vector_sum[2],
            vector_sum[3],
            sum_up,
            up_sum,
            sum_down,
            vector_sum[5],
        )

    return shards_body


def solution(mesh):
    return jax.shard_map(
        make_shards(mesh.shape["dp"], mesh.shape["mp"]),
        mesh=mesh,
        in_specs=(
            P("dp", None),
            P("dp", None),
            P(),
            P(),
            P(None, None, "mp"),
            P(None, "mp"),
            P("mp", None),
            P(),
            P(),
            P(),
            P(None, "mp"),
            P("mp"),
            P("mp", None),
            P(),
            P("dp", None),
        ),
        out_specs=(
            P("dp", None),
            P("dp", None),
            P(),
            P(),
            P("dp", None, "mp"),
            P(None, "mp"),
            P("mp", "dp"),
            P(),
            P(),
            P(),
            P("dp", "mp"),
            P("mp"),
            P("mp", "dp"),
            P(),
        ),
        check_vma=False,
    )
```

```python
import math

import jax
import jax.numpy as jnp
from jax import lax
from jax.sharding import PartitionSpec as P


HD = 64


epsilon = 1e-05


def normalize(values):
    average = jnp.mean(values, axis=-1, keepdims=True)
    centered = values - average
    variance = jnp.mean(centered * centered, axis=-1, keepdims=True)
    inverse = lax.rsqrt(variance + epsilon)
    return (centered * inverse, inverse)


def norm_back(grad_out, normal_rows, inverse, gain):
    grad_unit = grad_out * gain
    return inverse * (
        grad_unit
        - jnp.mean(grad_unit, axis=-1, keepdims=True)
        - normal_rows * jnp.mean(grad_unit * normal_rows, axis=-1, keepdims=True)
    )


def gelu_tanh(values):
    return (
        0.5
        * values
        * (1.0 + jnp.tanh(0.7978845608028654 * (values + 0.044715 * values * values * values)))
    )


MAX_DOC = 512


def key_window(offset, block_rows, seq_len):
    start = max(0, offset + 1 - MAX_DOC)
    start = (start // 128) * 128
    return start, min(seq_len, offset + block_rows)


def query_block_rows(seq_len):
    return min(256, seq_len)


def block_scores(query_block, key_rows, doc_rows, offset):
    block_rows = query_block.shape[0]
    kstart, kend = key_window(offset, block_rows, key_rows.shape[0])
    scores = jnp.einsum(
        "qhd,khd->hqk", query_block, key_rows[kstart:kend], preferred_element_type=jnp.float32
    ) * (1.0 / math.sqrt(HD))
    query_pos = offset + lax.iota(jnp.int32, block_rows)
    key_pos = kstart + lax.iota(jnp.int32, kend - kstart)
    block_docs = doc_rows[offset : offset + block_rows]
    allowed = (block_docs[:, None] == doc_rows[None, kstart:kend]) & (
        query_pos[:, None] >= key_pos[None, :]
    )
    return jnp.where(allowed[None], scores, -1e30)


def attend_forward(queries, key_rows, value_rows, doc_rows):
    seq_len = queries.shape[0]
    block_rows = query_block_rows(seq_len)
    outputs = []
    log_parts = []
    for offset in range(0, seq_len, block_rows):
      scores = block_scores(queries[offset : offset + block_rows], key_rows, doc_rows, offset)
      row_max = jnp.max(scores, axis=-1, keepdims=True)
      log_total = row_max + jnp.log(jnp.sum(jnp.exp(scores - row_max), axis=-1, keepdims=True))
      probabilities = jnp.exp(scores - log_total).astype(jnp.bfloat16)
      kstart, kend = key_window(offset, block_rows, seq_len)
      outputs.append(
          jnp.einsum(
              "hqk,khd->qhd",
              probabilities,
              value_rows[kstart:kend],
              preferred_element_type=jnp.float32,
          )
      )
      log_parts.append(log_total[..., 0])
    return (jnp.concatenate(outputs, axis=0), jnp.concatenate(log_parts, axis=1))


def attend_backward(queries, key_rows, value_rows, doc_rows, log_totals, grad_out):
    seq_len = queries.shape[0]
    block_rows = query_block_rows(seq_len)
    scale_factor = 1.0 / math.sqrt(HD)
    grad_queries = []
    grad_keys = jnp.zeros(key_rows.shape, jnp.float32)
    grad_values = jnp.zeros(value_rows.shape, jnp.float32)
    for offset in range(0, seq_len, block_rows):
      query_block = queries[offset : offset + block_rows]
      grad_block = grad_out[offset : offset + block_rows]
      kstart, kend = key_window(offset, block_rows, seq_len)
      scores = block_scores(query_block, key_rows, doc_rows, offset)
      probabilities = jnp.exp(scores - log_totals[:, offset : offset + block_rows, None])
      grad_probs = jnp.einsum(
          "qhd,khd->hqk", grad_block, value_rows[kstart:kend], preferred_element_type=jnp.float32
      )
      row_dots = jnp.sum(probabilities * grad_probs, axis=-1, keepdims=True)
      grad_scores = (probabilities * (grad_probs - row_dots)).astype(jnp.bfloat16)
      grad_queries.append(
          scale_factor
          * jnp.einsum(
              "hqk,khd->qhd",
              grad_scores,
              key_rows[kstart:kend],
              preferred_element_type=jnp.float32,
          )
      )
      grad_keys = grad_keys.at[kstart:kend].add(scale_factor * jnp.einsum(
          "hqk,qhd->khd", grad_scores, query_block, preferred_element_type=jnp.float32
      ))
      grad_values = grad_values.at[kstart:kend].add(jnp.einsum(
          "hqk,qhd->khd",
          probabilities.astype(jnp.bfloat16),
          grad_block,
          preferred_element_type=jnp.float32,
      ))
    return (jnp.concatenate(grad_queries, axis=0), grad_keys, grad_values)


def swap_mp(x):
    return lax.ppermute(x, "mp", [(0, 1), (1, 0)])


def row_halves(x, m):
    half = x.shape[0] // 2
    own = lax.dynamic_slice_in_dim(x, m * half, half, axis=0)
    other = lax.dynamic_slice_in_dim(x, (1 - m) * half, half, axis=0)
    return own, other


def join_pair(own, other, m, axis):
    return jnp.where(
        m == 0,
        jnp.concatenate([own, other], axis=axis),
        jnp.concatenate([other, own], axis=axis),
    )


def scatter_rows_mp(partial, m, send_dtype):
    own, other = row_halves(partial, m)
    return own + swap_mp(other.astype(send_dtype)).astype(own.dtype)


def gather_rows_mp(own, m):
    return join_pair(own, swap_mp(own), m, 0)


def gather_rows_into(own, m):
    half = own.shape[0]
    other = swap_mp(own)
    rows = jnp.zeros((2 * half,) + own.shape[1:], own.dtype)
    rows = lax.dynamic_update_slice_in_dim(rows, own, m * half, axis=0)
    return lax.dynamic_update_slice_in_dim(rows, other, (1 - m) * half, axis=0)


def scatter_dp(x, ndp, swap=False, vec=None):
    idx = lax.axis_index("dp")
    bits = ndp.bit_length() - 1
    chunk = x.shape[0] // ndp
    rest = x.shape[1:]
    cur = x.reshape((2,) * bits + (chunk,) + rest)
    remaining = list(range(bits - 1, -1, -1))
    order = list(range(bits))
    if swap and bits >= 3:
        order[1], order[2] = order[2], order[1]
    for level, bit in enumerate(order):
        pos = remaining.index(bit)
        mine = (idx >> bit) & 1
        keep = lax.dynamic_index_in_dim(cur, mine, pos, keepdims=False)
        send = lax.dynamic_index_in_dim(cur, 1 - mine, pos, keepdims=False)
        pairs = [(i, i ^ (1 << bit)) for i in range(ndp)]
        if vec is not None and level >= 1:
            flat = send.reshape(-1)
            got = lax.ppermute(jnp.concatenate([flat, vec]), "dp", pairs)
            vec = vec + got[flat.size :]
            got = got[: flat.size].reshape(send.shape)
        else:
            got = lax.ppermute(send, "dp", pairs)
        cur = keep + got
        remaining.pop(pos)
    out = cur.reshape((chunk,) + rest)
    if vec is None:
        return out
    vec = vec + lax.ppermute(vec, "dp", [(i, i ^ 1) for i in range(ndp)])
    return out, vec


def reduce_tree(x, name, size):
    bits = size.bit_length() - 1
    for bit in range(bits):
        x = x + lax.ppermute(x, name, [(i, i ^ (1 << bit)) for i in range(size)])
    return x


def make_shards(ndp, nmp):
    def shards_body(
        tokens,
        doc_ids,
        ln1_gain,
        ln1_bias,
        w_qkv,
        b_qv,
        w_out,
        b_out,
        ln2_gain,
        ln2_bias,
        w_up,
        b_up,
        w_down,
        b_down,
        cotangent,
    ):
        m = lax.axis_index("mp")
        w_out_other = swap_mp(w_out)
        row_count = tokens.shape[0]
        local_width = w_qkv.shape[2]
        seq_count, seq_len = doc_ids.shape
        seq_shape = (seq_count, seq_len, local_width // HD, HD)
        token_rows = tokens.astype(jnp.float32)
        normal_one, inv_one = normalize(token_rows)
        gain_one = ln1_gain.astype(jnp.float32)
        normed_one = (normal_one * gain_one + ln1_bias.astype(jnp.float32)).astype(jnp.bfloat16)
        projected = jnp.einsum(
            "td,dce->tce", normed_one, w_qkv, preferred_element_type=jnp.float32
        )
        bias_qv = b_qv.astype(jnp.float32)
        queries = (projected[:, 0] + bias_qv[0]).astype(jnp.bfloat16).reshape(seq_shape)
        key_rows = projected[:, 1].astype(jnp.bfloat16).reshape(seq_shape)
        value_rows = (projected[:, 2] + bias_qv[1]).astype(jnp.bfloat16).reshape(seq_shape)
        attended = []
        log_totals = []
        for s in range(seq_count):
            out_s, lse_s = attend_forward(queries[s], key_rows[s], value_rows[s], doc_ids[s])
            attended.append(out_s)
            log_totals.append(lse_s)
        mixed = jnp.stack(attended).reshape(row_count, local_width).astype(jnp.bfloat16)
        w_out_all = join_pair(w_out, w_out_other, m, 0)
        half_rows = row_count // 2
        attn_parts = []
        for part in range(2):
            rows = mixed[part * half_rows : (part + 1) * half_rows]
            rows_other = swap_mp(rows)
            attn_parts.append(
                jnp.dot(join_pair(rows, rows_other, m, 1), w_out_all,
                        preferred_element_type=jnp.float32)
            )
        attn_all = jnp.concatenate(attn_parts, axis=0)
        after_attn = token_rows + attn_all + b_out.astype(jnp.float32)
        gain_two = ln2_gain.astype(jnp.float32)
        normal_two, inv_two = normalize(after_attn)
        normed_two = (normal_two * gain_two + ln2_bias.astype(jnp.float32)).astype(jnp.bfloat16)
        up_rows = jnp.dot(normed_two, w_up, preferred_element_type=jnp.float32) + b_up.astype(
            jnp.float32
        )
        activated, gelu_pull = jax.vjp(gelu_tanh, up_rows)
        act_rows = activated.astype(jnp.bfloat16)
        ffn_part = jnp.dot(act_rows, w_down, preferred_element_type=jnp.float32)

        cot_rows = cotangent.astype(jnp.float32)
        cot_own, _ = row_halves(cot_rows, m)
        grad_w_down_t = jnp.einsum(
            "td,tf->df", cotangent, act_rows, preferred_element_type=jnp.float32
        )
        grad_act = jnp.einsum("td,fd->tf", cotangent, w_down, preferred_element_type=jnp.float32)
        grad_up = gelu_pull(grad_act)[0].astype(jnp.bfloat16)
        grad_w_up = jnp.einsum("td,tf->df", normed_two, grad_up, preferred_element_type=jnp.float32)
        grad_b_up = jnp.sum(grad_up.astype(jnp.float32), axis=0)
        norm_two_part = jnp.einsum("tf,df->td", grad_up, w_up, preferred_element_type=jnp.float32)
        grad_two_own = scatter_rows_mp(norm_two_part, m, jnp.bfloat16)
        normal_two_own, _ = row_halves(normal_two, m)
        inv_two_own, _ = row_halves(inv_two, m)
        grad_after_own = cot_own + norm_back(grad_two_own, normal_two_own, inv_two_own, gain_two)
        grad_attn_own = grad_after_own.astype(jnp.bfloat16)
        grad_attn_here = gather_rows_mp(grad_attn_own, m)
        ffn_late, grad_attn_here = lax.optimization_barrier((ffn_part, grad_attn_here))
        ffn_own = scatter_rows_mp(ffn_late, m, jnp.bfloat16)
        after_own, _ = row_halves(after_attn, m)
        out_own = (after_own + (ffn_own + b_down.astype(jnp.float32))).astype(jnp.bfloat16)
        block_out = gather_rows_mp(out_own, m)
        grad_w_out_t = jnp.einsum(
            "td,te->de", grad_attn_here, mixed, preferred_element_type=jnp.float32
        )
        grad_mixed = jnp.einsum(
            "td,ed->te", grad_attn_here, w_out, preferred_element_type=jnp.float32
        ).astype(jnp.bfloat16)
        grad_mixed = grad_mixed.reshape(seq_shape)
        gq, gk, gv = [], [], []
        for s in range(seq_count):
            dq_s, dk_s, dv_s = attend_backward(
                queries[s], key_rows[s], value_rows[s], doc_ids[s], log_totals[s], grad_mixed[s]
            )
            gq.append(dq_s)
            gk.append(dk_s)
            gv.append(dv_s)
        grad_q = jnp.stack(gq).reshape(row_count, local_width).astype(jnp.bfloat16)
        grad_k = jnp.stack(gk).reshape(row_count, local_width).astype(jnp.bfloat16)
        grad_v = jnp.stack(gv).reshape(row_count, local_width).astype(jnp.bfloat16)
        grad_proj = jnp.stack([grad_q, grad_k, grad_v], axis=1)
        grad_w_qkv = jnp.einsum(
            "td,tce->dce", normed_one, grad_proj, preferred_element_type=jnp.float32
        )
        grad_b_qv = jnp.stack(
            [
                jnp.sum(grad_q.astype(jnp.float32), axis=0),
                jnp.sum(grad_v.astype(jnp.float32), axis=0),
            ]
        )
        norm_one_part = jnp.einsum(
            "tce,dce->td", grad_proj, w_qkv, preferred_element_type=jnp.float32
        )
        grad_one_own = scatter_rows_mp(norm_one_part, m, jnp.bfloat16)
        normal_one_own, _ = row_halves(normal_one, m)
        inv_one_own, _ = row_halves(inv_one, m)
        grad_input_own = grad_after_own + norm_back(
            grad_one_own, normal_one_own, inv_one_own, gain_one
        )
        grad_input = gather_rows_into(grad_input_own, m)
        vector_terms = jnp.stack(
            [
                jnp.sum(grad_one_own * normal_one_own, axis=0),
                jnp.sum(grad_one_own, axis=0),
                jnp.sum(grad_two_own * normal_two_own, axis=0),
                jnp.sum(grad_two_own, axis=0),
                jnp.sum(grad_attn_own.astype(jnp.float32), axis=0),
                jnp.sum(cot_own, axis=0),
            ]
        )
        n_vec = vector_terms.size
        n_qv = grad_b_qv.size
        packed = jnp.concatenate([vector_terms.reshape(-1), grad_b_qv.reshape(-1), grad_b_up])
        qkv_cols = max(128, (grad_w_qkv.shape[2] * 2 // 3) // 128 * 128)
        qkv_a = scatter_dp(grad_w_qkv[:, :, :qkv_cols], ndp)
        qkv_b, packed = scatter_dp(grad_w_qkv[:, :, qkv_cols:], ndp, swap=True, vec=packed)
        sum_qkv = jnp.concatenate([qkv_a, qkv_b], axis=2)
        vector_sum = reduce_tree(packed[:n_vec], "mp", nmp).reshape(vector_terms.shape)
        qv_sum = packed[n_vec : n_vec + n_qv].reshape(grad_b_qv.shape)
        up_sum = packed[n_vec + n_qv :]
        sum_out = scatter_dp(grad_w_out_t, ndp).T
        sum_up = scatter_dp(grad_w_up, ndp)
        sum_down = scatter_dp(grad_w_down_t, ndp, swap=True).T
        return (
            block_out,
            grad_input,
            vector_sum[0],
            vector_sum[1],
            sum_qkv,
            qv_sum,
            sum_out,
            vector_sum[4],
            vector_sum[2],
            vector_sum[3],
            sum_up,
            up_sum,
            sum_down,
            vector_sum[5],
        )

    return shards_body


def solution(mesh):
    return jax.shard_map(
        make_shards(mesh.shape["dp"], mesh.shape["mp"]),
        mesh=mesh,
        in_specs=(
            P("dp", None),
            P("dp", None),
            P(),
            P(),
            P(None, None, "mp"),
            P(None, "mp"),
            P("mp", None),
            P(),
            P(),
            P(),
            P(None, "mp"),
            P("mp"),
            P("mp", None),
            P(),
            P("dp", None),
        ),
        out_specs=(
            P("dp", None),
            P("dp", None),
            P(),
            P(),
            P("dp", None, "mp"),
            P(None, "mp"),
            P("mp", "dp"),
            P(),
            P(),
            P(),
            P("dp", "mp"),
            P("mp"),
            P("mp", "dp"),
            P(),
        ),
        check_vma=False,
    )
```

```python
import math

import jax
import jax.numpy as jnp
from jax import lax
from jax.sharding import PartitionSpec as P


HD = 64


epsilon = 1e-05


def normalize(values):
    average = jnp.mean(values, axis=-1, keepdims=True)
    centered = values - average
    variance = jnp.mean(centered * centered, axis=-1, keepdims=True)
    inverse = lax.rsqrt(variance + epsilon)
    return (centered * inverse, inverse)


def norm_back(grad_out, normal_rows, inverse, gain):
    grad_unit = grad_out * gain
    return inverse * (
        grad_unit
        - jnp.mean(grad_unit, axis=-1, keepdims=True)
        - normal_rows * jnp.mean(grad_unit * normal_rows, axis=-1, keepdims=True)
    )


def gelu_tanh(values):
    return (
        0.5
        * values
        * (1.0 + jnp.tanh(0.7978845608028654 * (values + 0.044715 * values * values * values)))
    )


MAX_DOC = 512


def key_window(offset, block_rows, seq_len):
    start = max(0, offset + 1 - MAX_DOC)
    start = (start // 128) * 128
    return start, min(seq_len, offset + block_rows)


def query_block_rows(seq_len):
    return min(256, seq_len)


def block_scores(query_block, key_rows, doc_rows, offset):
    block_rows = query_block.shape[0]
    kstart, kend = key_window(offset, block_rows, key_rows.shape[0])
    scores = jnp.einsum(
        "qhd,khd->hqk", query_block, key_rows[kstart:kend], preferred_element_type=jnp.float32
    ) * (1.0 / math.sqrt(HD))
    query_pos = offset + lax.iota(jnp.int32, block_rows)
    key_pos = kstart + lax.iota(jnp.int32, kend - kstart)
    block_docs = doc_rows[offset : offset + block_rows]
    allowed = (block_docs[:, None] == doc_rows[None, kstart:kend]) & (
        query_pos[:, None] >= key_pos[None, :]
    )
    return jnp.where(allowed[None], scores, -1e30)


def attend_forward(queries, key_rows, value_rows, doc_rows):
    seq_len = queries.shape[0]
    block_rows = query_block_rows(seq_len)
    outputs = []
    log_parts = []
    for offset in range(0, seq_len, block_rows):
      scores = block_scores(queries[offset : offset + block_rows], key_rows, doc_rows, offset)
      row_max = jnp.max(scores, axis=-1, keepdims=True)
      log_total = row_max + jnp.log(jnp.sum(jnp.exp(scores - row_max), axis=-1, keepdims=True))
      probabilities = jnp.exp(scores - log_total).astype(jnp.bfloat16)
      kstart, kend = key_window(offset, block_rows, seq_len)
      outputs.append(
          jnp.einsum(
              "hqk,khd->qhd",
              probabilities,
              value_rows[kstart:kend],
              preferred_element_type=jnp.float32,
          )
      )
      log_parts.append(log_total[..., 0])
    return (jnp.concatenate(outputs, axis=0), jnp.concatenate(log_parts, axis=1))


def attend_backward(queries, key_rows, value_rows, doc_rows, log_totals, grad_out):
    seq_len = queries.shape[0]
    block_rows = query_block_rows(seq_len)
    scale_factor = 1.0 / math.sqrt(HD)
    grad_queries = []
    grad_keys = jnp.zeros(key_rows.shape, jnp.float32)
    grad_values = jnp.zeros(value_rows.shape, jnp.float32)
    for offset in range(0, seq_len, block_rows):
      query_block = queries[offset : offset + block_rows]
      grad_block = grad_out[offset : offset + block_rows]
      kstart, kend = key_window(offset, block_rows, seq_len)
      scores = block_scores(query_block, key_rows, doc_rows, offset)
      probabilities = jnp.exp(scores - log_totals[:, offset : offset + block_rows, None])
      grad_probs = jnp.einsum(
          "qhd,khd->hqk", grad_block, value_rows[kstart:kend], preferred_element_type=jnp.float32
      )
      row_dots = jnp.sum(probabilities * grad_probs, axis=-1, keepdims=True)
      grad_scores = (probabilities * (grad_probs - row_dots)).astype(jnp.bfloat16)
      grad_queries.append(
          scale_factor
          * jnp.einsum(
              "hqk,khd->qhd",
              grad_scores,
              key_rows[kstart:kend],
              preferred_element_type=jnp.float32,
          )
      )
      grad_keys = grad_keys.at[kstart:kend].add(scale_factor * jnp.einsum(
          "hqk,qhd->khd", grad_scores, query_block, preferred_element_type=jnp.float32
      ))
      grad_values = grad_values.at[kstart:kend].add(jnp.einsum(
          "hqk,qhd->khd",
          probabilities.astype(jnp.bfloat16),
          grad_block,
          preferred_element_type=jnp.float32,
      ))
    return (jnp.concatenate(grad_queries, axis=0), grad_keys, grad_values)


def swap_mp(x):
    return lax.ppermute(x, "mp", [(0, 1), (1, 0)])


def row_halves(x, m):
    half = x.shape[0] // 2
    own = lax.dynamic_slice_in_dim(x, m * half, half, axis=0)
    other = lax.dynamic_slice_in_dim(x, (1 - m) * half, half, axis=0)
    return own, other


def join_pair(own, other, m, axis):
    return jnp.where(
        m == 0,
        jnp.concatenate([own, other], axis=axis),
        jnp.concatenate([other, own], axis=axis),
    )


def scatter_rows_mp(partial, m, send_dtype):
    own, other = row_halves(partial, m)
    return own + swap_mp(other.astype(send_dtype)).astype(own.dtype)


def gather_rows_mp(own, m):
    return join_pair(own, swap_mp(own), m, 0)


def gather_rows_into(own, m):
    half = own.shape[0]
    other = swap_mp(own)
    rows = jnp.zeros((2 * half,) + own.shape[1:], own.dtype)
    rows = lax.dynamic_update_slice_in_dim(rows, own, m * half, axis=0)
    return lax.dynamic_update_slice_in_dim(rows, other, (1 - m) * half, axis=0)


def scatter_dp(x, ndp, swap=False, vec=None):
    idx = lax.axis_index("dp")
    bits = ndp.bit_length() - 1
    chunk = x.shape[0] // ndp
    rest = x.shape[1:]
    cur = x.reshape((2,) * bits + (chunk,) + rest)
    remaining = list(range(bits - 1, -1, -1))
    order = list(range(bits))
    if swap and bits >= 3:
        order[1], order[2] = order[2], order[1]
    for level, bit in enumerate(order):
        pos = remaining.index(bit)
        mine = (idx >> bit) & 1
        keep = lax.dynamic_index_in_dim(cur, mine, pos, keepdims=False)
        send = lax.dynamic_index_in_dim(cur, 1 - mine, pos, keepdims=False)
        pairs = [(i, i ^ (1 << bit)) for i in range(ndp)]
        if vec is not None and level >= 1:
            flat = send.reshape(-1)
            got = lax.ppermute(jnp.concatenate([flat, vec]), "dp", pairs)
            vec = vec + got[flat.size :]
            got = got[: flat.size].reshape(send.shape)
        else:
            got = lax.ppermute(send, "dp", pairs)
        cur = keep + got
        remaining.pop(pos)
    out = cur.reshape((chunk,) + rest)
    if vec is None:
        return out
    vec = vec + lax.ppermute(vec, "dp", [(i, i ^ 1) for i in range(ndp)])
    return out, vec


def reduce_tree(x, name, size):
    bits = size.bit_length() - 1
    for bit in range(bits):
        x = x + lax.ppermute(x, name, [(i, i ^ (1 << bit)) for i in range(size)])
    return x


def make_shards(ndp, nmp):
    def shards_body(
        tokens,
        doc_ids,
        ln1_gain,
        ln1_bias,
        w_qkv,
        b_qv,
        w_out,
        b_out,
        ln2_gain,
        ln2_bias,
        w_up,
        b_up,
        w_down,
        b_down,
        cotangent,
    ):
        m = lax.axis_index("mp")
        w_out_other = swap_mp(w_out)
        row_count = tokens.shape[0]
        local_width = w_qkv.shape[2]
        seq_count, seq_len = doc_ids.shape
        seq_shape = (seq_count, seq_len, local_width // HD, HD)
        token_rows = tokens.astype(jnp.float32)
        normal_one, inv_one = normalize(token_rows)
        gain_one = ln1_gain.astype(jnp.float32)
        normed_one = (normal_one * gain_one + ln1_bias.astype(jnp.float32)).astype(jnp.bfloat16)
        projected = jnp.einsum(
            "td,dce->tce", normed_one, w_qkv, preferred_element_type=jnp.float32
        )
        bias_qv = b_qv.astype(jnp.float32)
        queries = (projected[:, 0] + bias_qv[0]).astype(jnp.bfloat16).reshape(seq_shape)
        key_rows = projected[:, 1].astype(jnp.bfloat16).reshape(seq_shape)
        value_rows = (projected[:, 2] + bias_qv[1]).astype(jnp.bfloat16).reshape(seq_shape)
        attended = []
        log_totals = []
        for s in range(seq_count):
            out_s, lse_s = attend_forward(queries[s], key_rows[s], value_rows[s], doc_ids[s])
            attended.append(out_s)
            log_totals.append(lse_s)
        mixed = jnp.stack(attended).reshape(row_count, local_width).astype(jnp.bfloat16)
        w_out_all = join_pair(w_out, w_out_other, m, 0)
        half_rows = row_count // 2
        attn_parts = []
        for part in range(2):
            rows = mixed[part * half_rows : (part + 1) * half_rows]
            rows_other = swap_mp(rows)
            attn_parts.append(
                jnp.dot(join_pair(rows, rows_other, m, 1), w_out_all,
                        preferred_element_type=jnp.float32)
            )
        attn_all = jnp.concatenate(attn_parts, axis=0)
        after_attn = token_rows + attn_all + b_out.astype(jnp.float32)
        gain_two = ln2_gain.astype(jnp.float32)
        normal_two, inv_two = normalize(after_attn)
        normed_two = (normal_two * gain_two + ln2_bias.astype(jnp.float32)).astype(jnp.bfloat16)
        up_rows = jnp.dot(normed_two, w_up, preferred_element_type=jnp.float32) + b_up.astype(
            jnp.float32
        )
        activated, gelu_pull = jax.vjp(gelu_tanh, up_rows)
        act_rows = activated.astype(jnp.bfloat16)
        ffn_part = jnp.dot(act_rows, w_down, preferred_element_type=jnp.float32)

        cot_rows = cotangent.astype(jnp.float32)
        cot_own, _ = row_halves(cot_rows, m)
        grad_w_down_t = jnp.einsum(
            "td,tf->df", cotangent, act_rows, preferred_element_type=jnp.float32
        )
        grad_act = jnp.einsum("td,fd->tf", cotangent, w_down, preferred_element_type=jnp.float32)
        grad_up = gelu_pull(grad_act)[0].astype(jnp.bfloat16)
        grad_w_up = jnp.einsum("td,tf->df", normed_two, grad_up, preferred_element_type=jnp.float32)
        grad_b_up = jnp.sum(grad_up.astype(jnp.float32), axis=0)
        norm_two_part = jnp.einsum("tf,df->td", grad_up, w_up, preferred_element_type=jnp.float32)
        grad_two_own = scatter_rows_mp(norm_two_part, m, jnp.bfloat16)
        normal_two_own, _ = row_halves(normal_two, m)
        inv_two_own, _ = row_halves(inv_two, m)
        grad_after_own = cot_own + norm_back(grad_two_own, normal_two_own, inv_two_own, gain_two)
        grad_attn_own = grad_after_own.astype(jnp.bfloat16)
        grad_attn_here = gather_rows_mp(grad_attn_own, m)
        ffn_late, grad_attn_here = lax.optimization_barrier((ffn_part, grad_attn_here))
        ffn_own = scatter_rows_mp(ffn_late, m, jnp.bfloat16)
        after_own, _ = row_halves(after_attn, m)
        out_own = (after_own + (ffn_own + b_down.astype(jnp.float32))).astype(jnp.bfloat16)
        block_out = gather_rows_mp(out_own, m)
        grad_w_out_t = jnp.einsum(
            "td,te->de", grad_attn_here, mixed, preferred_element_type=jnp.float32
        )
        grad_mixed = jnp.einsum(
            "td,ed->te", grad_attn_here, w_out, preferred_element_type=jnp.float32
        ).astype(jnp.bfloat16)
        grad_mixed = grad_mixed.reshape(seq_shape)
        gq, gk, gv = [], [], []
        for s in range(seq_count):
            dq_s, dk_s, dv_s = attend_backward(
                queries[s], key_rows[s], value_rows[s], doc_ids[s], log_totals[s], grad_mixed[s]
            )
            gq.append(dq_s)
            gk.append(dk_s)
            gv.append(dv_s)
        grad_q = jnp.stack(gq).reshape(row_count, local_width).astype(jnp.bfloat16)
        grad_k = jnp.stack(gk).reshape(row_count, local_width).astype(jnp.bfloat16)
        grad_v = jnp.stack(gv).reshape(row_count, local_width).astype(jnp.bfloat16)
        grad_proj = jnp.stack([grad_q, grad_k, grad_v], axis=1)
        grad_w_qkv = jnp.einsum(
            "td,tce->dce", normed_one, grad_proj, preferred_element_type=jnp.float32
        )
        grad_b_qv = jnp.stack(
            [
                jnp.sum(grad_q.astype(jnp.float32), axis=0),
                jnp.sum(grad_v.astype(jnp.float32), axis=0),
            ]
        )
        norm_one_part = jnp.einsum(
            "tce,dce->td", grad_proj, w_qkv, preferred_element_type=jnp.float32
        )
        grad_one_own = scatter_rows_mp(norm_one_part, m, jnp.bfloat16)
        normal_one_own, _ = row_halves(normal_one, m)
        inv_one_own, _ = row_halves(inv_one, m)
        grad_input_own = grad_after_own + norm_back(
            grad_one_own, normal_one_own, inv_one_own, gain_one
        )
        grad_input = gather_rows_into(grad_input_own, m)
        vector_terms = jnp.stack(
            [
                jnp.sum(grad_one_own * normal_one_own, axis=0),
                jnp.sum(grad_one_own, axis=0),
                jnp.sum(grad_two_own * normal_two_own, axis=0),
                jnp.sum(grad_two_own, axis=0),
                jnp.sum(grad_attn_own.astype(jnp.float32), axis=0),
                jnp.sum(cot_own, axis=0),
            ]
        )
        n_vec = vector_terms.size
        n_qv = grad_b_qv.size
        packed = jnp.concatenate([vector_terms.reshape(-1), grad_b_qv.reshape(-1), grad_b_up])
        qkv_cols = max(128, (grad_w_qkv.shape[2] * 2 // 3) // 128 * 128)
        qkv_vec = qkv_cols // 2
        qkv_a, packed = scatter_dp(grad_w_qkv[:, :, :qkv_vec], ndp, vec=packed)
        qkv_c = scatter_dp(grad_w_qkv[:, :, qkv_vec:qkv_cols], ndp)
        qkv_b = scatter_dp(grad_w_qkv[:, :, qkv_cols:], ndp, swap=True)
        sum_qkv = jnp.concatenate([qkv_a, qkv_c, qkv_b], axis=2)
        vector_sum = reduce_tree(packed[:n_vec], "mp", nmp).reshape(vector_terms.shape)
        qv_sum = packed[n_vec : n_vec + n_qv].reshape(grad_b_qv.shape)
        up_sum = packed[n_vec + n_qv :]
        sum_out = scatter_dp(grad_w_out_t, ndp).T
        sum_up = scatter_dp(grad_w_up, ndp)
        sum_down = scatter_dp(grad_w_down_t, ndp, swap=True).T
        return (
            block_out,
            grad_input,
            vector_sum[0],
            vector_sum[1],
            sum_qkv,
            qv_sum,
            sum_out,
            vector_sum[4],
            vector_sum[2],
            vector_sum[3],
            sum_up,
            up_sum,
            sum_down,
            vector_sum[5],
        )

    return shards_body


def solution(mesh):
    return jax.shard_map(
        make_shards(mesh.shape["dp"], mesh.shape["mp"]),
        mesh=mesh,
        in_specs=(
            P("dp", None),
            P("dp", None),
            P(),
            P(),
            P(None, None, "mp"),
            P(None, "mp"),
            P("mp", None),
            P(),
            P(),
            P(),
            P(None, "mp"),
            P("mp"),
            P("mp", None),
            P(),
            P("dp", None),
        ),
        out_specs=(
            P("dp", None),
            P("dp", None),
            P(),
            P(),
            P("dp", None, "mp"),
            P(None, "mp"),
            P("mp", "dp"),
            P(),
            P(),
            P(),
            P("dp", "mp"),
            P("mp"),
            P("mp", "dp"),
            P(),
        ),
        check_vma=False,
    )
```

```python
import math

import jax
import jax.numpy as jnp
from jax import lax
from jax.sharding import PartitionSpec as P


HD = 64


epsilon = 1e-05


def normalize(values):
    average = jnp.mean(values, axis=-1, keepdims=True)
    centered = values - average
    variance = jnp.mean(centered * centered, axis=-1, keepdims=True)
    inverse = lax.rsqrt(variance + epsilon)
    return (centered * inverse, inverse)


def norm_back(grad_out, normal_rows, inverse, gain):
    grad_unit = grad_out * gain
    return inverse * (
        grad_unit
        - jnp.mean(grad_unit, axis=-1, keepdims=True)
        - normal_rows * jnp.mean(grad_unit * normal_rows, axis=-1, keepdims=True)
    )


def gelu_tanh(values):
    return (
        0.5
        * values
        * (1.0 + jnp.tanh(0.7978845608028654 * (values + 0.044715 * values * values * values)))
    )


MAX_DOC = 512


def key_window(offset, block_rows, seq_len):
    start = max(0, offset + 1 - MAX_DOC)
    start = (start // 128) * 128
    return start, min(seq_len, offset + block_rows)


def query_block_rows(seq_len):
    return min(256, seq_len)


def block_scores(query_block, key_rows, doc_rows, offset):
    block_rows = query_block.shape[0]
    kstart, kend = key_window(offset, block_rows, key_rows.shape[0])
    scores = jnp.einsum(
        "qhd,khd->hqk", query_block, key_rows[kstart:kend], preferred_element_type=jnp.float32
    ) * (1.0 / math.sqrt(HD))
    query_pos = offset + lax.iota(jnp.int32, block_rows)
    key_pos = kstart + lax.iota(jnp.int32, kend - kstart)
    block_docs = doc_rows[offset : offset + block_rows]
    allowed = (block_docs[:, None] == doc_rows[None, kstart:kend]) & (
        query_pos[:, None] >= key_pos[None, :]
    )
    return jnp.where(allowed[None], scores, -1e30)


def attend_forward(queries, key_rows, value_rows, doc_rows):
    seq_len = queries.shape[0]
    block_rows = query_block_rows(seq_len)
    outputs = []
    log_parts = []
    for offset in range(0, seq_len, block_rows):
      scores = block_scores(queries[offset : offset + block_rows], key_rows, doc_rows, offset)
      row_max = jnp.max(scores, axis=-1, keepdims=True)
      log_total = row_max + jnp.log(jnp.sum(jnp.exp(scores - row_max), axis=-1, keepdims=True))
      probabilities = jnp.exp(scores - log_total).astype(jnp.bfloat16)
      kstart, kend = key_window(offset, block_rows, seq_len)
      outputs.append(
          jnp.einsum(
              "hqk,khd->qhd",
              probabilities,
              value_rows[kstart:kend],
              preferred_element_type=jnp.float32,
          )
      )
      log_parts.append(log_total[..., 0])
    return (jnp.concatenate(outputs, axis=0), jnp.concatenate(log_parts, axis=1))


def attend_backward(queries, key_rows, value_rows, doc_rows, log_totals, grad_out):
    seq_len = queries.shape[0]
    block_rows = query_block_rows(seq_len)
    scale_factor = 1.0 / math.sqrt(HD)
    grad_queries = []
    grad_keys = jnp.zeros(key_rows.shape, jnp.float32)
    grad_values = jnp.zeros(value_rows.shape, jnp.float32)
    for offset in range(0, seq_len, block_rows):
      query_block = queries[offset : offset + block_rows]
      grad_block = grad_out[offset : offset + block_rows]
      kstart, kend = key_window(offset, block_rows, seq_len)
      scores = block_scores(query_block, key_rows, doc_rows, offset)
      probabilities = jnp.exp(scores - log_totals[:, offset : offset + block_rows, None])
      grad_probs = jnp.einsum(
          "qhd,khd->hqk", grad_block, value_rows[kstart:kend], preferred_element_type=jnp.float32
      )
      row_dots = jnp.sum(probabilities * grad_probs, axis=-1, keepdims=True)
      grad_scores = (probabilities * (grad_probs - row_dots)).astype(jnp.bfloat16)
      grad_queries.append(
          scale_factor
          * jnp.einsum(
              "hqk,khd->qhd",
              grad_scores,
              key_rows[kstart:kend],
              preferred_element_type=jnp.float32,
          )
      )
      grad_keys = grad_keys.at[kstart:kend].add(scale_factor * jnp.einsum(
          "hqk,qhd->khd", grad_scores, query_block, preferred_element_type=jnp.float32
      ))
      grad_values = grad_values.at[kstart:kend].add(jnp.einsum(
          "hqk,qhd->khd",
          probabilities.astype(jnp.bfloat16),
          grad_block,
          preferred_element_type=jnp.float32,
      ))
    return (jnp.concatenate(grad_queries, axis=0), grad_keys, grad_values)


def swap_mp(x):
    return lax.ppermute(x, "mp", [(0, 1), (1, 0)])


def row_halves(x, m):
    half = x.shape[0] // 2
    own = lax.dynamic_slice_in_dim(x, m * half, half, axis=0)
    other = lax.dynamic_slice_in_dim(x, (1 - m) * half, half, axis=0)
    return own, other


def join_pair(own, other, m, axis):
    return jnp.where(
        m == 0,
        jnp.concatenate([own, other], axis=axis),
        jnp.concatenate([other, own], axis=axis),
    )


def scatter_rows_mp(partial, m, send_dtype):
    own, other = row_halves(partial, m)
    return own + swap_mp(other.astype(send_dtype)).astype(own.dtype)


def gather_rows_mp(own, m):
    return join_pair(own, swap_mp(own), m, 0)


def gather_rows_into(own, m):
    half = own.shape[0]
    other = swap_mp(own)
    rows = jnp.zeros((2 * half,) + own.shape[1:], own.dtype)
    rows = lax.dynamic_update_slice_in_dim(rows, own, m * half, axis=0)
    return lax.dynamic_update_slice_in_dim(rows, other, (1 - m) * half, axis=0)


def scatter_dp(x, ndp, swap=False, vec=None):
    idx = lax.axis_index("dp")
    bits = ndp.bit_length() - 1
    chunk = x.shape[0] // ndp
    rest = x.shape[1:]
    cur = x.reshape((2,) * bits + (chunk,) + rest)
    remaining = list(range(bits - 1, -1, -1))
    order = list(range(bits))
    if swap and bits >= 3:
        order[1], order[2] = order[2], order[1]
    for level, bit in enumerate(order):
        pos = remaining.index(bit)
        mine = (idx >> bit) & 1
        keep = lax.dynamic_index_in_dim(cur, mine, pos, keepdims=False)
        send = lax.dynamic_index_in_dim(cur, 1 - mine, pos, keepdims=False)
        pairs = [(i, i ^ (1 << bit)) for i in range(ndp)]
        if vec is not None and level >= 1:
            flat = send.reshape(-1)
            got = lax.ppermute(jnp.concatenate([flat, vec]), "dp", pairs)
            vec = vec + got[flat.size :]
            got = got[: flat.size].reshape(send.shape)
        else:
            got = lax.ppermute(send, "dp", pairs)
        cur = keep + got
        remaining.pop(pos)
    out = cur.reshape((chunk,) + rest)
    if vec is None:
        return out
    vec = vec + lax.ppermute(vec, "dp", [(i, i ^ 1) for i in range(ndp)])
    return out, vec


def reduce_tree(x, name, size):
    bits = size.bit_length() - 1
    for bit in range(bits):
        x = x + lax.ppermute(x, name, [(i, i ^ (1 << bit)) for i in range(size)])
    return x


def make_shards(ndp, nmp):
    def shards_body(
        tokens,
        doc_ids,
        ln1_gain,
        ln1_bias,
        w_qkv,
        b_qv,
        w_out,
        b_out,
        ln2_gain,
        ln2_bias,
        w_up,
        b_up,
        w_down,
        b_down,
        cotangent,
    ):
        m = lax.axis_index("mp")
        w_out_other = swap_mp(w_out)
        row_count = tokens.shape[0]
        local_width = w_qkv.shape[2]
        seq_count, seq_len = doc_ids.shape
        seq_shape = (seq_count, seq_len, local_width // HD, HD)
        token_rows = tokens.astype(jnp.float32)
        normal_one, inv_one = normalize(token_rows)
        gain_one = ln1_gain.astype(jnp.float32)
        normed_one = (normal_one * gain_one + ln1_bias.astype(jnp.float32)).astype(jnp.bfloat16)
        projected = jnp.einsum(
            "td,dce->tce", normed_one, w_qkv, preferred_element_type=jnp.float32
        )
        bias_qv = b_qv.astype(jnp.float32)
        queries = (projected[:, 0] + bias_qv[0]).astype(jnp.bfloat16).reshape(seq_shape)
        key_rows = projected[:, 1].astype(jnp.bfloat16).reshape(seq_shape)
        value_rows = (projected[:, 2] + bias_qv[1]).astype(jnp.bfloat16).reshape(seq_shape)
        attended = []
        log_totals = []
        for s in range(seq_count):
            out_s, lse_s = attend_forward(queries[s], key_rows[s], value_rows[s], doc_ids[s])
            attended.append(out_s)
            log_totals.append(lse_s)
        mixed = jnp.stack(attended).reshape(row_count, local_width).astype(jnp.bfloat16)
        w_out_all = join_pair(w_out, w_out_other, m, 0)
        half_rows = row_count // 2
        attn_parts = []
        for part in range(2):
            rows = mixed[part * half_rows : (part + 1) * half_rows]
            rows_other = swap_mp(rows)
            attn_parts.append(
                jnp.dot(join_pair(rows, rows_other, m, 1), w_out_all,
                        preferred_element_type=jnp.float32)
            )
        attn_all = jnp.concatenate(attn_parts, axis=0)
        after_attn = token_rows + attn_all + b_out.astype(jnp.float32)
        gain_two = ln2_gain.astype(jnp.float32)
        normal_two, inv_two = normalize(after_attn)
        normed_two = (normal_two * gain_two + ln2_bias.astype(jnp.float32)).astype(jnp.bfloat16)
        up_rows = jnp.dot(normed_two, w_up, preferred_element_type=jnp.float32) + b_up.astype(
            jnp.float32
        )
        activated, gelu_pull = jax.vjp(gelu_tanh, up_rows)
        act_rows = activated.astype(jnp.bfloat16)
        ffn_part = jnp.dot(act_rows, w_down, preferred_element_type=jnp.float32)

        cot_rows = cotangent.astype(jnp.float32)
        cot_own, _ = row_halves(cot_rows, m)
        grad_w_down_t = jnp.einsum(
            "td,tf->df", cotangent, act_rows, preferred_element_type=jnp.float32
        )
        grad_act = jnp.einsum("td,fd->tf", cotangent, w_down, preferred_element_type=jnp.float32)
        grad_up = gelu_pull(grad_act)[0].astype(jnp.bfloat16)
        grad_w_up = jnp.einsum("td,tf->df", normed_two, grad_up, preferred_element_type=jnp.float32)
        grad_b_up = jnp.sum(grad_up.astype(jnp.float32), axis=0)
        norm_two_part = jnp.einsum("tf,df->td", grad_up, w_up, preferred_element_type=jnp.float32)
        grad_two_own = scatter_rows_mp(norm_two_part, m, jnp.bfloat16)
        normal_two_own, _ = row_halves(normal_two, m)
        inv_two_own, _ = row_halves(inv_two, m)
        grad_after_own = cot_own + norm_back(grad_two_own, normal_two_own, inv_two_own, gain_two)
        grad_attn_own = grad_after_own.astype(jnp.bfloat16)
        grad_attn_here = gather_rows_mp(grad_attn_own, m)
        ffn_late, grad_attn_here = lax.optimization_barrier((ffn_part, grad_attn_here))
        ffn_own = scatter_rows_mp(ffn_late, m, jnp.bfloat16)
        after_own, _ = row_halves(after_attn, m)
        out_own = (after_own + (ffn_own + b_down.astype(jnp.float32))).astype(jnp.bfloat16)
        block_out = gather_rows_mp(out_own, m)
        grad_w_out_t = jnp.einsum(
            "td,te->de", grad_attn_here, mixed, preferred_element_type=jnp.float32
        )
        grad_mixed = jnp.einsum(
            "td,ed->te", grad_attn_here, w_out, preferred_element_type=jnp.float32
        ).astype(jnp.bfloat16)
        grad_mixed = grad_mixed.reshape(seq_shape)
        gq, gk, gv = [], [], []
        for s in range(seq_count):
            dq_s, dk_s, dv_s = attend_backward(
                queries[s], key_rows[s], value_rows[s], doc_ids[s], log_totals[s], grad_mixed[s]
            )
            gq.append(dq_s)
            gk.append(dk_s)
            gv.append(dv_s)
        grad_q = jnp.stack(gq).reshape(row_count, local_width).astype(jnp.bfloat16)
        grad_k = jnp.stack(gk).reshape(row_count, local_width).astype(jnp.bfloat16)
        grad_v = jnp.stack(gv).reshape(row_count, local_width).astype(jnp.bfloat16)
        grad_proj = jnp.stack([grad_q, grad_k, grad_v], axis=1)
        grad_w_qkv = jnp.einsum(
            "td,tce->dce", normed_one, grad_proj, preferred_element_type=jnp.float32
        )
        grad_b_qv = jnp.stack(
            [
                jnp.sum(grad_q.astype(jnp.float32), axis=0),
                jnp.sum(grad_v.astype(jnp.float32), axis=0),
            ]
        )
        norm_one_part = jnp.einsum(
            "tce,dce->td", grad_proj, w_qkv, preferred_element_type=jnp.float32
        )
        grad_one_own = scatter_rows_mp(norm_one_part, m, jnp.bfloat16)
        normal_one_own, _ = row_halves(normal_one, m)
        inv_one_own, _ = row_halves(inv_one, m)
        grad_input_own = grad_after_own + norm_back(
            grad_one_own, normal_one_own, inv_one_own, gain_one
        )
        grad_input = gather_rows_into(grad_input_own, m)
        vector_terms = jnp.stack(
            [
                jnp.sum(grad_one_own * normal_one_own, axis=0),
                jnp.sum(grad_one_own, axis=0),
                jnp.sum(grad_two_own * normal_two_own, axis=0),
                jnp.sum(grad_two_own, axis=0),
                jnp.sum(grad_attn_own.astype(jnp.float32), axis=0),
                jnp.sum(cot_own, axis=0),
            ]
        )
        n_vec = vector_terms.size
        n_qv = grad_b_qv.size
        packed = jnp.concatenate([vector_terms.reshape(-1), grad_b_qv.reshape(-1), grad_b_up])
        qkv_cols = max(128, (grad_w_qkv.shape[2] * 2 // 3) // 128 * 128)
        qkv_a, packed = scatter_dp(grad_w_qkv[:, :, :qkv_cols], ndp, vec=packed)
        qkv_b = scatter_dp(grad_w_qkv[:, :, qkv_cols:], ndp, swap=True)
        sum_qkv = jnp.concatenate([qkv_a, qkv_b], axis=2)
        vector_sum = reduce_tree(packed[:n_vec], "mp", nmp).reshape(vector_terms.shape)
        qv_sum = packed[n_vec : n_vec + n_qv].reshape(grad_b_qv.shape)
        up_sum = packed[n_vec + n_qv :]
        sum_out = scatter_dp(grad_w_out_t, ndp, swap=True).T
        sum_up = scatter_dp(grad_w_up, ndp)
        sum_down = scatter_dp(grad_w_down_t, ndp, swap=True).T
        return (
            block_out,
            grad_input,
            vector_sum[0],
            vector_sum[1],
            sum_qkv,
            qv_sum,
            sum_out,
            vector_sum[4],
            vector_sum[2],
            vector_sum[3],
            sum_up,
            up_sum,
            sum_down,
            vector_sum[5],
        )

    return shards_body


def solution(mesh):
    return jax.shard_map(
        make_shards(mesh.shape["dp"], mesh.shape["mp"]),
        mesh=mesh,
        in_specs=(
            P("dp", None),
            P("dp", None),
            P(),
            P(),
            P(None, None, "mp"),
            P(None, "mp"),
            P("mp", None),
            P(),
            P(),
            P(),
            P(None, "mp"),
            P("mp"),
            P("mp", None),
            P(),
            P("dp", None),
        ),
        out_specs=(
            P("dp", None),
            P("dp", None),
            P(),
            P(),
            P("dp", None, "mp"),
            P(None, "mp"),
            P("mp", "dp"),
            P(),
            P(),
            P(),
            P("dp", "mp"),
            P("mp"),
            P("mp", "dp"),
            P(),
        ),
        check_vma=False,
    )
```

```python
import math

import jax
import jax.numpy as jnp
from jax import lax
from jax.sharding import PartitionSpec as P


HD = 64


epsilon = 1e-05


def normalize(values):
    average = jnp.mean(values, axis=-1, keepdims=True)
    centered = values - average
    variance = jnp.mean(centered * centered, axis=-1, keepdims=True)
    inverse = lax.rsqrt(variance + epsilon)
    return (centered * inverse, inverse)


def norm_back(grad_out, normal_rows, inverse, gain):
    grad_unit = grad_out * gain
    return inverse * (
        grad_unit
        - jnp.mean(grad_unit, axis=-1, keepdims=True)
        - normal_rows * jnp.mean(grad_unit * normal_rows, axis=-1, keepdims=True)
    )


def gelu_tanh(values):
    return (
        0.5
        * values
        * (1.0 + jnp.tanh(0.7978845608028654 * (values + 0.044715 * values * values * values)))
    )


MAX_DOC = 512


def key_window(offset, block_rows, seq_len):
    start = max(0, offset + 1 - MAX_DOC)
    start = (start // 128) * 128
    return start, min(seq_len, offset + block_rows)


def query_block_rows(seq_len):
    return min(256, seq_len)


def block_scores(query_block, key_rows, doc_rows, offset):
    block_rows = query_block.shape[0]
    kstart, kend = key_window(offset, block_rows, key_rows.shape[0])
    scores = jnp.einsum(
        "qhd,khd->hqk", query_block, key_rows[kstart:kend], preferred_element_type=jnp.float32
    ) * (1.0 / math.sqrt(HD))
    query_pos = offset + lax.iota(jnp.int32, block_rows)
    key_pos = kstart + lax.iota(jnp.int32, kend - kstart)
    block_docs = doc_rows[offset : offset + block_rows]
    allowed = (block_docs[:, None] == doc_rows[None, kstart:kend]) & (
        query_pos[:, None] >= key_pos[None, :]
    )
    return jnp.where(allowed[None], scores, -1e30)


def attend_forward(queries, key_rows, value_rows, doc_rows):
    seq_len = queries.shape[0]
    block_rows = query_block_rows(seq_len)
    outputs = []
    log_parts = []
    for offset in range(0, seq_len, block_rows):
      scores = block_scores(queries[offset : offset + block_rows], key_rows, doc_rows, offset)
      row_max = jnp.max(scores, axis=-1, keepdims=True)
      log_total = row_max + jnp.log(jnp.sum(jnp.exp(scores - row_max), axis=-1, keepdims=True))
      probabilities = jnp.exp(scores - log_total).astype(jnp.bfloat16)
      kstart, kend = key_window(offset, block_rows, seq_len)
      outputs.append(
          jnp.einsum(
              "hqk,khd->qhd",
              probabilities,
              value_rows[kstart:kend],
              preferred_element_type=jnp.float32,
          )
      )
      log_parts.append(log_total[..., 0])
    return (jnp.concatenate(outputs, axis=0), jnp.concatenate(log_parts, axis=1))


def attend_backward(queries, key_rows, value_rows, doc_rows, log_totals, grad_out):
    seq_len = queries.shape[0]
    block_rows = query_block_rows(seq_len)
    scale_factor = 1.0 / math.sqrt(HD)
    grad_queries = []
    grad_keys = jnp.zeros(key_rows.shape, jnp.float32)
    grad_values = jnp.zeros(value_rows.shape, jnp.float32)
    for offset in range(0, seq_len, block_rows):
      query_block = queries[offset : offset + block_rows]
      grad_block = grad_out[offset : offset + block_rows]
      kstart, kend = key_window(offset, block_rows, seq_len)
      scores = block_scores(query_block, key_rows, doc_rows, offset)
      probabilities = jnp.exp(scores - log_totals[:, offset : offset + block_rows, None])
      grad_probs = jnp.einsum(
          "qhd,khd->hqk", grad_block, value_rows[kstart:kend], preferred_element_type=jnp.float32
      )
      row_dots = jnp.sum(probabilities * grad_probs, axis=-1, keepdims=True)
      grad_scores = (probabilities * (grad_probs - row_dots)).astype(jnp.bfloat16)
      grad_queries.append(
          scale_factor
          * jnp.einsum(
              "hqk,khd->qhd",
              grad_scores,
              key_rows[kstart:kend],
              preferred_element_type=jnp.float32,
          )
      )
      grad_keys = grad_keys.at[kstart:kend].add(scale_factor * jnp.einsum(
          "hqk,qhd->khd", grad_scores, query_block, preferred_element_type=jnp.float32
      ))
      grad_values = grad_values.at[kstart:kend].add(jnp.einsum(
          "hqk,qhd->khd",
          probabilities.astype(jnp.bfloat16),
          grad_block,
          preferred_element_type=jnp.float32,
      ))
    return (jnp.concatenate(grad_queries, axis=0), grad_keys, grad_values)


def swap_mp(x):
    return lax.ppermute(x, "mp", [(0, 1), (1, 0)])


def row_halves(x, m):
    half = x.shape[0] // 2
    own = lax.dynamic_slice_in_dim(x, m * half, half, axis=0)
    other = lax.dynamic_slice_in_dim(x, (1 - m) * half, half, axis=0)
    return own, other


def join_pair(own, other, m, axis):
    return jnp.where(
        m == 0,
        jnp.concatenate([own, other], axis=axis),
        jnp.concatenate([other, own], axis=axis),
    )


def scatter_rows_mp(partial, m, send_dtype):
    own, other = row_halves(partial, m)
    return own + swap_mp(other.astype(send_dtype)).astype(own.dtype)


def gather_rows_mp(own, m):
    return join_pair(own, swap_mp(own), m, 0)


def gather_rows_into(own, m):
    half = own.shape[0]
    other = swap_mp(own)
    rows = jnp.zeros((2 * half,) + own.shape[1:], own.dtype)
    rows = lax.dynamic_update_slice_in_dim(rows, own, m * half, axis=0)
    return lax.dynamic_update_slice_in_dim(rows, other, (1 - m) * half, axis=0)


def scatter_dp(x, ndp, swap=False, vec=None):
    idx = lax.axis_index("dp")
    bits = ndp.bit_length() - 1
    chunk = x.shape[0] // ndp
    rest = x.shape[1:]
    cur = x.reshape((2,) * bits + (chunk,) + rest)
    remaining = list(range(bits - 1, -1, -1))
    order = list(range(bits))
    if swap and bits >= 3:
        order[1], order[2] = order[2], order[1]
    for level, bit in enumerate(order):
        pos = remaining.index(bit)
        mine = (idx >> bit) & 1
        keep = lax.dynamic_index_in_dim(cur, mine, pos, keepdims=False)
        send = lax.dynamic_index_in_dim(cur, 1 - mine, pos, keepdims=False)
        pairs = [(i, i ^ (1 << bit)) for i in range(ndp)]
        if vec is not None and level >= 1:
            flat = send.reshape(-1)
            got = lax.ppermute(jnp.concatenate([flat, vec]), "dp", pairs)
            vec = vec + got[flat.size :]
            got = got[: flat.size].reshape(send.shape)
        else:
            got = lax.ppermute(send, "dp", pairs)
        cur = keep + got
        remaining.pop(pos)
    out = cur.reshape((chunk,) + rest)
    if vec is None:
        return out
    vec = vec + lax.ppermute(vec, "dp", [(i, i ^ 1) for i in range(ndp)])
    return out, vec


def reduce_tree(x, name, size):
    bits = size.bit_length() - 1
    for bit in range(bits):
        x = x + lax.ppermute(x, name, [(i, i ^ (1 << bit)) for i in range(size)])
    return x


def make_shards(ndp, nmp):
    def shards_body(
        tokens,
        doc_ids,
        ln1_gain,
        ln1_bias,
        w_qkv,
        b_qv,
        w_out,
        b_out,
        ln2_gain,
        ln2_bias,
        w_up,
        b_up,
        w_down,
        b_down,
        cotangent,
    ):
        m = lax.axis_index("mp")
        w_out_other = swap_mp(w_out)
        row_count = tokens.shape[0]
        local_width = w_qkv.shape[2]
        seq_count, seq_len = doc_ids.shape
        seq_shape = (seq_count, seq_len, local_width // HD, HD)
        token_rows = tokens.astype(jnp.float32)
        normal_one, inv_one = normalize(token_rows)
        gain_one = ln1_gain.astype(jnp.float32)
        normed_one = (normal_one * gain_one + ln1_bias.astype(jnp.float32)).astype(jnp.bfloat16)
        projected = jnp.einsum(
            "td,dce->tce", normed_one, w_qkv, preferred_element_type=jnp.float32
        )
        bias_qv = b_qv.astype(jnp.float32)
        queries = (projected[:, 0] + bias_qv[0]).astype(jnp.bfloat16).reshape(seq_shape)
        key_rows = projected[:, 1].astype(jnp.bfloat16).reshape(seq_shape)
        value_rows = (projected[:, 2] + bias_qv[1]).astype(jnp.bfloat16).reshape(seq_shape)
        attended = []
        log_totals = []
        for s in range(seq_count):
            out_s, lse_s = attend_forward(queries[s], key_rows[s], value_rows[s], doc_ids[s])
            attended.append(out_s)
            log_totals.append(lse_s)
        mixed = jnp.stack(attended).reshape(row_count, local_width).astype(jnp.bfloat16)
        w_out_all = join_pair(w_out, w_out_other, m, 0)
        half_rows = row_count // 2
        attn_parts = []
        for part in range(2):
            rows = mixed[part * half_rows : (part + 1) * half_rows]
            rows_other = swap_mp(rows)
            attn_parts.append(
                jnp.dot(join_pair(rows, rows_other, m, 1), w_out_all,
                        preferred_element_type=jnp.float32)
            )
        attn_all = jnp.concatenate(attn_parts, axis=0)
        after_attn = token_rows + attn_all + b_out.astype(jnp.float32)
        gain_two = ln2_gain.astype(jnp.float32)
        normal_two, inv_two = normalize(after_attn)
        normed_two = (normal_two * gain_two + ln2_bias.astype(jnp.float32)).astype(jnp.bfloat16)
        up_rows = jnp.dot(normed_two, w_up, preferred_element_type=jnp.float32) + b_up.astype(
            jnp.float32
        )
        activated, gelu_pull = jax.vjp(gelu_tanh, up_rows)
        act_rows = activated.astype(jnp.bfloat16)
        ffn_part = jnp.dot(act_rows, w_down, preferred_element_type=jnp.float32)

        cot_rows = cotangent.astype(jnp.float32)
        cot_own, _ = row_halves(cot_rows, m)
        grad_w_down_t = jnp.einsum(
            "td,tf->df", cotangent, act_rows, preferred_element_type=jnp.float32
        )
        grad_act = jnp.einsum("td,fd->tf", cotangent, w_down, preferred_element_type=jnp.float32)
        grad_up = gelu_pull(grad_act)[0].astype(jnp.bfloat16)
        grad_w_up = jnp.einsum("td,tf->df", normed_two, grad_up, preferred_element_type=jnp.float32)
        grad_b_up = jnp.sum(grad_up.astype(jnp.float32), axis=0)
        norm_two_part = jnp.einsum("tf,df->td", grad_up, w_up, preferred_element_type=jnp.float32)
        grad_two_own = scatter_rows_mp(norm_two_part, m, jnp.bfloat16)
        normal_two_own, _ = row_halves(normal_two, m)
        inv_two_own, _ = row_halves(inv_two, m)
        grad_after_own = cot_own + norm_back(grad_two_own, normal_two_own, inv_two_own, gain_two)
        grad_attn_own = grad_after_own.astype(jnp.bfloat16)
        grad_attn_here = gather_rows_mp(grad_attn_own, m)
        ffn_late, grad_attn_here = lax.optimization_barrier((ffn_part, grad_attn_here))
        ffn_own = scatter_rows_mp(ffn_late, m, jnp.bfloat16)
        after_own, _ = row_halves(after_attn, m)
        out_own = (after_own + (ffn_own + b_down.astype(jnp.float32))).astype(jnp.bfloat16)
        block_out = gather_rows_mp(out_own, m)
        grad_w_out_t = jnp.einsum(
            "td,te->de", grad_attn_here, mixed, preferred_element_type=jnp.float32
        )
        grad_mixed = jnp.einsum(
            "td,ed->te", grad_attn_here, w_out, preferred_element_type=jnp.float32
        ).astype(jnp.bfloat16)
        grad_mixed = grad_mixed.reshape(seq_shape)
        gq, gk, gv = [], [], []
        for s in range(seq_count):
            dq_s, dk_s, dv_s = attend_backward(
                queries[s], key_rows[s], value_rows[s], doc_ids[s], log_totals[s], grad_mixed[s]
            )
            gq.append(dq_s)
            gk.append(dk_s)
            gv.append(dv_s)
        grad_q = jnp.stack(gq).reshape(row_count, local_width).astype(jnp.bfloat16)
        grad_k = jnp.stack(gk).reshape(row_count, local_width).astype(jnp.bfloat16)
        grad_v = jnp.stack(gv).reshape(row_count, local_width).astype(jnp.bfloat16)
        grad_proj = jnp.stack([grad_q, grad_k, grad_v], axis=1)
        grad_w_qkv = jnp.einsum(
            "td,tce->dce", normed_one, grad_proj, preferred_element_type=jnp.float32
        )
        grad_b_qv = jnp.stack(
            [
                jnp.sum(grad_q.astype(jnp.float32), axis=0),
                jnp.sum(grad_v.astype(jnp.float32), axis=0),
            ]
        )
        norm_one_part = jnp.einsum(
            "tce,dce->td", grad_proj, w_qkv, preferred_element_type=jnp.float32
        )
        grad_one_own = scatter_rows_mp(norm_one_part, m, jnp.bfloat16)
        normal_one_own, _ = row_halves(normal_one, m)
        inv_one_own, _ = row_halves(inv_one, m)
        grad_input_own = grad_after_own + norm_back(
            grad_one_own, normal_one_own, inv_one_own, gain_one
        )
        grad_input = gather_rows_into(grad_input_own, m)
        vector_terms = jnp.stack(
            [
                jnp.sum(grad_one_own * normal_one_own, axis=0),
                jnp.sum(grad_one_own, axis=0),
                jnp.sum(grad_two_own * normal_two_own, axis=0),
                jnp.sum(grad_two_own, axis=0),
                jnp.sum(grad_attn_own.astype(jnp.float32), axis=0),
                jnp.sum(cot_own, axis=0),
            ]
        )
        n_vec = vector_terms.size
        n_qv = grad_b_qv.size
        packed = jnp.concatenate([vector_terms.reshape(-1), grad_b_qv.reshape(-1), grad_b_up])
        qkv_cols = max(128, (grad_w_qkv.shape[2] * 2 // 3) // 128 * 128)
        qkv_a, packed = scatter_dp(grad_w_qkv[:, :, :qkv_cols], ndp, vec=packed)
        qkv_b = scatter_dp(grad_w_qkv[:, :, qkv_cols:], ndp, swap=True)
        sum_qkv = jnp.concatenate([qkv_a, qkv_b], axis=2)
        vector_sum = reduce_tree(packed[:n_vec], "mp", nmp).reshape(vector_terms.shape)
        qv_sum = packed[n_vec : n_vec + n_qv].reshape(grad_b_qv.shape)
        up_sum = packed[n_vec + n_qv :]
        sum_out = scatter_dp(grad_w_out_t, ndp).T
        up_cols = grad_w_up.shape[1]
        ffn_grads = jnp.concatenate([grad_w_up, grad_w_down_t], axis=1)
        ffn_cut = max(128, (ffn_grads.shape[1] * 2 // 3) // 128 * 128)
        sum_ffn = jnp.concatenate(
            [
                scatter_dp(ffn_grads[:, :ffn_cut], ndp),
                scatter_dp(ffn_grads[:, ffn_cut:], ndp, swap=True),
            ],
            axis=1,
        )
        sum_up = sum_ffn[:, :up_cols]
        sum_down = sum_ffn[:, up_cols:].T
        return (
            block_out,
            grad_input,
            vector_sum[0],
            vector_sum[1],
            sum_qkv,
            qv_sum,
            sum_out,
            vector_sum[4],
            vector_sum[2],
            vector_sum[3],
            sum_up,
            up_sum,
            sum_down,
            vector_sum[5],
        )

    return shards_body


def solution(mesh):
    return jax.shard_map(
        make_shards(mesh.shape["dp"], mesh.shape["mp"]),
        mesh=mesh,
        in_specs=(
            P("dp", None),
            P("dp", None),
            P(),
            P(),
            P(None, None, "mp"),
            P(None, "mp"),
            P("mp", None),
            P(),
            P(),
            P(),
            P(None, "mp"),
            P("mp"),
            P("mp", None),
            P(),
            P("dp", None),
        ),
        out_specs=(
            P("dp", None),
            P("dp", None),
            P(),
            P(),
            P("dp", None, "mp"),
            P(None, "mp"),
            P("mp", "dp"),
            P(),
            P(),
            P(),
            P("dp", "mp"),
            P("mp"),
            P("mp", "dp"),
            P(),
        ),
        check_vma=False,
    )
```
